256 devices in a mesh: level: 4 (over x), basin: 32 (over y, z), group: 2 (over core).
Axes of the slice: x: 4, y: 4, z: 8, core: 2. Of those that a mesh axis runs over, the one named last changes fastest.
Arguments:
- lateral: float32 [96, 131072], P('group', ('level', 'basin')), may hold values from 0.02 to 2
- cotangent: float32 [96, 131072], P('group', ('level', 'basin')), may hold values from -6 to 6
- attributes: float32 [16, 131072], P(None, ('level', 'basin')), may hold values from -6 to 6
- region: int32 [131072], P(('level', 'basin')), may hold values from 0 to 127
- feeders: int32 [2, 131072], P(None, ('level', 'basin')), may hold values from 0 to 1151
- feeder_count: int32 [131072], P(('level', 'basin')), may hold values from 0 to 2
- live_blocks: int32 [128], P(('level', 'basin')), may hold values from 1 to 8, as said below
- net_weight: float32 [128, 16, 2], replicated, may hold values from -1.5 to 1.5
Outputs:
- outflow: float32 [96, 131072], P('group', ('level', 'basin'))
- grad_net: float32 [128, 16, 2], P('basin')
The draws below stay inside these ranges and needn't reach their ends.
Inputs may be any that keep to these rules, and one draw needn't show every extreme that they name: `feeders`: entries below 1024 name a reach slot of the same basin shard one level lower in the order; an entry e of 1024 or more names reach slot e - 1024 of the previous basin shard one level lower. Nothing feeds level 0, and the previous shard of basin shard 0 is empty. `live_blocks`: reach slots at or past 128 times this count are padding; some shard is full in every draw.
All inputs are finite; a program needn't handle non-finite values.
Results may differ from the reference program's by a relative error of at most 0.00029.
Values sent between devices are 32-bit elements; how exact they have to be, the bound alone decides.
No kernel may reach another device: no remote copies, remote signals or barrier semaphores. Data moves between devices by JAX's collectives and lax.ppermute only.
A program may use at most 64 MiB of HBM per device.

```python
import math
import jax
import jax.numpy as jnp
from jax import lax

WINDOW = 96
BLOCK = 128
BLOCKS_DEV = 8
REACH_DEV = 1024
OUTLETS = 128
SHARDS = 128
REACHES = 131072
UP = 2
ATTR = 16
PARAMS = 2
REGIONS = 128
N_LEVEL = 4
N_BASIN = 32


def draw_live_blocks(key, part):
    counts = jax.random.randint(key, (SHARDS,), 1, BLOCKS_DEV + 1)
    return counts.at[0].set(BLOCKS_DEV).astype(jnp.int32)


def with_ends(drawn, stream_key, low, high):
    longest = drawn.shape.index(max(drawn.shape))
    spots = []
    for shift in (0, 1):
        where = [jax.random.randint(jax.random.fold_in(stream_key, axis), (), 0, length) for axis, length in enumerate(drawn.shape)]
        where[longest] = (where[longest] + shift) % drawn.shape[longest]
        spots.append(tuple(where))
    return drawn.at[spots[0]].set(low).at[spots[1]].set(high)


def steps_of(rng, dims, pieces, low, high):
    def one(axis_at, shards_of):
        draws = jax.random.uniform(jax.random.fold_in(jax.random.fold_in(rng, 6), axis_at), (shards_of,), jnp.float32, low / len(pieces), high / len(pieces))
        return jnp.repeat(jnp.exp(draws), dims[axis_at] // shards_of).reshape((-1,) + (1,) * (len(dims) - axis_at - 1))

    level = one(*pieces[0])
    for cut in pieces[1:]:
        level = level * one(*cut)
    return level


def normal_values(stream_key, dims, width, reach, cuts=(), held_as=jnp.bfloat16):
    values = jax.random.normal(stream_key, dims, jnp.float32) * width
    if len(cuts) > 0:
        values = steps_of(stream_key, dims, cuts, -0.22, 0.18) * values
    return jnp.clip(values, min=-reach, max=reach).astype(held_as)


def setup_inputs(seed: int = 0) -> dict:
    key_list = jax.random.split(jax.random.key(seed), 9)
    lateral = jnp.clip(jnp.exp(math.log(2.0) - 4.6051702 * jax.random.uniform(key_list[0], (WINDOW, REACHES), jnp.float32) ** steps_of(key_list[0], (WINDOW, REACHES), ((0, 2), (1, 128)), -0.2, 0.2)), 0.02, 2.0)
    cotangent = normal_values(key_list[1], (WINDOW, REACHES), 1.0, 6.0, ((0, 2), (1, 128)), jnp.float32)
    attributes = normal_values(key_list[2], (ATTR, REACHES), 1.0, 6.0, ((1, 128),), jnp.float32)
    region = with_ends(jax.random.randint(key_list[3], (REACHES,), 0, REGIONS), jax.random.fold_in(key_list[3], 1), 0, REGIONS - 1).astype(jnp.int32)
    feeders = with_ends(jax.random.randint(key_list[4], (UP, REACHES), 0, REACH_DEV + OUTLETS), jax.random.fold_in(key_list[4], 1), 0, (REACH_DEV + OUTLETS) - 1).astype(jnp.int32)
    feeder_count = with_ends(jax.random.randint(key_list[5], (REACHES,), 0, UP + 1), jax.random.fold_in(key_list[5], 1), 0, UP).astype(jnp.int32)
    live_blocks = draw_live_blocks(jax.random.fold_in(key_list[8], 71), 0)
    net_weight = normal_values(key_list[7], (REGIONS, ATTR, PARAMS), ATTR ** -0.5, 1.5, (), jnp.float32)
    return {"lateral": lateral, "cotangent": cotangent, "attributes": attributes, "region": region, "feeders": feeders, "feeder_count": feeder_count, "live_blocks": live_blocks, "net_weight": net_weight}


def coefficients(raw_params):
    travel = 1.0 + 47.0 * jax.nn.sigmoid(raw_params[0])
    weighting = 0.05 + 0.4 * jax.nn.sigmoid(raw_params[1])
    storage = travel * (1.0 - weighting)
    divisor = storage + 0.5
    return ((0.5 - travel * weighting) / divisor, (0.5 + travel * weighting) / divisor, (storage - 0.5) / divisor, 1.0 / divisor)

def route_window(coef_level, inflow, lateral_level):
    gain_now, gain_prev, retain, gain_side = coef_level

    def advance(carry, inputs):
        flow_prev, inflow_prev = carry
        inflow_now, lateral_now = inputs
        result = retain * flow_prev + (gain_now * inflow_now + gain_prev * inflow_prev + gain_side * lateral_now)
        return ((result, inflow_now), result)
    zero_state = jnp.zeros(inflow.shape[1:], jnp.float32)
    unused, flows = lax.scan(advance, (zero_state, zero_state), (inflow, lateral_level))
    return flows

def reference(lateral, cotangent, attributes, region, feeders, feeder_count, live_blocks, net_weight):
    window = lateral.shape[0]
    lateral_grid = lateral.reshape(window, N_LEVEL, N_BASIN, REACH_DEV)
    slot_ids = jnp.arange(REACH_DEV, dtype=jnp.int32)
    live_mask = (slot_ids[None, None, :] < live_blocks.reshape(N_LEVEL, N_BASIN)[:, :, None] * BLOCK).astype(jnp.float32)
    feeder_grid = feeders.reshape(UP, N_LEVEL, N_BASIN, REACH_DEV)
    count_grid = feeder_count.reshape(N_LEVEL, N_BASIN, REACH_DEV)

    def forward(weight):
        chosen = weight[region]
        raw_params = jnp.einsum('nap,an->pn', chosen, attributes, precision=lax.Precision.HIGHEST)
        raw_params = raw_params.reshape(PARAMS, N_LEVEL, N_BASIN, REACH_DEV)
        coef_grid = coefficients(raw_params)
        zero_flow = jnp.zeros((window, N_BASIN, REACH_DEV), jnp.float32)
        upper_flow = zero_flow
        levels_out = []
        for level_pos in range(N_LEVEL):
            inflow = zero_flow
            if level_pos > 0:
                side_flow = jnp.concatenate([jnp.zeros((window, 1, OUTLETS), jnp.float32), upper_flow[:, :-1, :OUTLETS]], axis=1)
                source = jnp.concatenate([upper_flow, side_flow], axis=2)
                for upslot in range(UP):
                    index_grid = jnp.broadcast_to(feeder_grid[upslot, level_pos][None], (window, N_BASIN, REACH_DEV))
                    picked = jnp.take_along_axis(source, index_grid, axis=2)
                    inflow = inflow + jnp.where(upslot < count_grid[level_pos][None], picked, 0.0)
            coef_level = tuple((coef_part[level_pos] for coef_part in coef_grid))
            result = route_window(coef_level, inflow, lateral_grid[:, level_pos]) * live_mask[level_pos][None]
            levels_out.append(result)
            upper_flow = result
        return jnp.stack(levels_out, axis=1).reshape(window, N_LEVEL * N_BASIN * REACH_DEV)
    outflow, pull_back = jax.vjp(forward, net_weight)
    grad_net = pull_back(cotangent)[0]
    return (outflow, grad_net)
```

```python
import jax
import jax.numpy as jnp
from jax import lax
from jax.sharding import PartitionSpec as P

BLOCK = 128


def shifted(value, axis, steps):
    count = lax.axis_size(axis)
    leading, last = (max(0, -steps), min(count, count - steps))
    return lax.ppermute(value, axis, [(source, source + steps) for source in range(leading, last)])


def diagonal(value, steps):
    levels, basins = lax.axis_size("level"), lax.axis_size("basin")
    pairs = []
    for level in range(max(0, -steps), min(levels, levels - steps)):
        for basin in range(max(0, -steps), min(basins, basins - steps)):
            pairs.append((level * basins + basin, (level + steps) * basins + basin + steps))
    return lax.ppermute(value, ("level", "basin"), pairs)


def exchanged(value, axis, mask):
    count = lax.axis_size(axis)
    return lax.ppermute(value, axis, [(source, source ^ mask) for source in range(count)])


def scattered_sum(blocks, axis):
    count, mine = (lax.axis_size(axis), lax.axis_index(axis))
    width = count
    while width > 1:
        width //= 2
        lower, upper = blocks[:width], blocks[width:]
        high = (mine & width) > 0
        kept = jnp.where(high, upper, lower)
        sent = jnp.where(high, lower, upper)
        blocks = kept + exchanged(sent, axis, width)
    return blocks[0]


def butterfly_sum(value, axis):
    mask = 1
    while mask < lax.axis_size(axis):
        value = value + exchanged(value, axis, mask)
        mask *= 2
    return value


def carried_in(value, axis, join, neutral, backward):
    count, mine = (lax.axis_size(axis), lax.axis_index(axis))
    pieces = lax.all_gather(value, axis)
    if backward:
        pieces = pieces[::-1]
        mine = count - 1 - mine
    subtotal = jnp.full_like(value, 0) + jnp.asarray(neutral, value.dtype)

    def turn(position, subtotal):
        longer = join(subtotal, pieces[position])
        return jnp.where(position < mine, longer, subtotal)

    return lax.fori_loop(0, count - 1, turn, subtotal)


def coefficients(raw_params):
    travel = 1.0 + 47.0 * jax.nn.sigmoid(raw_params[0])
    weighting = 0.05 + 0.4 * jax.nn.sigmoid(raw_params[1])
    storage = travel * (1.0 - weighting)
    divisor = storage + 0.5
    return (
        (0.5 - travel * weighting) / divisor,
        (0.5 + travel * weighting) / divisor,
        (storage - 0.5) / divisor,
        1.0 / divisor,
    )


def affine_join(earlier, latter):
    return (earlier[0] * latter[0], latter[0] * earlier[1] + latter[1])


def stack_affine(pair):
    return jnp.stack([pair[0], pair[1]], axis=0)


def split_affine(stacked):
    return (stacked[0], stacked[1])


def stacked_affine(earlier, latter):
    return stack_affine(affine_join(split_affine(earlier), split_affine(latter)))


def body(lateral, cotangent, attributes, region, feeders, feeder_count, live_blocks, net_weight):
    steps_dev, reach_dev = lateral.shape
    outlets = reach_dev // 8
    regions, attr_count, param_count = net_weight.shape
    levels = lax.axis_size("level")
    up_count = feeders.shape[0]
    slot_ids = lax.broadcasted_iota(jnp.int32, (reach_dev,), 0)
    live_mask = (slot_ids < live_blocks[0] * BLOCK).astype(jnp.float32)
    member_table = (
        region[None, :] == lax.broadcasted_iota(jnp.int32, (regions, reach_dev), 0)
    ).astype(jnp.float32)
    per_region = jnp.dot(
        jnp.transpose(net_weight, (0, 2, 1)).reshape(regions * param_count, attr_count),
        attributes,
        precision=lax.Precision.HIGHEST,
        preferred_element_type=jnp.float32,
    )
    raw_params = jnp.einsum(
        "rpi,ri->pi",
        per_region.reshape(regions, param_count, reach_dev),
        member_table,
        precision=lax.Precision.HIGHEST,
    )
    coef_set, coef_pull = jax.vjp(coefficients, raw_params)
    gain_now, gain_prev, retain, gain_side = coef_set
    zero_row = jnp.zeros((reach_dev,), jnp.float32)
    unit_row = jnp.ones((reach_dev,), jnp.float32)
    affine_identity = stack_affine((unit_row, zero_row))
    retention = jnp.broadcast_to(retain, (steps_dev, reach_dev))
    zero_flow = jnp.zeros((steps_dev, reach_dev), jnp.float32)

    def route_level(inflow):
        inflow_in = shifted(inflow[-1], "group", 1)
        inflow_before = jnp.concatenate([inflow_in[None], inflow[:-1]], axis=0)
        drive = gain_now * inflow + gain_prev * inflow_before + gain_side * lateral
        powers, local_flow = lax.associative_scan(affine_join, (retention, drive), axis=0)
        edge_scan = carried_in(
            stack_affine((powers[-1], local_flow[-1])),
            "group",
            stacked_affine,
            affine_identity,
            False,
        )
        state_in = edge_scan[1]
        result = local_flow + powers * state_in
        return (result * live_mask, state_in, inflow_in)

    inflow = zero_flow
    outflow, state_in, inflow_in = route_level(inflow)
    for level_step in range(levels - 1):
        upper_flow = shifted(outflow, "level", 1)
        side_flow = diagonal(outflow[:, :outlets], 1)
        source = jnp.concatenate([upper_flow, side_flow], axis=1)
        summed_flow = jnp.zeros((source.shape[0], feeder_count.shape[0]), jnp.float32)
        for sum_upslot in range(up_count):
            picked_flow = jnp.take(source, feeders[sum_upslot], axis=1)
            summed_flow = summed_flow + jnp.where(sum_upslot < feeder_count, picked_flow, 0.0)
        inflow = summed_flow
        outflow, state_in, inflow_in = route_level(inflow)
    adjoint_down = zero_flow
    adjoint = zero_flow
    for level_step in range(levels):
        adjoint_load = live_mask * (cotangent + adjoint_down)
        rev_power, local_adj = lax.associative_scan(
            affine_join, (retention, adjoint_load), axis=0, reverse=True
        )
        edge_adj = carried_in(
            stack_affine((rev_power[0], local_adj[0])),
            "group",
            stacked_affine,
            affine_identity,
            True,
        )
        adjoint_in = edge_adj[1]
        adjoint = local_adj + rev_power * adjoint_in
        if level_step + 1 < levels:
            later_adj = jnp.concatenate([adjoint[1:], adjoint_in[None]], axis=0)
            to_inflow = gain_now * adjoint + gain_prev * later_adj
            spread = jnp.zeros((to_inflow.shape[0], reach_dev + outlets), jnp.float32)
            for upslot in range(up_count):
                spread = spread.at[:, feeders[upslot]].add(
                    jnp.where(upslot < feeder_count, to_inflow, 0.0)
                )
            own_part = spread[:, :reach_dev]
            side_part = spread[:, reach_dev:]
            returned = diagonal(side_part, -1)
            adjoint_down = shifted(own_part, "level", -1).at[:, :outlets].add(returned)
    flow_before = jnp.concatenate([state_in[None], outflow[:-1]], axis=0)
    inflow_before = jnp.concatenate([inflow_in[None], inflow[:-1]], axis=0)
    coef_grads = (
        jnp.sum(adjoint * inflow, axis=0),
        jnp.sum(adjoint * inflow_before, axis=0),
        jnp.sum(adjoint * flow_before, axis=0),
        jnp.sum(adjoint * lateral, axis=0),
    )
    raw_grad = coef_pull(coef_grads)[0]
    owned_rows = regions // lax.axis_size("basin")
    owner_table = (
        region[None, :] == lax.broadcasted_iota(jnp.int32, (regions, reach_dev), 0)
    ).astype(jnp.float32)
    weighted = (owner_table[:, None, :] * raw_grad[None, :, :]).reshape(
        regions * param_count, reach_dev
    )
    summed = jnp.dot(
        weighted, attributes.T, precision=lax.Precision.HIGHEST, preferred_element_type=jnp.float32
    )
    local_grad = jnp.transpose(summed.reshape(regions, param_count, attr_count), (0, 2, 1))
    basins = lax.axis_size("basin")
    owned_share = scattered_sum(
        local_grad.reshape(basins, owned_rows, attr_count, param_count), "basin"
    )
    grad_net = butterfly_sum(butterfly_sum(owned_share, "group"), "level")
    return (outflow, grad_net)


def solution(mesh):
    in_specs = (
        P("group", ("level", "basin")),
        P("group", ("level", "basin")),
        P(None, ("level", "basin")),
        P(("level", "basin")),
        P(None, ("level", "basin")),
        P(("level", "basin")),
        P(("level", "basin")),
        P(),
    )
    out_specs = (P("group", ("level", "basin")), P("basin", None, None))
    return jax.shard_map(body, mesh=mesh, in_specs=in_specs, out_specs=out_specs, check_vma=False)
```

```python
import functools

import jax
import jax.numpy as jnp
from jax import lax
from jax.sharding import PartitionSpec as P
from jax.experimental import pallas as pl
from jax.experimental.pallas import tpu as pltpu

BLOCK = 128


def shifted(value, axis, steps):
    count = lax.axis_size(axis)
    leading, last = (max(0, -steps), min(count, count - steps))
    return lax.ppermute(value, axis, [(source, source + steps) for source in range(leading, last)])


def diagonal(value, steps):
    levels, basins = lax.axis_size("level"), lax.axis_size("basin")
    pairs = []
    for level in range(max(0, -steps), min(levels, levels - steps)):
        for basin in range(max(0, -steps), min(basins, basins - steps)):
            pairs.append((level * basins + basin, (level + steps) * basins + basin + steps))
    return lax.ppermute(value, ("level", "basin"), pairs)


def exchanged(value, axis, mask):
    count = lax.axis_size(axis)
    return lax.ppermute(value, axis, [(source, source ^ mask) for source in range(count)])


def scattered_sum(blocks, axis):
    count, mine = (lax.axis_size(axis), lax.axis_index(axis))
    width = count
    while width > 1:
        width //= 2
        lower, upper = blocks[:width], blocks[width:]
        high = (mine & width) > 0
        kept = jnp.where(high, upper, lower)
        sent = jnp.where(high, lower, upper)
        blocks = kept + exchanged(sent, axis, width)
    return blocks[0]


def butterfly_sum(value, axis):
    mask = 1
    while mask < lax.axis_size(axis):
        value = value + exchanged(value, axis, mask)
        mask *= 2
    return value


def whole_window(value):
    return lax.all_gather(value, "group", axis=0, tiled=True)


def carried_in(value, axis, join, neutral, backward):
    count, mine = (lax.axis_size(axis), lax.axis_index(axis))
    pieces = lax.all_gather(value, axis)
    if backward:
        pieces = pieces[::-1]
        mine = count - 1 - mine
    subtotal = jnp.full_like(value, 0) + jnp.asarray(neutral, value.dtype)

    def turn(position, subtotal):
        longer = join(subtotal, pieces[position])
        return jnp.where(position < mine, longer, subtotal)

    return lax.fori_loop(0, count - 1, turn, subtotal)


def recurrence_kernel(retain_ref, drive_ref, out_ref, *, reverse):
    steps = drive_ref.shape[0]
    keep = retain_ref[...]

    def advance(position, state):
        hour = steps - 1 - position if reverse else position
        state = keep * state + drive_ref[pl.ds(hour, 1), :]
        out_ref[pl.ds(hour, 1), :] = state
        return state

    lax.fori_loop(0, steps, advance, jnp.zeros_like(keep), unroll=8)


def recurrence(retain_row, drive, reverse=False):
    steps, width = drive.shape
    return pl.pallas_call(
        functools.partial(recurrence_kernel, reverse=reverse),
        out_shape=jax.ShapeDtypeStruct((steps, width), jnp.float32),
        in_specs=[pl.BlockSpec(memory_space=pltpu.VMEM), pl.BlockSpec(memory_space=pltpu.VMEM)],
        out_specs=pl.BlockSpec(memory_space=pltpu.VMEM),
        cost_estimate=pl.CostEstimate(
            flops=2 * steps * width, transcendentals=0, bytes_accessed=8 * steps * width + 4 * width
        ),
    )(retain_row, drive)


def coefficients(raw_params):
    travel = 1.0 + 47.0 * jax.nn.sigmoid(raw_params[0])
    weighting = 0.05 + 0.4 * jax.nn.sigmoid(raw_params[1])
    storage = travel * (1.0 - weighting)
    divisor = storage + 0.5
    return (
        (0.5 - travel * weighting) / divisor,
        (0.5 + travel * weighting) / divisor,
        (storage - 0.5) / divisor,
        1.0 / divisor,
    )


def affine_join(earlier, latter):
    return (earlier[0] * latter[0], latter[0] * earlier[1] + latter[1])


def stack_affine(pair):
    return jnp.stack([pair[0], pair[1]], axis=0)


def split_affine(stacked):
    return (stacked[0], stacked[1])


def stacked_affine(earlier, latter):
    return stack_affine(affine_join(split_affine(earlier), split_affine(latter)))


def body(lateral, cotangent, attributes, region, feeders, feeder_count, live_blocks, net_weight):
    steps_dev, reach_dev = lateral.shape
    outlets = reach_dev // 8
    regions, attr_count, param_count = net_weight.shape
    levels = lax.axis_size("level")
    up_count = feeders.shape[0]
    mine = lax.axis_index("group")
    slot_ids = lax.broadcasted_iota(jnp.int32, (reach_dev,), 0)
    live_mask = (slot_ids < live_blocks[0] * BLOCK).astype(jnp.float32)
    member_table = (
        region[None, :] == lax.broadcasted_iota(jnp.int32, (regions, reach_dev), 0)
    ).astype(jnp.float32)
    per_region = jnp.dot(
        jnp.transpose(net_weight, (0, 2, 1)).reshape(regions * param_count, attr_count),
        attributes,
        precision=lax.Precision.HIGHEST,
        preferred_element_type=jnp.float32,
    )
    raw_params = jnp.einsum(
        "rpi,ri->pi",
        per_region.reshape(regions, param_count, reach_dev),
        member_table,
        precision=lax.Precision.HIGHEST,
    )
    coef_set, coef_pull = jax.vjp(coefficients, raw_params)
    gain_now, gain_prev, retain, gain_side = coef_set
    lateral_all = whole_window(lateral)
    cotangent_all = whole_window(cotangent)
    steps_all = lateral_all.shape[0]
    source_ids = lax.broadcasted_iota(jnp.int32, (reach_dev + outlets, reach_dev), 0)
    confluence = jnp.zeros((reach_dev + outlets, reach_dev), jnp.float32)
    for upslot in range(up_count):
        confluence = confluence + (
            (source_ids == feeders[upslot][None, :]) & (upslot < feeder_count)[None, :]
        ).astype(jnp.float32)
    retain_row = retain[None, :]
    zero_flow = jnp.zeros((steps_all, reach_dev), jnp.float32)
    zero_row = jnp.zeros((1, reach_dev), jnp.float32)

    def own_half(value):
        return lax.dynamic_slice_in_dim(value, mine * steps_dev, steps_dev, axis=0)

    def route_level(inflow):
        inflow_before = jnp.concatenate([zero_row, inflow[:-1]], axis=0)
        drive = gain_now * inflow + gain_prev * inflow_before + gain_side * lateral_all
        flow = recurrence(retain_row, drive)
        return flow * live_mask

    inflow = zero_flow
    outflow = route_level(inflow)
    for level_step in range(levels - 1):
        upper_flow = whole_window(shifted(own_half(outflow), "level", 1))
        side_flow = diagonal(outflow[:, :outlets], 1)
        source = jnp.concatenate([upper_flow, side_flow], axis=1)
        inflow = jnp.dot(
            source, confluence, precision=lax.Precision.HIGHEST, preferred_element_type=jnp.float32
        )
        outflow = route_level(inflow)
    adjoint_down = zero_flow
    adjoint = zero_flow
    for level_step in range(levels):
        adjoint_load = live_mask * (cotangent_all + adjoint_down)
        adjoint = recurrence(retain_row, adjoint_load, reverse=True)
        if level_step + 1 < levels:
            later_adj = jnp.concatenate([adjoint[1:], zero_row], axis=0)
            to_inflow = gain_now * adjoint + gain_prev * later_adj
            spread = lax.dot_general(
                to_inflow,
                confluence,
                (((1,), (1,)), ((), ())),
                precision=lax.Precision.HIGHEST,
                preferred_element_type=jnp.float32,
            )
            returned = diagonal(spread[:, reach_dev:], -1)
            own_part = whole_window(shifted(own_half(spread[:, :reach_dev]), "level", -1))
            adjoint_down = own_part.at[:, :outlets].add(returned)
    flow_before = jnp.concatenate([zero_row, outflow[:-1]], axis=0)
    inflow_before = jnp.concatenate([zero_row, inflow[:-1]], axis=0)
    coef_grads = (
        jnp.sum(adjoint * inflow, axis=0),
        jnp.sum(adjoint * inflow_before, axis=0),
        jnp.sum(adjoint * flow_before, axis=0),
        jnp.sum(adjoint * lateral_all, axis=0),
    )
    raw_grad = coef_pull(coef_grads)[0]
    owned_rows = regions // lax.axis_size("basin")
    weighted = (member_table[:, None, :] * raw_grad[None, :, :]).reshape(
        regions * param_count, reach_dev
    )
    summed = jnp.dot(
        weighted, attributes.T, precision=lax.Precision.HIGHEST, preferred_element_type=jnp.float32
    )
    local_grad = jnp.transpose(summed.reshape(regions, param_count, attr_count), (0, 2, 1))
    basins = lax.axis_size("basin")
    owned_share = scattered_sum(
        local_grad.reshape(basins, owned_rows, attr_count, param_count), "basin"
    )
    grad_net = butterfly_sum(owned_share, "level")
    return (own_half(outflow), grad_net)


def solution(mesh):
    in_specs = (
        P("group", ("level", "basin")),
        P("group", ("level", "basin")),
        P(None, ("level", "basin")),
        P(("level", "basin")),
        P(None, ("level", "basin")),
        P(("level", "basin")),
        P(("level", "basin")),
        P(),
    )
    out_specs = (P("group", ("level", "basin")), P("basin", None, None))
    return jax.shard_map(body, mesh=mesh, in_specs=in_specs, out_specs=out_specs, check_vma=False)
```

```python
import functools

import jax
import jax.numpy as jnp
from jax import lax
from jax.sharding import PartitionSpec as P
from jax.experimental import pallas as pl
from jax.experimental.pallas import tpu as pltpu

BLOCK = 128


def shifted(value, axis, steps):
    count = lax.axis_size(axis)
    leading, last = (max(0, -steps), min(count, count - steps))
    return lax.ppermute(value, axis, [(source, source + steps) for source in range(leading, last)])


def diagonal(value, steps):
    levels, basins = lax.axis_size("level"), lax.axis_size("basin")
    pairs = []
    for level in range(max(0, -steps), min(levels, levels - steps)):
        for basin in range(max(0, -steps), min(basins, basins - steps)):
            pairs.append((level * basins + basin, (level + steps) * basins + basin + steps))
    return lax.ppermute(value, ("level", "basin"), pairs)


def exchanged(value, axis, mask):
    count = lax.axis_size(axis)
    return lax.ppermute(value, axis, [(source, source ^ mask) for source in range(count)])


def scattered_sum(blocks, axis):
    count, mine = (lax.axis_size(axis), lax.axis_index(axis))
    width = count
    while width > 1:
        width //= 2
        lower, upper = blocks[:width], blocks[width:]
        high = (mine & width) > 0
        kept = jnp.where(high, upper, lower)
        sent = jnp.where(high, lower, upper)
        blocks = kept + exchanged(sent, axis, width)
    return blocks[0]


def butterfly_sum(value, axis):
    mask = 1
    while mask < lax.axis_size(axis):
        value = value + exchanged(value, axis, mask)
        mask *= 2
    return value


def whole_window(value):
    return lax.all_gather(value, "group", axis=0, tiled=True)


def carried_in(value, axis, join, neutral, backward):
    count, mine = (lax.axis_size(axis), lax.axis_index(axis))
    pieces = lax.all_gather(value, axis)
    if backward:
        pieces = pieces[::-1]
        mine = count - 1 - mine
    subtotal = jnp.full_like(value, 0) + jnp.asarray(neutral, value.dtype)

    def turn(position, subtotal):
        longer = join(subtotal, pieces[position])
        return jnp.where(position < mine, longer, subtotal)

    return lax.fori_loop(0, count - 1, turn, subtotal)


def recurrence_kernel(retain_ref, drive_ref, out_ref, *, reverse):
    steps = drive_ref.shape[0]
    keep = retain_ref[...]

    def advance(position, state):
        hour = steps - 1 - position if reverse else position
        state = keep * state + drive_ref[pl.ds(hour, 1), :]
        out_ref[pl.ds(hour, 1), :] = state
        return state

    lax.fori_loop(0, steps, advance, jnp.zeros_like(keep), unroll=8)


def recurrence(retain_row, drive, reverse=False):
    steps, width = drive.shape
    return pl.pallas_call(
        functools.partial(recurrence_kernel, reverse=reverse),
        out_shape=jax.ShapeDtypeStruct((steps, width), jnp.float32),
        in_specs=[pl.BlockSpec(memory_space=pltpu.VMEM), pl.BlockSpec(memory_space=pltpu.VMEM)],
        out_specs=pl.BlockSpec(memory_space=pltpu.VMEM),
        cost_estimate=pl.CostEstimate(
            flops=2 * steps * width, transcendentals=0, bytes_accessed=8 * steps * width + 4 * width
        ),
    )(retain_row, drive)


def split_three(value):
    pieces = []
    rest = value
    for _ in range(3):
        piece = lax.reduce_precision(rest, exponent_bits=8, mantissa_bits=7)
        pieces.append(piece)
        rest = rest - piece
    return jnp.concatenate(pieces, axis=0).astype(jnp.bfloat16)


def joined_three(product):
    rows = product.shape[0] // 3
    return (product[:rows] + product[rows : 2 * rows]) + product[2 * rows :]


def coefficients(raw_params):
    travel = 1.0 + 47.0 * jax.nn.sigmoid(raw_params[0])
    weighting = 0.05 + 0.4 * jax.nn.sigmoid(raw_params[1])
    storage = travel * (1.0 - weighting)
    divisor = storage + 0.5
    return (
        (0.5 - travel * weighting) / divisor,
        (0.5 + travel * weighting) / divisor,
        (storage - 0.5) / divisor,
        1.0 / divisor,
    )


def affine_join(earlier, latter):
    return (earlier[0] * latter[0], latter[0] * earlier[1] + latter[1])


def stack_affine(pair):
    return jnp.stack([pair[0], pair[1]], axis=0)


def split_affine(stacked):
    return (stacked[0], stacked[1])


def stacked_affine(earlier, latter):
    return stack_affine(affine_join(split_affine(earlier), split_affine(latter)))


def body(lateral, cotangent, attributes, region, feeders, feeder_count, live_blocks, net_weight):
    steps_dev, reach_dev = lateral.shape
    outlets = reach_dev // 8
    regions, attr_count, param_count = net_weight.shape
    levels = lax.axis_size("level")
    up_count = feeders.shape[0]
    mine = lax.axis_index("group")
    slot_ids = lax.broadcasted_iota(jnp.int32, (reach_dev,), 0)
    live_mask = (slot_ids < live_blocks[0] * BLOCK).astype(jnp.float32)
    member_table = (
        region[None, :] == lax.broadcasted_iota(jnp.int32, (regions, reach_dev), 0)
    ).astype(jnp.float32)
    per_region = jnp.dot(
        jnp.transpose(net_weight, (0, 2, 1)).reshape(regions * param_count, attr_count),
        attributes,
        precision=lax.Precision.HIGHEST,
        preferred_element_type=jnp.float32,
    )
    raw_params = jnp.einsum(
        "rpi,ri->pi",
        per_region.reshape(regions, param_count, reach_dev),
        member_table,
        precision=lax.Precision.HIGHEST,
    )
    coef_set, coef_pull = jax.vjp(coefficients, raw_params)
    gain_now, gain_prev, retain, gain_side = coef_set
    lateral_all = whole_window(lateral)
    cotangent_all = whole_window(cotangent)
    steps_all = lateral_all.shape[0]
    source_ids = lax.broadcasted_iota(jnp.int32, (reach_dev + outlets, reach_dev), 0)
    confluence = jnp.zeros((reach_dev + outlets, reach_dev), jnp.float32)
    for upslot in range(up_count):
        confluence = confluence + (
            (source_ids == feeders[upslot][None, :]) & (upslot < feeder_count)[None, :]
        ).astype(jnp.float32)
    confluence = confluence.astype(jnp.bfloat16)
    retain_row = retain[None, :]
    zero_flow = jnp.zeros((steps_all, reach_dev), jnp.float32)
    zero_row = jnp.zeros((1, reach_dev), jnp.float32)

    def own_half(value):
        return lax.dynamic_slice_in_dim(value, mine * steps_dev, steps_dev, axis=0)

    def route_level(inflow):
        inflow_before = jnp.concatenate([zero_row, inflow[:-1]], axis=0)
        drive = gain_now * inflow + gain_prev * inflow_before + gain_side * lateral_all
        flow = recurrence(retain_row, drive)
        return flow * live_mask

    inflow = zero_flow
    outflow = route_level(inflow)
    for level_step in range(levels - 1):
        upper_flow = whole_window(shifted(own_half(outflow), "level", 1))
        side_flow = diagonal(outflow[:, :outlets], 1)
        source = jnp.concatenate([upper_flow, side_flow], axis=1)
        inflow = joined_three(
            jnp.dot(split_three(source), confluence, preferred_element_type=jnp.float32)
        )
        outflow = route_level(inflow)
    adjoint_down = zero_flow
    adjoint = zero_flow
    for level_step in range(levels):
        adjoint_load = live_mask * (cotangent_all + adjoint_down)
        adjoint = recurrence(retain_row, adjoint_load, reverse=True)
        if level_step + 1 < levels:
            later_adj = jnp.concatenate([adjoint[1:], zero_row], axis=0)
            to_inflow = gain_now * adjoint + gain_prev * later_adj
            spread = joined_three(
                lax.dot_general(
                    split_three(to_inflow),
                    confluence,
                    (((1,), (1,)), ((), ())),
                    preferred_element_type=jnp.float32,
                )
            )
            returned = diagonal(spread[:, reach_dev:], -1)
            own_part = whole_window(shifted(own_half(spread[:, :reach_dev]), "level", -1))
            adjoint_down = own_part.at[:, :outlets].add(returned)
    flow_before = jnp.concatenate([zero_row, outflow[:-1]], axis=0)
    inflow_before = jnp.concatenate([zero_row, inflow[:-1]], axis=0)
    coef_grads = (
        jnp.sum(adjoint * inflow, axis=0),
        jnp.sum(adjoint * inflow_before, axis=0),
        jnp.sum(adjoint * flow_before, axis=0),
        jnp.sum(adjoint * lateral_all, axis=0),
    )
    raw_grad = coef_pull(coef_grads)[0]
    owned_rows = regions // lax.axis_size("basin")
    weighted = (member_table[:, None, :] * raw_grad[None, :, :]).reshape(
        regions * param_count, reach_dev
    )
    summed = jnp.dot(
        weighted, attributes.T, precision=lax.Precision.HIGHEST, preferred_element_type=jnp.float32
    )
    local_grad = jnp.transpose(summed.reshape(regions, param_count, attr_count), (0, 2, 1))
    basins = lax.axis_size("basin")
    owned_share = scattered_sum(
        local_grad.reshape(basins, owned_rows, attr_count, param_count), "basin"
    )
    grad_net = butterfly_sum(owned_share, "level")
    return (own_half(outflow), grad_net)


def solution(mesh):
    in_specs = (
        P("group", ("level", "basin")),
        P("group", ("level", "basin")),
        P(None, ("level", "basin")),
        P(("level", "basin")),
        P(None, ("level", "basin")),
        P(("level", "basin")),
        P(("level", "basin")),
        P(),
    )
    out_specs = (P("group", ("level", "basin")), P("basin", None, None))
    return jax.shard_map(body, mesh=mesh, in_specs=in_specs, out_specs=out_specs, check_vma=False)
```

```python
import functools

import jax
import jax.numpy as jnp
from jax import lax
from jax.sharding import PartitionSpec as P
from jax.experimental import pallas as pl
from jax.experimental.pallas import tpu as pltpu

BLOCK = 128


def shifted(value, axis, steps):
    count = lax.axis_size(axis)
    leading, last = (max(0, -steps), min(count, count - steps))
    return lax.ppermute(value, axis, [(source, source + steps) for source in range(leading, last)])


def diagonal(value, steps):
    levels, basins = lax.axis_size("level"), lax.axis_size("basin")
    pairs = []
    for level in range(max(0, -steps), min(levels, levels - steps)):
        for basin in range(max(0, -steps), min(basins, basins - steps)):
            pairs.append((level * basins + basin, (level + steps) * basins + basin + steps))
    return lax.ppermute(value, ("level", "basin"), pairs)


def exchanged(value, axis, mask):
    count = lax.axis_size(axis)
    return lax.ppermute(value, axis, [(source, source ^ mask) for source in range(count)])


def scattered_sum(blocks, axis):
    count, mine = (lax.axis_size(axis), lax.axis_index(axis))
    width = count
    while width > 1:
        width //= 2
        lower, upper = blocks[:width], blocks[width:]
        high = (mine & width) > 0
        kept = jnp.where(high, upper, lower)
        sent = jnp.where(high, lower, upper)
        blocks = kept + exchanged(sent, axis, width)
    return blocks[0]


def butterfly_sum(value, axis):
    mask = 1
    while mask < lax.axis_size(axis):
        value = value + exchanged(value, axis, mask)
        mask *= 2
    return value


def whole_window(value):
    return lax.all_gather(value, "group", axis=0, tiled=True)


def carried_in(value, axis, join, neutral, backward):
    count, mine = (lax.axis_size(axis), lax.axis_index(axis))
    pieces = lax.all_gather(value, axis)
    if backward:
        pieces = pieces[::-1]
        mine = count - 1 - mine
    subtotal = jnp.full_like(value, 0) + jnp.asarray(neutral, value.dtype)

    def turn(position, subtotal):
        longer = join(subtotal, pieces[position])
        return jnp.where(position < mine, longer, subtotal)

    return lax.fori_loop(0, count - 1, turn, subtotal)


def recurrence_kernel(retain_ref, drive_ref, out_ref, *, reverse):
    steps = drive_ref.shape[0]
    keep = retain_ref[...]

    def advance(position, state):
        hour = steps - 1 - position if reverse else position
        state = keep * state + drive_ref[pl.ds(hour, 1), :]
        out_ref[pl.ds(hour, 1), :] = state
        return state

    lax.fori_loop(0, steps, advance, jnp.zeros_like(keep), unroll=8)


def recurrence(retain_row, drive, reverse=False):
    steps, width = drive.shape
    return pl.pallas_call(
        functools.partial(recurrence_kernel, reverse=reverse),
        out_shape=jax.ShapeDtypeStruct((steps, width), jnp.float32),
        in_specs=[pl.BlockSpec(memory_space=pltpu.VMEM), pl.BlockSpec(memory_space=pltpu.VMEM)],
        out_specs=pl.BlockSpec(memory_space=pltpu.VMEM),
        cost_estimate=pl.CostEstimate(
            flops=2 * steps * width, transcendentals=0, bytes_accessed=8 * steps * width + 4 * width
        ),
    )(retain_row, drive)


def split_three(value):
    pieces = []
    rest = value
    for _ in range(3):
        piece = lax.reduce_precision(rest, exponent_bits=8, mantissa_bits=7)
        pieces.append(piece)
        rest = rest - piece
    return jnp.concatenate(pieces, axis=0).astype(jnp.bfloat16)


def joined_three(product):
    rows = product.shape[0] // 3
    return (product[:rows] + product[rows : 2 * rows]) + product[2 * rows :]


def coefficients(raw_params):
    travel = 1.0 + 47.0 * jax.nn.sigmoid(raw_params[0])
    weighting = 0.05 + 0.4 * jax.nn.sigmoid(raw_params[1])
    storage = travel * (1.0 - weighting)
    divisor = storage + 0.5
    return (
        (0.5 - travel * weighting) / divisor,
        (0.5 + travel * weighting) / divisor,
        (storage - 0.5) / divisor,
        1.0 / divisor,
    )


def affine_join(earlier, latter):
    return (earlier[0] * latter[0], latter[0] * earlier[1] + latter[1])


def stack_affine(pair):
    return jnp.stack([pair[0], pair[1]], axis=0)


def split_affine(stacked):
    return (stacked[0], stacked[1])


def stacked_affine(earlier, latter):
    return stack_affine(affine_join(split_affine(earlier), split_affine(latter)))


def body(lateral, cotangent, attributes, region, feeders, feeder_count, live_blocks, net_weight):
    steps_dev, reach_dev = lateral.shape
    outlets = reach_dev // 8
    regions, attr_count, param_count = net_weight.shape
    levels = lax.axis_size("level")
    up_count = feeders.shape[0]
    mine = lax.axis_index("group")
    slot_ids = lax.broadcasted_iota(jnp.int32, (reach_dev,), 0)
    live_mask = (slot_ids < live_blocks[0] * BLOCK).astype(jnp.float32)
    member_table = (
        region[None, :] == lax.broadcasted_iota(jnp.int32, (regions, reach_dev), 0)
    ).astype(jnp.float32)
    per_region = jnp.dot(
        jnp.transpose(net_weight, (0, 2, 1)).reshape(regions * param_count, attr_count),
        attributes,
        precision=lax.Precision.HIGHEST,
        preferred_element_type=jnp.float32,
    )
    raw_params = jnp.einsum(
        "rpi,ri->pi",
        per_region.reshape(regions, param_count, reach_dev),
        member_table,
        precision=lax.Precision.HIGHEST,
    )
    coef_set, coef_pull = jax.vjp(coefficients, raw_params)
    gain_now, gain_prev, retain, gain_side = coef_set
    lateral_all = whole_window(lateral)
    cotangent_all = whole_window(cotangent)
    steps_all = lateral_all.shape[0]
    source_ids = lax.broadcasted_iota(jnp.int32, (reach_dev + outlets, reach_dev), 0)
    confluence = jnp.zeros((reach_dev + outlets, reach_dev), jnp.float32)
    for upslot in range(up_count):
        confluence = confluence + (
            (source_ids == feeders[upslot][None, :]) & (upslot < feeder_count)[None, :]
        ).astype(jnp.float32)
    confluence = confluence.astype(jnp.bfloat16)
    retain_row = retain[None, :]
    zero_flow = jnp.zeros((steps_all, reach_dev), jnp.float32)
    zero_row = jnp.zeros((1, reach_dev), jnp.float32)

    def own_half(value):
        return lax.dynamic_slice_in_dim(value, mine * steps_dev, steps_dev, axis=0)

    def route_level(inflow):
        inflow_before = jnp.concatenate([zero_row, inflow[:-1]], axis=0)
        drive = gain_now * inflow + gain_prev * inflow_before + gain_side * lateral_all
        flow = recurrence(retain_row, drive)
        return flow * live_mask

    inflow = zero_flow
    outflow = route_level(inflow)
    for level_step in range(levels - 1):
        upper_flow = whole_window(shifted(own_half(outflow), "level", 1))
        side_flow = diagonal(outflow[:, :outlets], 1)
        source = jnp.concatenate([upper_flow, side_flow], axis=1)
        inflow = joined_three(
            jnp.dot(split_three(source), confluence, preferred_element_type=jnp.float32)
        )
        outflow = route_level(inflow)
    adjoint_down = zero_flow
    adjoint = zero_flow
    for level_step in range(levels):
        adjoint_load = live_mask * (cotangent_all + adjoint_down)
        adjoint = recurrence(retain_row, adjoint_load, reverse=True)
        if level_step + 1 < levels:
            later_adj = jnp.concatenate([adjoint[1:], zero_row], axis=0)
            to_inflow = gain_now * adjoint + gain_prev * later_adj
            spread = joined_three(
                lax.dot_general(
                    split_three(to_inflow),
                    confluence,
                    (((1,), (1,)), ((), ())),
                    preferred_element_type=jnp.float32,
                )
            )
            returned = diagonal(spread[:, reach_dev:], -1)
            own_part = whole_window(shifted(own_half(spread[:, :reach_dev]), "level", -1))
            adjoint_down = own_part.at[:, :outlets].add(returned)
    flow_before = jnp.concatenate([zero_row, outflow[:-1]], axis=0)
    inflow_before = jnp.concatenate([zero_row, inflow[:-1]], axis=0)
    coef_grads = (
        jnp.sum(adjoint * inflow, axis=0),
        jnp.sum(adjoint * inflow_before, axis=0),
        jnp.sum(adjoint * flow_before, axis=0),
        jnp.sum(adjoint * lateral_all, axis=0),
    )
    raw_grad = coef_pull(coef_grads)[0]
    owned_rows = regions // lax.axis_size("basin")
    weighted = (member_table[:, None, :] * raw_grad[None, :, :]).reshape(
        regions * param_count, reach_dev
    )
    summed = jnp.dot(
        weighted, attributes.T, precision=lax.Precision.HIGHEST, preferred_element_type=jnp.float32
    )
    local_grad = jnp.transpose(summed.reshape(regions, param_count, attr_count), (0, 2, 1))
    basins = lax.axis_size("basin")
    share_size = owned_rows * attr_count * param_count
    replicated = jnp.broadcast_to(
        local_grad.reshape(1, basins, share_size), (levels, basins, share_size)
    ).reshape(levels * basins, share_size)
    grad_net = jnp.sum(
        lax.all_to_all(replicated, ("level", "basin"), 0, 0, tiled=True), axis=0
    ).reshape(owned_rows, attr_count, param_count)
    return (own_half(outflow), grad_net)


def solution(mesh):
    in_specs = (
        P("group", ("level", "basin")),
        P("group", ("level", "basin")),
        P(None, ("level", "basin")),
        P(("level", "basin")),
        P(None, ("level", "basin")),
        P(("level", "basin")),
        P(("level", "basin")),
        P(),
    )
    out_specs = (P("group", ("level", "basin")), P("basin", None, None))
    return jax.shard_map(body, mesh=mesh, in_specs=in_specs, out_specs=out_specs, check_vma=False)
```

```python
import functools

import jax
import jax.numpy as jnp
from jax import lax
from jax.sharding import PartitionSpec as P
from jax.experimental import pallas as pl
from jax.experimental.pallas import tpu as pltpu

BLOCK = 128


def shifted(value, axis, steps):
    count = lax.axis_size(axis)
    leading, last = (max(0, -steps), min(count, count - steps))
    return lax.ppermute(value, axis, [(source, source + steps) for source in range(leading, last)])


def diagonal(value, steps):
    levels, basins = lax.axis_size("level"), lax.axis_size("basin")
    pairs = []
    for level in range(max(0, -steps), min(levels, levels - steps)):
        for basin in range(max(0, -steps), min(basins, basins - steps)):
            pairs.append((level * basins + basin, (level + steps) * basins + basin + steps))
    return lax.ppermute(value, ("level", "basin"), pairs)


def exchanged(value, axis, mask):
    count = lax.axis_size(axis)
    return lax.ppermute(value, axis, [(source, source ^ mask) for source in range(count)])


def scattered_sum(blocks, axis):
    count, mine = (lax.axis_size(axis), lax.axis_index(axis))
    width = count
    while width > 1:
        width //= 2
        lower, upper = blocks[:width], blocks[width:]
        high = (mine & width) > 0
        kept = jnp.where(high, upper, lower)
        sent = jnp.where(high, lower, upper)
        blocks = kept + exchanged(sent, axis, width)
    return blocks[0]


def butterfly_sum(value, axis):
    mask = 1
    while mask < lax.axis_size(axis):
        value = value + exchanged(value, axis, mask)
        mask *= 2
    return value


def whole_window(value):
    return lax.all_gather(value, "group", axis=0, tiled=True)


def carried_in(value, axis, join, neutral, backward):
    count, mine = (lax.axis_size(axis), lax.axis_index(axis))
    pieces = lax.all_gather(value, axis)
    if backward:
        pieces = pieces[::-1]
        mine = count - 1 - mine
    subtotal = jnp.full_like(value, 0) + jnp.asarray(neutral, value.dtype)

    def turn(position, subtotal):
        longer = join(subtotal, pieces[position])
        return jnp.where(position < mine, longer, subtotal)

    return lax.fori_loop(0, count - 1, turn, subtotal)


def recurrence_kernel(retain_ref, drive_ref, out_ref, *, reverse):
    steps = drive_ref.shape[0]
    keep = retain_ref[...]

    def advance(position, state):
        hour = steps - 1 - position if reverse else position
        state = keep * state + drive_ref[pl.ds(hour, 1), :]
        out_ref[pl.ds(hour, 1), :] = state
        return state

    lax.fori_loop(0, steps, advance, jnp.zeros_like(keep), unroll=8)


def recurrence(retain_row, drive, reverse=False):
    steps, width = drive.shape
    return pl.pallas_call(
        functools.partial(recurrence_kernel, reverse=reverse),
        out_shape=jax.ShapeDtypeStruct((steps, width), jnp.float32),
        in_specs=[pl.BlockSpec(memory_space=pltpu.VMEM), pl.BlockSpec(memory_space=pltpu.VMEM)],
        out_specs=pl.BlockSpec(memory_space=pltpu.VMEM),
        cost_estimate=pl.CostEstimate(
            flops=2 * steps * width, transcendentals=0, bytes_accessed=8 * steps * width + 4 * width
        ),
    )(retain_row, drive)


def forward_kernel(*refs, has_inflow):
    if has_inflow:
        coef_ref, product_ref, lateral_ref, out_ref, outlet_ref, inflow_ref = refs
    else:
        coef_ref, lateral_ref, out_ref, outlet_ref = refs
    steps = lateral_ref.shape[0]
    narrow = outlet_ref.shape[1]
    gain_now, gain_prev, gain_side = coef_ref[0:1, :], coef_ref[1:2, :], coef_ref[2:3, :]
    keep, live = coef_ref[3:4, :], coef_ref[4:5, :]

    def advance(hour, carry):
        state, before = carry
        side_in = lateral_ref[pl.ds(hour, 1), :]
        if has_inflow:
            now = (
                product_ref[pl.ds(hour, 1), :] + product_ref[pl.ds(hour + steps, 1), :]
            ) + product_ref[pl.ds(hour + 2 * steps, 1), :]
            inflow_ref[pl.ds(hour, 1), :] = now
            drive = (gain_now * now + gain_prev * before) + gain_side * side_in
        else:
            now = before
            drive = gain_side * side_in
        state = keep * state + drive
        flow = state * live
        out_ref[pl.ds(hour, 1), :] = flow
        outlet_ref[pl.ds(hour, 1), :] = flow[:, :narrow]
        return state, now

    zero = jnp.zeros_like(keep)
    lax.fori_loop(0, steps, advance, (zero, zero), unroll=8)


def backward_kernel(*refs, has_down, emit):
    refs = list(refs)
    coef_ref, cot_ref = refs[0], refs[1]
    rest = refs[2:]
    if has_down:
        down_ref, side_ref = rest[0], rest[1]
        rest = rest[2:]
    adj_ref = rest[0]
    piece_ref = rest[1] if emit else None
    steps = cot_ref.shape[0]
    gain_now, gain_prev = coef_ref[0:1, :], coef_ref[1:2, :]
    keep, live = coef_ref[3:4, :], coef_ref[4:5, :]

    def advance(position, carry):
        hour = steps - 1 - position
        state, later = carry
        load = cot_ref[pl.ds(hour, 1), :]
        if has_down:
            down = down_ref[pl.ds(hour, 1), :]
            side = side_ref[pl.ds(hour, 1), :]
            narrow = side.shape[1]
            down = jnp.concatenate([down[:, :narrow] + side, down[:, narrow:]], axis=1)
            load = load + down
        state = keep * state + live * load
        adj_ref[pl.ds(hour, 1), :] = state
        if emit:
            remainder = gain_now * state + gain_prev * later
            for piece_at in range(3):
                piece = remainder.astype(jnp.bfloat16).astype(jnp.float32)
                piece_ref[pl.ds(hour + piece_at * steps, 1), :] = piece
                remainder = remainder - piece
        return state, state

    zero = jnp.zeros_like(keep)
    lax.fori_loop(0, steps, advance, (zero, zero), unroll=8)


def vmem_call(kernel, outs, *args):
    steps, width = outs[0]
    return pl.pallas_call(
        kernel,
        out_shape=[jax.ShapeDtypeStruct(shape, jnp.float32) for shape in outs],
        in_specs=[pl.BlockSpec(memory_space=pltpu.VMEM)] * len(args),
        out_specs=[pl.BlockSpec(memory_space=pltpu.VMEM)] * len(outs),
        cost_estimate=pl.CostEstimate(
            flops=10 * steps * width,
            transcendentals=0,
            bytes_accessed=4 * (sum(a.size for a in args) + sum(r * c for r, c in outs)),
        ),
    )(*args)


def routed(coef, lateral_all, product=None):
    steps, width = lateral_all.shape
    narrow = width // 8
    if product is None:
        kernel = functools.partial(forward_kernel, has_inflow=False)
        flow, outlet = vmem_call(kernel, [(steps, width), (steps, narrow)], coef, lateral_all)
        return flow, outlet, None
    kernel = functools.partial(forward_kernel, has_inflow=True)
    return vmem_call(
        kernel, [(steps, width), (steps, narrow), (steps, width)], coef, product, lateral_all
    )


def adjoined(coef, cotangent_all, down=None, side=None, emit=True):
    steps, width = cotangent_all.shape
    kernel = functools.partial(backward_kernel, has_down=down is not None, emit=emit)
    args = (coef, cotangent_all) if down is None else (coef, cotangent_all, down, side)
    outs = [(steps, width)] + ([(3 * steps, width)] if emit else [])
    results = vmem_call(kernel, outs, *args)
    return results[0], (results[1] if emit else None)


def split_three(value):
    pieces = []
    rest = value
    for _ in range(3):
        piece = lax.reduce_precision(rest, exponent_bits=8, mantissa_bits=7)
        pieces.append(piece)
        rest = rest - piece
    return jnp.concatenate(pieces, axis=0).astype(jnp.bfloat16)


def joined_three(product):
    rows = product.shape[0] // 3
    return (product[:rows] + product[rows : 2 * rows]) + product[2 * rows :]


def coefficients(raw_params):
    travel = 1.0 + 47.0 * jax.nn.sigmoid(raw_params[0])
    weighting = 0.05 + 0.4 * jax.nn.sigmoid(raw_params[1])
    storage = travel * (1.0 - weighting)
    divisor = storage + 0.5
    return (
        (0.5 - travel * weighting) / divisor,
        (0.5 + travel * weighting) / divisor,
        (storage - 0.5) / divisor,
        1.0 / divisor,
    )


def affine_join(earlier, latter):
    return (earlier[0] * latter[0], latter[0] * earlier[1] + latter[1])


def stack_affine(pair):
    return jnp.stack([pair[0], pair[1]], axis=0)


def split_affine(stacked):
    return (stacked[0], stacked[1])


def stacked_affine(earlier, latter):
    return stack_affine(affine_join(split_affine(earlier), split_affine(latter)))


def body(lateral, cotangent, attributes, region, feeders, feeder_count, live_blocks, net_weight):
    steps_dev, reach_dev = lateral.shape
    outlets = reach_dev // 8
    regions, attr_count, param_count = net_weight.shape
    levels = lax.axis_size("level")
    up_count = feeders.shape[0]
    mine = lax.axis_index("group")
    slot_ids = lax.broadcasted_iota(jnp.int32, (reach_dev,), 0)
    live_mask = (slot_ids < live_blocks[0] * BLOCK).astype(jnp.float32)
    member_table = (
        region[None, :] == lax.broadcasted_iota(jnp.int32, (regions, reach_dev), 0)
    ).astype(jnp.float32)
    per_region = jnp.dot(
        jnp.transpose(net_weight, (0, 2, 1)).reshape(regions * param_count, attr_count),
        attributes,
        precision=lax.Precision.HIGHEST,
        preferred_element_type=jnp.float32,
    )
    raw_params = jnp.einsum(
        "rpi,ri->pi",
        per_region.reshape(regions, param_count, reach_dev),
        member_table,
        precision=lax.Precision.HIGHEST,
    )
    coef_set, coef_pull = jax.vjp(coefficients, raw_params)
    gain_now, gain_prev, retain, gain_side = coef_set
    zero_row = jnp.zeros((reach_dev,), jnp.float32)
    coef = jnp.stack(
        [gain_now, gain_prev, gain_side, retain, live_mask, zero_row, zero_row, zero_row], axis=0
    )
    lateral_all = whole_window(lateral)
    cotangent_all = whole_window(cotangent)
    source_ids = lax.broadcasted_iota(jnp.int32, (reach_dev + outlets, reach_dev), 0)
    confluence = jnp.zeros((reach_dev + outlets, reach_dev), jnp.float32)
    for upslot in range(up_count):
        confluence = confluence + (
            (source_ids == feeders[upslot][None, :]) & (upslot < feeder_count)[None, :]
        ).astype(jnp.float32)
    confluence = confluence.astype(jnp.bfloat16)

    def own_half(value):
        return lax.dynamic_slice_in_dim(value, mine * steps_dev, steps_dev, axis=0)

    outflow, outlet_flow, inflow = routed(coef, lateral_all)
    for level_step in range(levels - 1):
        upper_flow = whole_window(shifted(own_half(outflow), "level", 1))
        side_flow = diagonal(outlet_flow, 1)
        source = jnp.concatenate([upper_flow, side_flow], axis=1)
        product = jnp.dot(split_three(source), confluence, preferred_element_type=jnp.float32)
        outflow, outlet_flow, inflow = routed(coef, lateral_all, product)
    adjoint, pieces = adjoined(coef, cotangent_all)
    for level_step in range(1, levels):
        spread = joined_three(
            lax.dot_general(
                pieces.astype(jnp.bfloat16),
                confluence,
                (((1,), (1,)), ((), ())),
                preferred_element_type=jnp.float32,
            )
        )
        returned = diagonal(spread[:, reach_dev:], -1)
        own_part = whole_window(shifted(own_half(spread[:, :reach_dev]), "level", -1))
        adjoint, pieces = adjoined(
            coef, cotangent_all, own_part, returned, emit=level_step + 1 < levels
        )
    zero_first = jnp.zeros((1, reach_dev), jnp.float32)
    flow_before = jnp.concatenate([zero_first, outflow[:-1]], axis=0)
    inflow_before = jnp.concatenate([zero_first, inflow[:-1]], axis=0)
    coef_grads = (
        jnp.sum(adjoint * inflow, axis=0),
        jnp.sum(adjoint * inflow_before, axis=0),
        jnp.sum(adjoint * flow_before, axis=0),
        jnp.sum(adjoint * lateral_all, axis=0),
    )
    raw_grad = coef_pull(coef_grads)[0]
    owned_rows = regions // lax.axis_size("basin")
    weighted = (member_table[:, None, :] * raw_grad[None, :, :]).reshape(
        regions * param_count, reach_dev
    )
    summed = jnp.dot(
        weighted, attributes.T, precision=lax.Precision.HIGHEST, preferred_element_type=jnp.float32
    )
    local_grad = jnp.transpose(summed.reshape(regions, param_count, attr_count), (0, 2, 1))
    basins = lax.axis_size("basin")
    share_size = owned_rows * attr_count * param_count
    replicated = jnp.broadcast_to(
        local_grad.reshape(1, basins, share_size), (levels, basins, share_size)
    ).reshape(levels * basins, share_size)
    grad_net = jnp.sum(
        lax.all_to_all(replicated, ("level", "basin"), 0, 0, tiled=True), axis=0
    ).reshape(owned_rows, attr_count, param_count)
    return (own_half(outflow), grad_net)


def solution(mesh):
    in_specs = (
        P("group", ("level", "basin")),
        P("group", ("level", "basin")),
        P(None, ("level", "basin")),
        P(("level", "basin")),
        P(None, ("level", "basin")),
        P(("level", "basin")),
        P(("level", "basin")),
        P(),
    )
    out_specs = (P("group", ("level", "basin")), P("basin", None, None))
    return jax.shard_map(body, mesh=mesh, in_specs=in_specs, out_specs=out_specs, check_vma=False)
```

```python
import functools

import jax
import jax.numpy as jnp
from jax import lax
from jax.sharding import PartitionSpec as P
from jax.experimental import pallas as pl
from jax.experimental.pallas import tpu as pltpu

BLOCK = 128


def shifted(value, axis, steps):
    count = lax.axis_size(axis)
    leading, last = (max(0, -steps), min(count, count - steps))
    return lax.ppermute(value, axis, [(source, source + steps) for source in range(leading, last)])


def diagonal(value, steps):
    levels, basins = lax.axis_size("level"), lax.axis_size("basin")
    pairs = []
    for level in range(max(0, -steps), min(levels, levels - steps)):
        for basin in range(max(0, -steps), min(basins, basins - steps)):
            pairs.append((level * basins + basin, (level + steps) * basins + basin + steps))
    return lax.ppermute(value, ("level", "basin"), pairs)


def exchanged(value, axis, mask):
    count = lax.axis_size(axis)
    return lax.ppermute(value, axis, [(source, source ^ mask) for source in range(count)])


def scattered_sum(blocks, axis):
    count, mine = (lax.axis_size(axis), lax.axis_index(axis))
    width = count
    while width > 1:
        width //= 2
        lower, upper = blocks[:width], blocks[width:]
        high = (mine & width) > 0
        kept = jnp.where(high, upper, lower)
        sent = jnp.where(high, lower, upper)
        blocks = kept + exchanged(sent, axis, width)
    return blocks[0]


def butterfly_sum(value, axis):
    mask = 1
    while mask < lax.axis_size(axis):
        value = value + exchanged(value, axis, mask)
        mask *= 2
    return value


def whole_window(value):
    return lax.all_gather(value, "group", axis=0, tiled=True)


def carried_in(value, axis, join, neutral, backward):
    count, mine = (lax.axis_size(axis), lax.axis_index(axis))
    pieces = lax.all_gather(value, axis)
    if backward:
        pieces = pieces[::-1]
        mine = count - 1 - mine
    subtotal = jnp.full_like(value, 0) + jnp.asarray(neutral, value.dtype)

    def turn(position, subtotal):
        longer = join(subtotal, pieces[position])
        return jnp.where(position < mine, longer, subtotal)

    return lax.fori_loop(0, count - 1, turn, subtotal)


def recurrence_kernel(retain_ref, drive_ref, out_ref, *, reverse):
    steps = drive_ref.shape[0]
    keep = retain_ref[...]

    def advance(position, state):
        hour = steps - 1 - position if reverse else position
        state = keep * state + drive_ref[pl.ds(hour, 1), :]
        out_ref[pl.ds(hour, 1), :] = state
        return state

    lax.fori_loop(0, steps, advance, jnp.zeros_like(keep), unroll=8)


def recurrence(retain_row, drive, reverse=False):
    steps, width = drive.shape
    return pl.pallas_call(
        functools.partial(recurrence_kernel, reverse=reverse),
        out_shape=jax.ShapeDtypeStruct((steps, width), jnp.float32),
        in_specs=[pl.BlockSpec(memory_space=pltpu.VMEM), pl.BlockSpec(memory_space=pltpu.VMEM)],
        out_specs=pl.BlockSpec(memory_space=pltpu.VMEM),
        cost_estimate=pl.CostEstimate(
            flops=2 * steps * width, transcendentals=0, bytes_accessed=8 * steps * width + 4 * width
        ),
    )(retain_row, drive)


def forward_kernel(*refs, has_inflow):
    if has_inflow:
        coef_ref, product_ref, lateral_ref, out_ref, outlet_ref, inflow_ref = refs
    else:
        coef_ref, lateral_ref, out_ref, outlet_ref = refs
    steps = lateral_ref.shape[0]
    narrow = outlet_ref.shape[1]
    gain_now, gain_prev, gain_side = coef_ref[0:1, :], coef_ref[1:2, :], coef_ref[2:3, :]
    keep, live = coef_ref[3:4, :], coef_ref[4:5, :]

    def advance(hour, carry):
        state, before = carry
        side_in = lateral_ref[pl.ds(hour, 1), :]
        if has_inflow:
            now = (
                product_ref[pl.ds(hour, 1), :] + product_ref[pl.ds(hour + steps, 1), :]
            ) + product_ref[pl.ds(hour + 2 * steps, 1), :]
            inflow_ref[pl.ds(hour, 1), :] = now
            drive = (gain_now * now + gain_prev * before) + gain_side * side_in
        else:
            now = before
            drive = gain_side * side_in
        state = keep * state + drive
        flow = state * live
        out_ref[pl.ds(hour, 1), :] = flow
        outlet_ref[pl.ds(hour, 1), :] = flow[:, :narrow]
        return state, now

    zero = jnp.zeros_like(keep)
    lax.fori_loop(0, steps, advance, (zero, zero), unroll=8)


def backward_kernel(*refs, has_down, emit):
    refs = list(refs)
    coef_ref, cot_ref = refs[0], refs[1]
    rest = refs[2:]
    if has_down:
        down_ref, side_ref = rest[0], rest[1]
        rest = rest[2:]
    adj_ref = rest[0]
    piece_ref = rest[1] if emit else None
    steps = cot_ref.shape[0]
    gain_now, gain_prev = coef_ref[0:1, :], coef_ref[1:2, :]
    keep, live = coef_ref[3:4, :], coef_ref[4:5, :]

    def advance(position, carry):
        hour = steps - 1 - position
        state, later = carry
        load = cot_ref[pl.ds(hour, 1), :]
        if has_down:
            down = down_ref[pl.ds(hour, 1), :]
            side = side_ref[pl.ds(hour, 1), :]
            narrow = side.shape[1]
            down = jnp.concatenate([down[:, :narrow] + side, down[:, narrow:]], axis=1)
            load = load + down
        state = keep * state + live * load
        adj_ref[pl.ds(hour, 1), :] = state
        if emit:
            remainder = gain_now * state + gain_prev * later
            for piece_at in range(3):
                piece = remainder.astype(jnp.bfloat16).astype(jnp.float32)
                piece_ref[pl.ds(hour + piece_at * steps, 1), :] = piece
                remainder = remainder - piece
        return state, state

    zero = jnp.zeros_like(keep)
    lax.fori_loop(0, steps, advance, (zero, zero), unroll=8)


def vmem_call(kernel, outs, *args):
    steps, width = outs[0]
    return pl.pallas_call(
        kernel,
        out_shape=[jax.ShapeDtypeStruct(shape, jnp.float32) for shape in outs],
        in_specs=[pl.BlockSpec(memory_space=pltpu.VMEM)] * len(args),
        out_specs=[pl.BlockSpec(memory_space=pltpu.VMEM)] * len(outs),
        cost_estimate=pl.CostEstimate(
            flops=10 * steps * width,
            transcendentals=0,
            bytes_accessed=4 * (sum(a.size for a in args) + sum(r * c for r, c in outs)),
        ),
    )(*args)


def routed(coef, lateral_all, product=None):
    steps, width = lateral_all.shape
    narrow = width // 8
    if product is None:
        kernel = functools.partial(forward_kernel, has_inflow=False)
        flow, outlet = vmem_call(kernel, [(steps, width), (steps, narrow)], coef, lateral_all)
        return flow, outlet, None
    kernel = functools.partial(forward_kernel, has_inflow=True)
    return vmem_call(
        kernel, [(steps, width), (steps, narrow), (steps, width)], coef, product, lateral_all
    )


def adjoined(coef, cotangent_all, down=None, side=None, emit=True):
    steps, width = cotangent_all.shape
    kernel = functools.partial(backward_kernel, has_down=down is not None, emit=emit)
    args = (coef, cotangent_all) if down is None else (coef, cotangent_all, down, side)
    outs = [(steps, width)] + ([(3 * steps, width)] if emit else [])
    results = vmem_call(kernel, outs, *args)
    return results[0], (results[1] if emit else None)


def split_three(value):
    pieces = []
    rest = value
    for _ in range(3):
        piece = lax.reduce_precision(rest, exponent_bits=8, mantissa_bits=7)
        pieces.append(piece)
        rest = rest - piece
    return jnp.concatenate(pieces, axis=0).astype(jnp.bfloat16)


def joined_three(product):
    rows = product.shape[0] // 3
    return (product[:rows] + product[rows : 2 * rows]) + product[2 * rows :]


def coefficients(raw_params):
    travel = 1.0 + 47.0 * jax.nn.sigmoid(raw_params[0])
    weighting = 0.05 + 0.4 * jax.nn.sigmoid(raw_params[1])
    storage = travel * (1.0 - weighting)
    divisor = storage + 0.5
    return (
        (0.5 - travel * weighting) / divisor,
        (0.5 + travel * weighting) / divisor,
        (storage - 0.5) / divisor,
        1.0 / divisor,
    )


def affine_join(earlier, latter):
    return (earlier[0] * latter[0], latter[0] * earlier[1] + latter[1])


def stack_affine(pair):
    return jnp.stack([pair[0], pair[1]], axis=0)


def split_affine(stacked):
    return (stacked[0], stacked[1])


def stacked_affine(earlier, latter):
    return stack_affine(affine_join(split_affine(earlier), split_affine(latter)))


def linear_pairs(steps_up, steps_side, core):
    levels, basins, groups = (
        lax.axis_size("level"),
        lax.axis_size("basin"),
        lax.axis_size("group"),
    )
    pairs = []
    for level in range(levels):
        for basin in range(basins):
            target_level, target_basin = level + steps_up, basin + steps_side
            if 0 <= target_level < levels and 0 <= target_basin < basins:
                pairs.append(
                    (
                        (level * basins + basin) * groups + core,
                        (target_level * basins + target_basin) * groups + core,
                    )
                )
    return pairs


def both_ways(value, side_steps):
    pairs = linear_pairs(1, side_steps, 0) + linear_pairs(-1, -side_steps, 1)
    return lax.ppermute(value, ("level", "basin", "group"), pairs)


def body(lateral, cotangent, attributes, region, feeders, feeder_count, live_blocks, net_weight):
    steps_dev, reach_dev = lateral.shape
    outlets = reach_dev // 8
    regions, attr_count, param_count = net_weight.shape
    levels = lax.axis_size("level")
    up_count = feeders.shape[0]
    mine = lax.axis_index("group")
    slot_ids = lax.broadcasted_iota(jnp.int32, (reach_dev,), 0)
    live_mask = (slot_ids < live_blocks[0] * BLOCK).astype(jnp.float32)
    member_table = (
        region[None, :] == lax.broadcasted_iota(jnp.int32, (regions, reach_dev), 0)
    ).astype(jnp.float32)
    per_region = jnp.dot(
        jnp.transpose(net_weight, (0, 2, 1)).reshape(regions * param_count, attr_count),
        attributes,
        precision=lax.Precision.HIGHEST,
        preferred_element_type=jnp.float32,
    )
    raw_params = jnp.einsum(
        "rpi,ri->pi",
        per_region.reshape(regions, param_count, reach_dev),
        member_table,
        precision=lax.Precision.HIGHEST,
    )
    coef_set, coef_pull = jax.vjp(coefficients, raw_params)
    gain_now, gain_prev, retain, gain_side = coef_set
    zero_row = jnp.zeros((reach_dev,), jnp.float32)
    coef = jnp.stack(
        [gain_now, gain_prev, gain_side, retain, live_mask, zero_row, zero_row, zero_row], axis=0
    )
    lateral_all = whole_window(lateral)
    cotangent_all = whole_window(cotangent)
    steps_all = lateral_all.shape[0]
    source_ids = lax.broadcasted_iota(jnp.int32, (reach_dev + outlets, reach_dev), 0)
    confluence = jnp.zeros((reach_dev + outlets, reach_dev), jnp.float32)
    for upslot in range(up_count):
        confluence = confluence + (
            (source_ids == feeders[upslot][None, :]) & (upslot < feeder_count)[None, :]
        ).astype(jnp.float32)
    confluence = confluence.astype(jnp.bfloat16)
    zero_flow = jnp.zeros((steps_all, reach_dev), jnp.float32)

    def spread_of(pieces):
        spread = joined_three(
            lax.dot_general(
                pieces.astype(jnp.bfloat16),
                confluence,
                (((1,), (1,)), ((), ())),
                preferred_element_type=jnp.float32,
            )
        )
        return spread[:, :reach_dev], spread[:, reach_dev:]

    def forward_first(operands):
        flow, outlet, unused = routed(coef, lateral_all)
        return flow, outlet, jnp.stack([flow, zero_flow], axis=0)

    def backward_first(operands):
        adjoint, pieces = adjoined(coef, cotangent_all)
        own, side = spread_of(pieces)
        return own, side, jnp.stack([adjoint, zero_flow], axis=0)

    def forward_step(operands):
        upper, side = operands
        source = jnp.concatenate([upper, side], axis=1)
        product = jnp.dot(split_three(source), confluence, preferred_element_type=jnp.float32)
        flow, outlet, inflow = routed(coef, lateral_all, product)
        return flow, outlet, jnp.stack([flow, inflow], axis=0)

    def backward_step(operands):
        upper, side = operands
        adjoint, pieces = adjoined(coef, cotangent_all, upper, side)
        own, side = spread_of(pieces)
        return own, side, jnp.stack([adjoint, zero_flow], axis=0)

    def backward_last(operands):
        upper, side = operands
        adjoint, unused = adjoined(coef, cotangent_all, upper, side, emit=False)
        return zero_flow, side, jnp.stack([adjoint, zero_flow], axis=0)

    message, outlet_message, kept = lax.cond(mine == 0, forward_first, backward_first, None)
    for level_step in range(1, levels):
        upper = both_ways(message, 0)
        side = both_ways(outlet_message, 1)
        later = backward_step if level_step + 1 < levels else backward_last
        message, outlet_message, kept = lax.cond(
            mine == 0, forward_step, later, (upper, side)
        )
    other = lax.ppermute(kept, "group", [(0, 1), (1, 0)])
    forward_kept = jnp.where(mine == 0, kept, other)
    backward_kept = jnp.where(mine == 0, other, kept)
    outflow, inflow = forward_kept[0], forward_kept[1]
    adjoint = backward_kept[0]
    zero_first = jnp.zeros((1, reach_dev), jnp.float32)
    flow_before = jnp.concatenate([zero_first, outflow[:-1]], axis=0)
    inflow_before = jnp.concatenate([zero_first, inflow[:-1]], axis=0)
    coef_grads = (
        jnp.sum(adjoint * inflow, axis=0),
        jnp.sum(adjoint * inflow_before, axis=0),
        jnp.sum(adjoint * flow_before, axis=0),
        jnp.sum(adjoint * lateral_all, axis=0),
    )
    raw_grad = coef_pull(coef_grads)[0]
    owned_rows = regions // lax.axis_size("basin")
    weighted = (member_table[:, None, :] * raw_grad[None, :, :]).reshape(
        regions * param_count, reach_dev
    )
    summed = jnp.dot(
        weighted, attributes.T, precision=lax.Precision.HIGHEST, preferred_element_type=jnp.float32
    )
    local_grad = jnp.transpose(summed.reshape(regions, param_count, attr_count), (0, 2, 1))
    basins = lax.axis_size("basin")
    share_size = owned_rows * attr_count * param_count
    replicated = jnp.broadcast_to(
        local_grad.reshape(1, basins, share_size), (levels, basins, share_size)
    ).reshape(levels * basins, share_size)
    grad_net = jnp.sum(
        lax.all_to_all(replicated, ("level", "basin"), 0, 0, tiled=True), axis=0
    ).reshape(owned_rows, attr_count, param_count)
    own_hours = lax.dynamic_slice_in_dim(outflow, mine * steps_dev, steps_dev, axis=0)
    return (own_hours, grad_net)


def solution(mesh):
    in_specs = (
        P("group", ("level", "basin")),
        P("group", ("level", "basin")),
        P(None, ("level", "basin")),
        P(("level", "basin")),
        P(None, ("level", "basin")),
        P(("level", "basin")),
        P(("level", "basin")),
        P(),
    )
    out_specs = (P("group", ("level", "basin")), P("basin", None, None))
    return jax.shard_map(body, mesh=mesh, in_specs=in_specs, out_specs=out_specs, check_vma=False)
```

```python
import functools

import jax
import jax.numpy as jnp
from jax import lax
from jax.sharding import PartitionSpec as P
from jax.experimental import pallas as pl
from jax.experimental.pallas import tpu as pltpu

BLOCK = 128
PIECES = 2


def shifted(value, axis, steps):
    count = lax.axis_size(axis)
    leading, last = (max(0, -steps), min(count, count - steps))
    return lax.ppermute(value, axis, [(source, source + steps) for source in range(leading, last)])


def diagonal(value, steps):
    levels, basins = lax.axis_size("level"), lax.axis_size("basin")
    pairs = []
    for level in range(max(0, -steps), min(levels, levels - steps)):
        for basin in range(max(0, -steps), min(basins, basins - steps)):
            pairs.append((level * basins + basin, (level + steps) * basins + basin + steps))
    return lax.ppermute(value, ("level", "basin"), pairs)


def exchanged(value, axis, mask):
    count = lax.axis_size(axis)
    return lax.ppermute(value, axis, [(source, source ^ mask) for source in range(count)])


def scattered_sum(blocks, axis):
    count, mine = (lax.axis_size(axis), lax.axis_index(axis))
    width = count
    while width > 1:
        width //= 2
        lower, upper = blocks[:width], blocks[width:]
        high = (mine & width) > 0
        kept = jnp.where(high, upper, lower)
        sent = jnp.where(high, lower, upper)
        blocks = kept + exchanged(sent, axis, width)
    return blocks[0]


def butterfly_sum(value, axis):
    mask = 1
    while mask < lax.axis_size(axis):
        value = value + exchanged(value, axis, mask)
        mask *= 2
    return value


def whole_window(value):
    return lax.all_gather(value, "group", axis=0, tiled=True)


def carried_in(value, axis, join, neutral, backward):
    count, mine = (lax.axis_size(axis), lax.axis_index(axis))
    pieces = lax.all_gather(value, axis)
    if backward:
        pieces = pieces[::-1]
        mine = count - 1 - mine
    subtotal = jnp.full_like(value, 0) + jnp.asarray(neutral, value.dtype)

    def turn(position, subtotal):
        longer = join(subtotal, pieces[position])
        return jnp.where(position < mine, longer, subtotal)

    return lax.fori_loop(0, count - 1, turn, subtotal)


def recurrence_kernel(retain_ref, drive_ref, out_ref, *, reverse):
    steps = drive_ref.shape[0]
    keep = retain_ref[...]

    def advance(position, state):
        hour = steps - 1 - position if reverse else position
        state = keep * state + drive_ref[pl.ds(hour, 1), :]
        out_ref[pl.ds(hour, 1), :] = state
        return state

    lax.fori_loop(0, steps, advance, jnp.zeros_like(keep), unroll=8)


def recurrence(retain_row, drive, reverse=False):
    steps, width = drive.shape
    return pl.pallas_call(
        functools.partial(recurrence_kernel, reverse=reverse),
        out_shape=jax.ShapeDtypeStruct((steps, width), jnp.float32),
        in_specs=[pl.BlockSpec(memory_space=pltpu.VMEM), pl.BlockSpec(memory_space=pltpu.VMEM)],
        out_specs=pl.BlockSpec(memory_space=pltpu.VMEM),
        cost_estimate=pl.CostEstimate(
            flops=2 * steps * width, transcendentals=0, bytes_accessed=8 * steps * width + 4 * width
        ),
    )(retain_row, drive)


def forward_kernel(*refs, has_inflow):
    if has_inflow:
        coef_ref, product_ref, lateral_ref, out_ref, outlet_ref, inflow_ref = refs
    else:
        coef_ref, lateral_ref, out_ref, outlet_ref = refs
    steps = lateral_ref.shape[0]
    narrow = outlet_ref.shape[1]
    gain_now, gain_prev, gain_side = coef_ref[0:1, :], coef_ref[1:2, :], coef_ref[2:3, :]
    keep, live = coef_ref[3:4, :], coef_ref[4:5, :]

    def advance(hour, carry):
        state, before = carry
        side_in = lateral_ref[pl.ds(hour, 1), :]
        if has_inflow:
            now = product_ref[pl.ds(hour, 1), :]
            for piece_at in range(1, PIECES):
                now = now + product_ref[pl.ds(hour + piece_at * steps, 1), :]
            inflow_ref[pl.ds(hour, 1), :] = now
            drive = (gain_now * now + gain_prev * before) + gain_side * side_in
        else:
            now = before
            drive = gain_side * side_in
        state = keep * state + drive
        flow = state * live
        out_ref[pl.ds(hour, 1), :] = flow
        outlet_ref[pl.ds(hour, 1), :] = flow[:, :narrow]
        return state, now

    zero = jnp.zeros_like(keep)
    lax.fori_loop(0, steps, advance, (zero, zero), unroll=8)


def backward_kernel(*refs, has_down, emit):
    refs = list(refs)
    coef_ref, cot_ref = refs[0], refs[1]
    rest = refs[2:]
    if has_down:
        down_ref, side_ref = rest[0], rest[1]
        rest = rest[2:]
    adj_ref = rest[0]
    piece_ref = rest[1] if emit else None
    steps = cot_ref.shape[0]
    gain_now, gain_prev = coef_ref[0:1, :], coef_ref[1:2, :]
    keep, live = coef_ref[3:4, :], coef_ref[4:5, :]

    def advance(position, carry):
        hour = steps - 1 - position
        state, later = carry
        load = cot_ref[pl.ds(hour, 1), :]
        if has_down:
            down = down_ref[pl.ds(hour, 1), :]
            side = side_ref[pl.ds(hour, 1), :]
            narrow = side.shape[1]
            down = jnp.concatenate([down[:, :narrow] + side, down[:, narrow:]], axis=1)
            load = load + down
        state = keep * state + live * load
        adj_ref[pl.ds(hour, 1), :] = state
        if emit:
            remainder = gain_now * state + gain_prev * later
            for piece_at in range(PIECES):
                piece = remainder.astype(jnp.bfloat16).astype(jnp.float32)
                piece_ref[pl.ds(hour + piece_at * steps, 1), :] = piece
                remainder = remainder - piece
        return state, state

    zero = jnp.zeros_like(keep)
    lax.fori_loop(0, steps, advance, (zero, zero), unroll=8)


def vmem_call(kernel, outs, *args):
    steps, width = outs[0]
    return pl.pallas_call(
        kernel,
        out_shape=[jax.ShapeDtypeStruct(shape, jnp.float32) for shape in outs],
        in_specs=[pl.BlockSpec(memory_space=pltpu.VMEM)] * len(args),
        out_specs=[pl.BlockSpec(memory_space=pltpu.VMEM)] * len(outs),
        cost_estimate=pl.CostEstimate(
            flops=10 * steps * width,
            transcendentals=0,
            bytes_accessed=4 * (sum(a.size for a in args) + sum(r * c for r, c in outs)),
        ),
    )(*args)


def routed(coef, lateral_all, product=None):
    steps, width = lateral_all.shape
    narrow = width // 8
    if product is None:
        kernel = functools.partial(forward_kernel, has_inflow=False)
        flow, outlet = vmem_call(kernel, [(steps, width), (steps, narrow)], coef, lateral_all)
        return flow, outlet, None
    kernel = functools.partial(forward_kernel, has_inflow=True)
    return vmem_call(
        kernel, [(steps, width), (steps, narrow), (steps, width)], coef, product, lateral_all
    )


def adjoined(coef, cotangent_all, down=None, side=None, emit=True):
    steps, width = cotangent_all.shape
    kernel = functools.partial(backward_kernel, has_down=down is not None, emit=emit)
    args = (coef, cotangent_all) if down is None else (coef, cotangent_all, down, side)
    outs = [(steps, width)] + ([(PIECES * steps, width)] if emit else [])
    results = vmem_call(kernel, outs, *args)
    return results[0], (results[1] if emit else None)


def split_three(value):
    pieces = []
    rest = value
    for _ in range(PIECES):
        piece = lax.reduce_precision(rest, exponent_bits=8, mantissa_bits=7)
        pieces.append(piece)
        rest = rest - piece
    return jnp.concatenate(pieces, axis=0).astype(jnp.bfloat16)


def joined_three(product):
    rows = product.shape[0] // PIECES
    total = product[:rows]
    for piece_at in range(1, PIECES):
        total = total + product[piece_at * rows : (piece_at + 1) * rows]
    return total


def coefficients(raw_params):
    travel = 1.0 + 47.0 * jax.nn.sigmoid(raw_params[0])
    weighting = 0.05 + 0.4 * jax.nn.sigmoid(raw_params[1])
    storage = travel * (1.0 - weighting)
    divisor = storage + 0.5
    return (
        (0.5 - travel * weighting) / divisor,
        (0.5 + travel * weighting) / divisor,
        (storage - 0.5) / divisor,
        1.0 / divisor,
    )


def affine_join(earlier, latter):
    return (earlier[0] * latter[0], latter[0] * earlier[1] + latter[1])


def stack_affine(pair):
    return jnp.stack([pair[0], pair[1]], axis=0)


def split_affine(stacked):
    return (stacked[0], stacked[1])


def stacked_affine(earlier, latter):
    return stack_affine(affine_join(split_affine(earlier), split_affine(latter)))


def linear_pairs(steps_up, steps_side, core):
    levels, basins, groups = (
        lax.axis_size("level"),
        lax.axis_size("basin"),
        lax.axis_size("group"),
    )
    pairs = []
    for level in range(levels):
        for basin in range(basins):
            target_level, target_basin = level + steps_up, basin + steps_side
            if 0 <= target_level < levels and 0 <= target_basin < basins:
                pairs.append(
                    (
                        (level * basins + basin) * groups + core,
                        (target_level * basins + target_basin) * groups + core,
                    )
                )
    return pairs


def both_ways(value, side_steps):
    pairs = linear_pairs(1, side_steps, 0) + linear_pairs(-1, -side_steps, 1)
    return lax.ppermute(value, ("level", "basin", "group"), pairs)


def body(lateral, cotangent, attributes, region, feeders, feeder_count, live_blocks, net_weight):
    steps_dev, reach_dev = lateral.shape
    outlets = reach_dev // 8
    regions, attr_count, param_count = net_weight.shape
    levels = lax.axis_size("level")
    up_count = feeders.shape[0]
    mine = lax.axis_index("group")
    slot_ids = lax.broadcasted_iota(jnp.int32, (reach_dev,), 0)
    live_mask = (slot_ids < live_blocks[0] * BLOCK).astype(jnp.float32)
    member_table = (
        region[None, :] == lax.broadcasted_iota(jnp.int32, (regions, reach_dev), 0)
    ).astype(jnp.float32)
    per_region = jnp.dot(
        jnp.transpose(net_weight, (0, 2, 1)).reshape(regions * param_count, attr_count),
        attributes,
        precision=lax.Precision.HIGHEST,
        preferred_element_type=jnp.float32,
    )
    raw_params = jnp.einsum(
        "rpi,ri->pi",
        per_region.reshape(regions, param_count, reach_dev),
        member_table,
        precision=lax.Precision.HIGHEST,
    )
    coef_set, coef_pull = jax.vjp(coefficients, raw_params)
    gain_now, gain_prev, retain, gain_side = coef_set
    zero_row = jnp.zeros((reach_dev,), jnp.float32)
    coef = jnp.stack(
        [gain_now, gain_prev, gain_side, retain, live_mask, zero_row, zero_row, zero_row], axis=0
    )
    arrived = lax.ppermute(jnp.where(mine == 0, cotangent, lateral), "group", [(0, 1), (1, 0)])
    window = jnp.where(
        mine == 0,
        jnp.concatenate([lateral, arrived], axis=0),
        jnp.concatenate([arrived, cotangent], axis=0),
    )
    lateral_all = window
    cotangent_all = window
    steps_all = window.shape[0]
    source_ids = lax.broadcasted_iota(jnp.int32, (reach_dev + outlets, reach_dev), 0)
    confluence = jnp.zeros((reach_dev + outlets, reach_dev), jnp.float32)
    for upslot in range(up_count):
        confluence = confluence + (
            (source_ids == feeders[upslot][None, :]) & (upslot < feeder_count)[None, :]
        ).astype(jnp.float32)
    confluence = confluence.astype(jnp.bfloat16)
    zero_flow = jnp.zeros((steps_all, reach_dev), jnp.float32)

    def spread_of(pieces):
        spread = joined_three(
            lax.dot_general(
                pieces.astype(jnp.bfloat16),
                confluence,
                (((1,), (1,)), ((), ())),
                preferred_element_type=jnp.float32,
            )
        )
        return spread[:, :reach_dev], spread[:, reach_dev:]

    def forward_first(operands):
        flow, outlet, unused = routed(coef, lateral_all)
        return flow, outlet, flow, zero_flow, lateral_all

    def backward_first(operands):
        adjoint, pieces = adjoined(coef, cotangent_all)
        own, side = spread_of(pieces)
        return own, side, adjoint, zero_flow, zero_flow

    def forward_step(operands):
        upper, side = operands
        source = jnp.concatenate([upper, side], axis=1)
        product = jnp.dot(split_three(source), confluence, preferred_element_type=jnp.float32)
        flow, outlet, inflow = routed(coef, lateral_all, product)
        return flow, outlet, flow, inflow, lateral_all

    def backward_step(operands):
        upper, side = operands
        adjoint, pieces = adjoined(coef, cotangent_all, upper, side)
        own, side = spread_of(pieces)
        return own, side, adjoint, zero_flow, zero_flow

    def backward_last(operands):
        upper, side = operands
        adjoint, unused = adjoined(coef, cotangent_all, upper, side, emit=False)
        return zero_flow, side, adjoint, zero_flow, zero_flow

    message, outlet_message, *kept = lax.cond(mine == 0, forward_first, backward_first, None)
    for level_step in range(1, levels):
        upper = both_ways(message, 0)
        side = both_ways(outlet_message, 1)
        later = backward_step if level_step + 1 < levels else backward_last
        message, outlet_message, *kept = lax.cond(
            mine == 0, forward_step, later, (upper, side)
        )
    kept = jnp.stack(kept, axis=0)
    other = lax.ppermute(kept, "group", [(0, 1), (1, 0)])
    forward_kept = jnp.where(mine == 0, kept, other)
    backward_kept = jnp.where(mine == 0, other, kept)
    outflow, inflow, lateral_all = forward_kept[0], forward_kept[1], forward_kept[2]
    adjoint = backward_kept[0]
    zero_first = jnp.zeros((1, reach_dev), jnp.float32)
    flow_before = jnp.concatenate([zero_first, outflow[:-1]], axis=0)
    inflow_before = jnp.concatenate([zero_first, inflow[:-1]], axis=0)
    coef_grads = (
        jnp.sum(adjoint * inflow, axis=0),
        jnp.sum(adjoint * inflow_before, axis=0),
        jnp.sum(adjoint * flow_before, axis=0),
        jnp.sum(adjoint * lateral_all, axis=0),
    )
    raw_grad = coef_pull(coef_grads)[0]
    owned_rows = regions // lax.axis_size("basin")
    weighted = (member_table[:, None, :] * raw_grad[None, :, :]).reshape(
        regions * param_count, reach_dev
    )
    summed = jnp.dot(
        weighted, attributes.T, precision=lax.Precision.HIGHEST, preferred_element_type=jnp.float32
    )
    local_grad = jnp.transpose(summed.reshape(regions, param_count, attr_count), (0, 2, 1))
    basins = lax.axis_size("basin")
    share_size = owned_rows * attr_count * param_count
    replicated = jnp.broadcast_to(
        local_grad.reshape(1, basins, share_size), (levels, basins, share_size)
    ).reshape(levels * basins, share_size)
    grad_net = jnp.sum(
        lax.all_to_all(replicated, ("level", "basin"), 0, 0, tiled=True), axis=0
    ).reshape(owned_rows, attr_count, param_count)
    own_hours = lax.dynamic_slice_in_dim(outflow, mine * steps_dev, steps_dev, axis=0)
    return (own_hours, grad_net)


def solution(mesh):
    in_specs = (
        P("group", ("level", "basin")),
        P("group", ("level", "basin")),
        P(None, ("level", "basin")),
        P(("level", "basin")),
        P(None, ("level", "basin")),
        P(("level", "basin")),
        P(("level", "basin")),
        P(),
    )
    out_specs = (P("group", ("level", "basin")), P("basin", None, None))
    return jax.shard_map(body, mesh=mesh, in_specs=in_specs, out_specs=out_specs, check_vma=False)
```

```python
import functools

import jax
import jax.numpy as jnp
from jax import lax
from jax.sharding import PartitionSpec as P
from jax.experimental import pallas as pl
from jax.experimental.pallas import tpu as pltpu

BLOCK = 128
PIECES = 2


def shifted(value, axis, steps):
    count = lax.axis_size(axis)
    leading, last = (max(0, -steps), min(count, count - steps))
    return lax.ppermute(value, axis, [(source, source + steps) for source in range(leading, last)])


def diagonal(value, steps):
    levels, basins = lax.axis_size("level"), lax.axis_size("basin")
    pairs = []
    for level in range(max(0, -steps), min(levels, levels - steps)):
        for basin in range(max(0, -steps), min(basins, basins - steps)):
            pairs.append((level * basins + basin, (level + steps) * basins + basin + steps))
    return lax.ppermute(value, ("level", "basin"), pairs)


def exchanged(value, axis, mask):
    count = lax.axis_size(axis)
    return lax.ppermute(value, axis, [(source, source ^ mask) for source in range(count)])


def scattered_sum(blocks, axis):
    count, mine = (lax.axis_size(axis), lax.axis_index(axis))
    width = count
    while width > 1:
        width //= 2
        lower, upper = blocks[:width], blocks[width:]
        high = (mine & width) > 0
        kept = jnp.where(high, upper, lower)
        sent = jnp.where(high, lower, upper)
        blocks = kept + exchanged(sent, axis, width)
    return blocks[0]


def butterfly_sum(value, axis):
    mask = 1
    while mask < lax.axis_size(axis):
        value = value + exchanged(value, axis, mask)
        mask *= 2
    return value


def whole_window(value):
    return lax.all_gather(value, "group", axis=0, tiled=True)


def carried_in(value, axis, join, neutral, backward):
    count, mine = (lax.axis_size(axis), lax.axis_index(axis))
    pieces = lax.all_gather(value, axis)
    if backward:
        pieces = pieces[::-1]
        mine = count - 1 - mine
    subtotal = jnp.full_like(value, 0) + jnp.asarray(neutral, value.dtype)

    def turn(position, subtotal):
        longer = join(subtotal, pieces[position])
        return jnp.where(position < mine, longer, subtotal)

    return lax.fori_loop(0, count - 1, turn, subtotal)


def recurrence_kernel(retain_ref, drive_ref, out_ref, *, reverse):
    steps = drive_ref.shape[0]
    keep = retain_ref[...]

    def advance(position, state):
        hour = steps - 1 - position if reverse else position
        state = keep * state + drive_ref[pl.ds(hour, 1), :]
        out_ref[pl.ds(hour, 1), :] = state
        return state

    lax.fori_loop(0, steps, advance, jnp.zeros_like(keep), unroll=8)


def recurrence(retain_row, drive, reverse=False):
    steps, width = drive.shape
    return pl.pallas_call(
        functools.partial(recurrence_kernel, reverse=reverse),
        out_shape=jax.ShapeDtypeStruct((steps, width), jnp.float32),
        in_specs=[pl.BlockSpec(memory_space=pltpu.VMEM), pl.BlockSpec(memory_space=pltpu.VMEM)],
        out_specs=pl.BlockSpec(memory_space=pltpu.VMEM),
        cost_estimate=pl.CostEstimate(
            flops=2 * steps * width, transcendentals=0, bytes_accessed=8 * steps * width + 4 * width
        ),
    )(retain_row, drive)


def forward_kernel(*refs, has_inflow):
    if has_inflow:
        coef_ref, product_ref, early_ref, late_ref, out_ref, outlet_ref, inflow_ref = refs
    else:
        coef_ref, early_ref, late_ref, out_ref, outlet_ref = refs
    half = early_ref.shape[0]
    steps = 2 * half
    narrow = outlet_ref.shape[1]
    gain_now, gain_prev, gain_side = coef_ref[0:1, :], coef_ref[1:2, :], coef_ref[2:3, :]
    keep, live = coef_ref[3:4, :], coef_ref[4:5, :]

    def advance(hour, carry, side_ref, side_at):
        state, before = carry
        side_in = side_ref[pl.ds(side_at, 1), :]
        if has_inflow:
            now = product_ref[pl.ds(hour, 1), :]
            for piece_at in range(1, PIECES):
                now = now + product_ref[pl.ds(hour + piece_at * steps, 1), :]
            inflow_ref[pl.ds(hour, 1), :] = now
            drive = (gain_now * now + gain_prev * before) + gain_side * side_in
        else:
            now = before
            drive = gain_side * side_in
        state = keep * state + drive
        flow = state * live
        out_ref[pl.ds(hour, 1), :] = flow
        outlet_ref[pl.ds(hour, 1), :] = flow[:, :narrow]
        return state, now

    zero = jnp.zeros_like(keep)
    carry = lax.fori_loop(
        0, half, lambda hour, carry: advance(hour, carry, early_ref, hour), (zero, zero), unroll=8
    )
    lax.fori_loop(
        0,
        half,
        lambda position, carry: advance(position + half, carry, late_ref, position),
        carry,
        unroll=8,
    )


def backward_kernel(*refs, has_down, emit):
    refs = list(refs)
    coef_ref, early_ref, late_ref = refs[0], refs[1], refs[2]
    rest = refs[3:]
    if has_down:
        down_ref, side_ref = rest[0], rest[1]
        rest = rest[2:]
    adj_ref = rest[0]
    piece_ref = rest[1] if emit else None
    half = early_ref.shape[0]
    steps = 2 * half
    gain_now, gain_prev = coef_ref[0:1, :], coef_ref[1:2, :]
    keep, live = coef_ref[3:4, :], coef_ref[4:5, :]

    def advance(hour, carry, cot_ref, cot_at):
        state, later = carry
        load = cot_ref[pl.ds(cot_at, 1), :]
        if has_down:
            down = down_ref[pl.ds(hour, 1), :]
            side = side_ref[pl.ds(hour, 1), :]
            narrow = side.shape[1]
            down = jnp.concatenate([down[:, :narrow] + side, down[:, narrow:]], axis=1)
            load = load + down
        state = keep * state + live * load
        adj_ref[pl.ds(hour, 1), :] = state
        if emit:
            remainder = gain_now * state + gain_prev * later
            for piece_at in range(PIECES):
                piece = remainder.astype(jnp.bfloat16).astype(jnp.float32)
                piece_ref[pl.ds(hour + piece_at * steps, 1), :] = piece
                remainder = remainder - piece
        return state, state

    zero = jnp.zeros_like(keep)
    carry = lax.fori_loop(
        0,
        half,
        lambda position, carry: advance(steps - 1 - position, carry, late_ref, half - 1 - position),
        (zero, zero),
        unroll=8,
    )
    lax.fori_loop(
        0,
        half,
        lambda position, carry: advance(half - 1 - position, carry, early_ref, half - 1 - position),
        carry,
        unroll=8,
    )


def vmem_call(kernel, outs, *args):
    steps, width = outs[0]
    return pl.pallas_call(
        kernel,
        out_shape=[jax.ShapeDtypeStruct(shape, jnp.float32) for shape in outs],
        in_specs=[pl.BlockSpec(memory_space=pltpu.VMEM)] * len(args),
        out_specs=[pl.BlockSpec(memory_space=pltpu.VMEM)] * len(outs),
        cost_estimate=pl.CostEstimate(
            flops=10 * steps * width,
            transcendentals=0,
            bytes_accessed=4 * (sum(a.size for a in args) + sum(r * c for r, c in outs)),
        ),
    )(*args)


def routed(coef, early, late, product=None):
    half, width = early.shape
    steps = 2 * half
    narrow = width // 8
    if product is None:
        kernel = functools.partial(forward_kernel, has_inflow=False)
        flow, outlet = vmem_call(kernel, [(steps, width), (steps, narrow)], coef, early, late)
        return flow, outlet, None
    kernel = functools.partial(forward_kernel, has_inflow=True)
    return vmem_call(
        kernel, [(steps, width), (steps, narrow), (steps, width)], coef, product, early, late
    )


def adjoined(coef, early, late, down=None, side=None, emit=True):
    half, width = early.shape
    steps = 2 * half
    kernel = functools.partial(backward_kernel, has_down=down is not None, emit=emit)
    args = (coef, early, late) if down is None else (coef, early, late, down, side)
    outs = [(steps, width)] + ([(PIECES * steps, width)] if emit else [])
    results = vmem_call(kernel, outs, *args)
    return results[0], (results[1] if emit else None)


def split_three(value):
    pieces = []
    rest = value
    for _ in range(PIECES):
        piece = lax.reduce_precision(rest, exponent_bits=8, mantissa_bits=7)
        pieces.append(piece)
        rest = rest - piece
    return jnp.concatenate(pieces, axis=0).astype(jnp.bfloat16)


def joined_three(product):
    rows = product.shape[0] // PIECES
    total = product[:rows]
    for piece_at in range(1, PIECES):
        total = total + product[piece_at * rows : (piece_at + 1) * rows]
    return total


def coefficients(raw_params):
    travel = 1.0 + 47.0 * jax.nn.sigmoid(raw_params[0])
    weighting = 0.05 + 0.4 * jax.nn.sigmoid(raw_params[1])
    storage = travel * (1.0 - weighting)
    divisor = storage + 0.5
    return (
        (0.5 - travel * weighting) / divisor,
        (0.5 + travel * weighting) / divisor,
        (storage - 0.5) / divisor,
        1.0 / divisor,
    )


def affine_join(earlier, latter):
    return (earlier[0] * latter[0], latter[0] * earlier[1] + latter[1])


def stack_affine(pair):
    return jnp.stack([pair[0], pair[1]], axis=0)


def split_affine(stacked):
    return (stacked[0], stacked[1])


def stacked_affine(earlier, latter):
    return stack_affine(affine_join(split_affine(earlier), split_affine(latter)))


def linear_pairs(steps_up, steps_side, core):
    levels, basins, groups = (
        lax.axis_size("level"),
        lax.axis_size("basin"),
        lax.axis_size("group"),
    )
    pairs = []
    for level in range(levels):
        for basin in range(basins):
            target_level, target_basin = level + steps_up, basin + steps_side
            if 0 <= target_level < levels and 0 <= target_basin < basins:
                pairs.append(
                    (
                        (level * basins + basin) * groups + core,
                        (target_level * basins + target_basin) * groups + core,
                    )
                )
    return pairs


def both_ways(value, side_steps):
    pairs = linear_pairs(1, side_steps, 0) + linear_pairs(-1, -side_steps, 1)
    return lax.ppermute(value, ("level", "basin", "group"), pairs)


def body(lateral, cotangent, attributes, region, feeders, feeder_count, live_blocks, net_weight):
    steps_dev, reach_dev = lateral.shape
    outlets = reach_dev // 8
    regions, attr_count, param_count = net_weight.shape
    levels = lax.axis_size("level")
    up_count = feeders.shape[0]
    mine = lax.axis_index("group")
    slot_ids = lax.broadcasted_iota(jnp.int32, (reach_dev,), 0)
    live_mask = (slot_ids < live_blocks[0] * BLOCK).astype(jnp.float32)
    member_table = (
        region[None, :] == lax.broadcasted_iota(jnp.int32, (regions, reach_dev), 0)
    ).astype(jnp.float32)
    per_region = jnp.dot(
        jnp.transpose(net_weight, (0, 2, 1)).reshape(regions * param_count, attr_count),
        attributes,
        precision=lax.Precision.HIGHEST,
        preferred_element_type=jnp.float32,
    )
    raw_params = jnp.einsum(
        "rpi,ri->pi",
        per_region.reshape(regions, param_count, reach_dev),
        member_table,
        precision=lax.Precision.HIGHEST,
    )
    coef_set, coef_pull = jax.vjp(coefficients, raw_params)
    gain_now, gain_prev, retain, gain_side = coef_set
    zero_row = jnp.zeros((reach_dev,), jnp.float32)
    coef = jnp.stack(
        [gain_now, gain_prev, gain_side, retain, live_mask, zero_row, zero_row, zero_row], axis=0
    )
    late_lateral = lax.ppermute(lateral, "group", [(1, 0)])
    early_cotangent = lax.ppermute(cotangent, "group", [(0, 1)])
    steps_all = 2 * steps_dev
    source_ids = lax.broadcasted_iota(jnp.int32, (reach_dev + outlets, reach_dev), 0)
    confluence = jnp.zeros((reach_dev + outlets, reach_dev), jnp.float32)
    for upslot in range(up_count):
        confluence = confluence + (
            (source_ids == feeders[upslot][None, :]) & (upslot < feeder_count)[None, :]
        ).astype(jnp.float32)
    confluence = confluence.astype(jnp.bfloat16)
    zero_flow = jnp.zeros((steps_all, reach_dev), jnp.float32)

    def spread_of(pieces):
        spread = joined_three(
            lax.dot_general(
                pieces.astype(jnp.bfloat16),
                confluence,
                (((1,), (1,)), ((), ())),
                preferred_element_type=jnp.float32,
            )
        )
        return spread[:, :reach_dev], spread[:, reach_dev:]

    def forward_first(operands):
        flow, outlet, unused = routed(coef, lateral, late_lateral)
        return flow, outlet, flow, zero_flow, zero_flow

    def backward_first(operands):
        adjoint, pieces = adjoined(coef, early_cotangent, cotangent)
        own, side = spread_of(pieces)
        return own, side, adjoint, zero_flow, zero_flow

    def forward_step(operands):
        upper, side = operands
        source = jnp.concatenate([upper, side], axis=1)
        product = jnp.dot(split_three(source), confluence, preferred_element_type=jnp.float32)
        flow, outlet, inflow = routed(coef, lateral, late_lateral, product)
        lateral_all = jnp.concatenate([lateral, late_lateral], axis=0)
        return flow, outlet, flow, inflow, lateral_all

    def backward_step(operands):
        upper, side = operands
        adjoint, pieces = adjoined(coef, early_cotangent, cotangent, upper, side)
        own, side = spread_of(pieces)
        return own, side, adjoint, zero_flow, zero_flow

    def backward_last(operands):
        upper, side = operands
        adjoint, unused = adjoined(coef, early_cotangent, cotangent, upper, side, emit=False)
        return zero_flow, side, adjoint, zero_flow, zero_flow

    message, outlet_message, *kept = lax.cond(mine == 0, forward_first, backward_first, None)
    for level_step in range(1, levels):
        side = both_ways(outlet_message, 1)
        upper = both_ways(message, 0)
        later = backward_step if level_step + 1 < levels else backward_last
        message, outlet_message, *kept = lax.cond(
            mine == 0, forward_step, later, (upper, side)
        )
    kept = jnp.stack(kept, axis=0)
    other = lax.ppermute(kept, "group", [(0, 1), (1, 0)])
    forward_kept = jnp.where(mine == 0, kept, other)
    backward_kept = jnp.where(mine == 0, other, kept)
    outflow, inflow, lateral_all = forward_kept[0], forward_kept[1], forward_kept[2]
    adjoint = backward_kept[0]
    zero_first = jnp.zeros((1, reach_dev), jnp.float32)
    flow_before = jnp.concatenate([zero_first, outflow[:-1]], axis=0)
    inflow_before = jnp.concatenate([zero_first, inflow[:-1]], axis=0)
    coef_grads = (
        jnp.sum(adjoint * inflow, axis=0),
        jnp.sum(adjoint * inflow_before, axis=0),
        jnp.sum(adjoint * flow_before, axis=0),
        jnp.sum(adjoint * lateral_all, axis=0),
    )
    raw_grad = coef_pull(coef_grads)[0]
    owned_rows = regions // lax.axis_size("basin")
    weighted = (member_table[:, None, :] * raw_grad[None, :, :]).reshape(
        regions * param_count, reach_dev
    )
    summed = jnp.dot(
        weighted, attributes.T, precision=lax.Precision.HIGHEST, preferred_element_type=jnp.float32
    )
    local_grad = jnp.transpose(summed.reshape(regions, param_count, attr_count), (0, 2, 1))
    basins = lax.axis_size("basin")
    share_size = owned_rows * attr_count * param_count
    replicated = jnp.broadcast_to(
        local_grad.reshape(1, basins, share_size), (levels, basins, share_size)
    ).reshape(levels * basins, share_size)
    grad_net = jnp.sum(
        lax.all_to_all(replicated, ("level", "basin"), 0, 0, tiled=True), axis=0
    ).reshape(owned_rows, attr_count, param_count)
    own_hours = lax.dynamic_slice_in_dim(outflow, mine * steps_dev, steps_dev, axis=0)
    return (own_hours, grad_net)


def solution(mesh):
    in_specs = (
        P("group", ("level", "basin")),
        P("group", ("level", "basin")),
        P(None, ("level", "basin")),
        P(("level", "basin")),
        P(None, ("level", "basin")),
        P(("level", "basin")),
        P(("level", "basin")),
        P(),
    )
    out_specs = (P("group", ("level", "basin")), P("basin", None, None))
    return jax.shard_map(body, mesh=mesh, in_specs=in_specs, out_specs=out_specs, check_vma=False)
```

```python
import functools

import jax
import jax.numpy as jnp
from jax import lax
from jax.sharding import PartitionSpec as P
from jax.experimental import pallas as pl
from jax.experimental.pallas import tpu as pltpu

BLOCK = 128
PIECES = 2


def shifted(value, axis, steps):
    count = lax.axis_size(axis)
    leading, last = (max(0, -steps), min(count, count - steps))
    return lax.ppermute(value, axis, [(source, source + steps) for source in range(leading, last)])


def diagonal(value, steps):
    levels, basins = lax.axis_size("level"), lax.axis_size("basin")
    pairs = []
    for level in range(max(0, -steps), min(levels, levels - steps)):
        for basin in range(max(0, -steps), min(basins, basins - steps)):
            pairs.append((level * basins + basin, (level + steps) * basins + basin + steps))
    return lax.ppermute(value, ("level", "basin"), pairs)


def exchanged(value, axis, mask):
    count = lax.axis_size(axis)
    return lax.ppermute(value, axis, [(source, source ^ mask) for source in range(count)])


def scattered_sum(blocks, axis):
    count, mine = (lax.axis_size(axis), lax.axis_index(axis))
    width = count
    while width > 1:
        width //= 2
        lower, upper = blocks[:width], blocks[width:]
        high = (mine & width) > 0
        kept = jnp.where(high, upper, lower)
        sent = jnp.where(high, lower, upper)
        blocks = kept + exchanged(sent, axis, width)
    return blocks[0]


def butterfly_sum(value, axis):
    mask = 1
    while mask < lax.axis_size(axis):
        value = value + exchanged(value, axis, mask)
        mask *= 2
    return value


def whole_window(value):
    return lax.all_gather(value, "group", axis=0, tiled=True)


def carried_in(value, axis, join, neutral, backward):
    count, mine = (lax.axis_size(axis), lax.axis_index(axis))
    pieces = lax.all_gather(value, axis)
    if backward:
        pieces = pieces[::-1]
        mine = count - 1 - mine
    subtotal = jnp.full_like(value, 0) + jnp.asarray(neutral, value.dtype)

    def turn(position, subtotal):
        longer = join(subtotal, pieces[position])
        return jnp.where(position < mine, longer, subtotal)

    return lax.fori_loop(0, count - 1, turn, subtotal)


def recurrence_kernel(retain_ref, drive_ref, out_ref, *, reverse):
    steps = drive_ref.shape[0]
    keep = retain_ref[...]

    def advance(position, state):
        hour = steps - 1 - position if reverse else position
        state = keep * state + drive_ref[pl.ds(hour, 1), :]
        out_ref[pl.ds(hour, 1), :] = state
        return state

    lax.fori_loop(0, steps, advance, jnp.zeros_like(keep), unroll=8)


def recurrence(retain_row, drive, reverse=False):
    steps, width = drive.shape
    return pl.pallas_call(
        functools.partial(recurrence_kernel, reverse=reverse),
        out_shape=jax.ShapeDtypeStruct((steps, width), jnp.float32),
        in_specs=[pl.BlockSpec(memory_space=pltpu.VMEM), pl.BlockSpec(memory_space=pltpu.VMEM)],
        out_specs=pl.BlockSpec(memory_space=pltpu.VMEM),
        cost_estimate=pl.CostEstimate(
            flops=2 * steps * width, transcendentals=0, bytes_accessed=8 * steps * width + 4 * width
        ),
    )(retain_row, drive)


def split_pair(value):
    high = value.astype(jnp.bfloat16)
    low = (value - high.astype(jnp.float32)).astype(jnp.bfloat16)
    return jnp.concatenate([high, low], axis=0)


def forward_kernel(*refs, has_inflow):
    if has_inflow:
        coef_ref, upper_ref, side_ref, conf_ref, lateral_ref, out_ref, outlet_ref, inflow_ref = refs
    else:
        coef_ref, lateral_ref, out_ref, outlet_ref = refs
    steps = lateral_ref.shape[0]
    narrow = outlet_ref.shape[1]
    gain_now, gain_prev, gain_side = coef_ref[0:1, :], coef_ref[1:2, :], coef_ref[2:3, :]
    keep, live = coef_ref[3:4, :], coef_ref[4:5, :]
    if has_inflow:
        source = jnp.concatenate([upper_ref[...], side_ref[...]], axis=1)
        product = jnp.dot(split_pair(source), conf_ref[...], preferred_element_type=jnp.float32)
        inflow_ref[...] = product[:steps] + product[steps:]

    def advance(hour, carry):
        state, before = carry
        side_in = lateral_ref[pl.ds(hour, 1), :]
        if has_inflow:
            now = inflow_ref[pl.ds(hour, 1), :]
            drive = (gain_now * now + gain_prev * before) + gain_side * side_in
        else:
            now = before
            drive = gain_side * side_in
        state = keep * state + drive
        flow = state * live
        out_ref[pl.ds(hour, 1), :] = flow
        outlet_ref[pl.ds(hour, 1), :] = flow[:, :narrow]
        return state, now

    zero = jnp.zeros_like(keep)
    lax.fori_loop(0, steps, advance, (zero, zero), unroll=8)


def backward_kernel(*refs, has_down, emit):
    refs = list(refs)
    coef_ref, cot_ref = refs[0], refs[1]
    rest = refs[2:]
    if has_down:
        down_ref, side_ref = rest[0], rest[1]
        rest = rest[2:]
    if emit:
        conf_ref, adj_ref, own_ref, spill_ref, work_ref = rest
    else:
        (adj_ref,) = rest
    steps = cot_ref.shape[0]
    gain_now, gain_prev = coef_ref[0:1, :], coef_ref[1:2, :]
    keep, live = coef_ref[3:4, :], coef_ref[4:5, :]

    def advance(position, carry):
        hour = steps - 1 - position
        state, later = carry
        load = cot_ref[pl.ds(hour, 1), :]
        if has_down:
            down = down_ref[pl.ds(hour, 1), :]
            side = side_ref[pl.ds(hour, 1), :]
            narrow = side.shape[1]
            down = jnp.concatenate([down[:, :narrow] + side, down[:, narrow:]], axis=1)
            load = load + down
        state = keep * state + live * load
        adj_ref[pl.ds(hour, 1), :] = state
        if emit:
            work_ref[pl.ds(hour, 1), :] = gain_now * state + gain_prev * later
        return state, state

    zero = jnp.zeros_like(keep)
    lax.fori_loop(0, steps, advance, (zero, zero), unroll=8)
    if emit:
        spread = jnp.dot(split_pair(work_ref[...]), conf_ref[...], preferred_element_type=jnp.float32)
        width = own_ref.shape[1]
        own_ref[...] = spread[:steps, :width] + spread[steps:, :width]
        spill_ref[...] = spread[:steps, width:] + spread[steps:, width:]


def vmem_call(kernel, outs, *args, scratch=()):
    steps, width = outs[0]
    return pl.pallas_call(
        kernel,
        out_shape=[jax.ShapeDtypeStruct(shape, jnp.float32) for shape in outs],
        in_specs=[pl.BlockSpec(memory_space=pltpu.VMEM)] * len(args),
        out_specs=[pl.BlockSpec(memory_space=pltpu.VMEM)] * len(outs),
        scratch_shapes=[pltpu.VMEM(shape, jnp.float32) for shape in scratch],
        cost_estimate=pl.CostEstimate(
            flops=10 * steps * width + 4 * steps * width * (width + width // 8),
            transcendentals=0,
            bytes_accessed=sum(a.size * a.dtype.itemsize for a in args) + 4 * sum(r * c for r, c in outs),
        ),
    )(*args)


def routed(coef, lateral_all, upper=None, side=None, confluence=None):
    steps, width = lateral_all.shape
    narrow = width // 8
    if upper is None:
        kernel = functools.partial(forward_kernel, has_inflow=False)
        flow, outlet = vmem_call(kernel, [(steps, width), (steps, narrow)], coef, lateral_all)
        return flow, outlet, None
    kernel = functools.partial(forward_kernel, has_inflow=True)
    return vmem_call(
        kernel,
        [(steps, width), (steps, narrow), (steps, width)],
        coef, upper, side, confluence, lateral_all,
    )


def adjoined(coef, cotangent_all, down=None, side=None, confluence_t=None):
    steps, width = cotangent_all.shape
    emit = confluence_t is not None
    kernel = functools.partial(backward_kernel, has_down=down is not None, emit=emit)
    args = (coef, cotangent_all) if down is None else (coef, cotangent_all, down, side)
    if not emit:
        return vmem_call(kernel, [(steps, width)], *args)[0], None, None
    adjoint, own, spill = vmem_call(
        kernel,
        [(steps, width), (steps, width), (steps, width // 8)],
        *args,
        confluence_t,
        scratch=[(steps, width)],
    )
    return adjoint, own, spill


def split_three(value):
    pieces = []
    rest = value
    for _ in range(PIECES):
        piece = lax.reduce_precision(rest, exponent_bits=8, mantissa_bits=7)
        pieces.append(piece)
        rest = rest - piece
    return jnp.concatenate(pieces, axis=0).astype(jnp.bfloat16)


def joined_three(product):
    rows = product.shape[0] // PIECES
    total = product[:rows]
    for piece_at in range(1, PIECES):
        total = total + product[piece_at * rows : (piece_at + 1) * rows]
    return total


def coefficients(raw_params):
    travel = 1.0 + 47.0 * jax.nn.sigmoid(raw_params[0])
    weighting = 0.05 + 0.4 * jax.nn.sigmoid(raw_params[1])
    storage = travel * (1.0 - weighting)
    divisor = storage + 0.5
    return (
        (0.5 - travel * weighting) / divisor,
        (0.5 + travel * weighting) / divisor,
        (storage - 0.5) / divisor,
        1.0 / divisor,
    )


def affine_join(earlier, latter):
    return (earlier[0] * latter[0], latter[0] * earlier[1] + latter[1])


def stack_affine(pair):
    return jnp.stack([pair[0], pair[1]], axis=0)


def split_affine(stacked):
    return (stacked[0], stacked[1])


def stacked_affine(earlier, latter):
    return stack_affine(affine_join(split_affine(earlier), split_affine(latter)))


def linear_pairs(steps_up, steps_side, core):
    levels, basins, groups = (
        lax.axis_size("level"),
        lax.axis_size("basin"),
        lax.axis_size("group"),
    )
    pairs = []
    for level in range(levels):
        for basin in range(basins):
            target_level, target_basin = level + steps_up, basin + steps_side
            if 0 <= target_level < levels and 0 <= target_basin < basins:
                pairs.append(
                    (
                        (level * basins + basin) * groups + core,
                        (target_level * basins + target_basin) * groups + core,
                    )
                )
    return pairs


def both_ways(value, side_steps):
    pairs = linear_pairs(1, side_steps, 0) + linear_pairs(-1, -side_steps, 1)
    return lax.ppermute(value, ("level", "basin", "group"), pairs)


def body(lateral, cotangent, attributes, region, feeders, feeder_count, live_blocks, net_weight):
    steps_dev, reach_dev = lateral.shape
    outlets = reach_dev // 8
    regions, attr_count, param_count = net_weight.shape
    levels = lax.axis_size("level")
    up_count = feeders.shape[0]
    mine = lax.axis_index("group")
    slot_ids = lax.broadcasted_iota(jnp.int32, (reach_dev,), 0)
    live_mask = (slot_ids < live_blocks[0] * BLOCK).astype(jnp.float32)
    member_table = (
        region[None, :] == lax.broadcasted_iota(jnp.int32, (regions, reach_dev), 0)
    ).astype(jnp.float32)
    per_region = jnp.dot(
        jnp.transpose(net_weight, (0, 2, 1)).reshape(regions * param_count, attr_count),
        attributes,
        precision=lax.Precision.HIGHEST,
        preferred_element_type=jnp.float32,
    )
    raw_params = jnp.einsum(
        "rpi,ri->pi",
        per_region.reshape(regions, param_count, reach_dev),
        member_table,
        precision=lax.Precision.HIGHEST,
    )
    coef_set, coef_pull = jax.vjp(coefficients, raw_params)
    gain_now, gain_prev, retain, gain_side = coef_set
    zero_row = jnp.zeros((reach_dev,), jnp.float32)
    coef = jnp.stack(
        [gain_now, gain_prev, gain_side, retain, live_mask, zero_row, zero_row, zero_row], axis=0
    )
    arrived = lax.ppermute(jnp.where(mine == 0, cotangent, lateral), "group", [(0, 1), (1, 0)])
    window = jnp.where(
        mine == 0,
        jnp.concatenate([lateral, arrived], axis=0),
        jnp.concatenate([arrived, cotangent], axis=0),
    )
    lateral_all = window
    cotangent_all = window
    steps_all = window.shape[0]
    source_ids = lax.broadcasted_iota(jnp.int32, (reach_dev + outlets, reach_dev), 0)
    confluence = jnp.zeros((reach_dev + outlets, reach_dev), jnp.float32)
    for upslot in range(up_count):
        confluence = confluence + (
            (source_ids == feeders[upslot][None, :]) & (upslot < feeder_count)[None, :]
        ).astype(jnp.float32)
    confluence = confluence.astype(jnp.bfloat16)
    target_ids = lax.broadcasted_iota(jnp.int32, (reach_dev, reach_dev + outlets), 1)
    confluence_t = jnp.zeros((reach_dev, reach_dev + outlets), jnp.float32)
    for upslot in range(up_count):
        confluence_t = confluence_t + (
            (target_ids == feeders[upslot][:, None]) & (upslot < feeder_count)[:, None]
        ).astype(jnp.float32)
    confluence_t = confluence_t.astype(jnp.bfloat16)
    zero_flow = jnp.zeros((steps_all, reach_dev), jnp.float32)

    def forward_first(operands):
        flow, outlet, unused = routed(coef, lateral_all)
        return flow, outlet, flow, zero_flow, lateral_all

    def backward_first(operands):
        adjoint, own, side = adjoined(coef, cotangent_all, confluence_t=confluence_t)
        return own, side, adjoint, zero_flow, zero_flow

    def forward_step(operands):
        upper, side = operands
        flow, outlet, inflow = routed(coef, lateral_all, upper, side, confluence)
        return flow, outlet, flow, inflow, lateral_all

    def backward_step(operands):
        upper, side = operands
        adjoint, own, side = adjoined(coef, cotangent_all, upper, side, confluence_t)
        return own, side, adjoint, zero_flow, zero_flow

    def backward_last(operands):
        upper, side = operands
        adjoint, unused, unused_side = adjoined(coef, cotangent_all, upper, side)
        return zero_flow, side, adjoint, zero_flow, zero_flow

    message, outlet_message, *kept = lax.cond(mine == 0, forward_first, backward_first, None)
    for level_step in range(1, levels):
        upper = both_ways(message, 0)
        side = both_ways(outlet_message, 1)
        later = backward_step if level_step + 1 < levels else backward_last
        message, outlet_message, *kept = lax.cond(
            mine == 0, forward_step, later, (upper, side)
        )
    kept = jnp.stack(kept, axis=0)
    other = lax.ppermute(kept, "group", [(0, 1), (1, 0)])
    forward_kept = jnp.where(mine == 0, kept, other)
    backward_kept = jnp.where(mine == 0, other, kept)
    outflow, inflow, lateral_all = forward_kept[0], forward_kept[1], forward_kept[2]
    adjoint = backward_kept[0]
    zero_first = jnp.zeros((1, reach_dev), jnp.float32)
    flow_before = jnp.concatenate([zero_first, outflow[:-1]], axis=0)
    inflow_before = jnp.concatenate([zero_first, inflow[:-1]], axis=0)
    coef_grads = (
        jnp.sum(adjoint * inflow, axis=0),
        jnp.sum(adjoint * inflow_before, axis=0),
        jnp.sum(adjoint * flow_before, axis=0),
        jnp.sum(adjoint * lateral_all, axis=0),
    )
    raw_grad = coef_pull(coef_grads)[0]
    owned_rows = regions // lax.axis_size("basin")
    weighted = (member_table[:, None, :] * raw_grad[None, :, :]).reshape(
        regions * param_count, reach_dev
    )
    summed = jnp.dot(
        weighted, attributes.T, precision=lax.Precision.HIGHEST, preferred_element_type=jnp.float32
    )
    local_grad = jnp.transpose(summed.reshape(regions, param_count, attr_count), (0, 2, 1))
    basins = lax.axis_size("basin")
    share_size = owned_rows * attr_count * param_count
    replicated = jnp.broadcast_to(
        local_grad.reshape(1, basins, share_size), (levels, basins, share_size)
    ).reshape(levels * basins, share_size)
    grad_net = jnp.sum(
        lax.all_to_all(replicated, ("level", "basin"), 0, 0, tiled=True), axis=0
    ).reshape(owned_rows, attr_count, param_count)
    own_hours = lax.dynamic_slice_in_dim(outflow, mine * steps_dev, steps_dev, axis=0)
    return (own_hours, grad_net)


def solution(mesh):
    in_specs = (
        P("group", ("level", "basin")),
        P("group", ("level", "basin")),
        P(None, ("level", "basin")),
        P(("level", "basin")),
        P(None, ("level", "basin")),
        P(("level", "basin")),
        P(("level", "basin")),
        P(),
    )
    out_specs = (P("group", ("level", "basin")), P("basin", None, None))
    return jax.shard_map(body, mesh=mesh, in_specs=in_specs, out_specs=out_specs, check_vma=False)
```

```python
import functools

import jax
import jax.numpy as jnp
from jax import lax
from jax.sharding import PartitionSpec as P
from jax.experimental import pallas as pl
from jax.experimental.pallas import tpu as pltpu

BLOCK = 128
PIECES = 2


def shifted(value, axis, steps):
    count = lax.axis_size(axis)
    leading, last = (max(0, -steps), min(count, count - steps))
    return lax.ppermute(value, axis, [(source, source + steps) for source in range(leading, last)])


def diagonal(value, steps):
    levels, basins = lax.axis_size("level"), lax.axis_size("basin")
    pairs = []
    for level in range(max(0, -steps), min(levels, levels - steps)):
        for basin in range(max(0, -steps), min(basins, basins - steps)):
            pairs.append((level * basins + basin, (level + steps) * basins + basin + steps))
    return lax.ppermute(value, ("level", "basin"), pairs)


def exchanged(value, axis, mask):
    count = lax.axis_size(axis)
    return lax.ppermute(value, axis, [(source, source ^ mask) for source in range(count)])


def scattered_sum(blocks, axis):
    count, mine = (lax.axis_size(axis), lax.axis_index(axis))
    width = count
    while width > 1:
        width //= 2
        lower, upper = blocks[:width], blocks[width:]
        high = (mine & width) > 0
        kept = jnp.where(high, upper, lower)
        sent = jnp.where(high, lower, upper)
        blocks = kept + exchanged(sent, axis, width)
    return blocks[0]


def butterfly_sum(value, axis):
    mask = 1
    while mask < lax.axis_size(axis):
        value = value + exchanged(value, axis, mask)
        mask *= 2
    return value


def whole_window(value):
    return lax.all_gather(value, "group", axis=0, tiled=True)


def carried_in(value, axis, join, neutral, backward):
    count, mine = (lax.axis_size(axis), lax.axis_index(axis))
    pieces = lax.all_gather(value, axis)
    if backward:
        pieces = pieces[::-1]
        mine = count - 1 - mine
    subtotal = jnp.full_like(value, 0) + jnp.asarray(neutral, value.dtype)

    def turn(position, subtotal):
        longer = join(subtotal, pieces[position])
        return jnp.where(position < mine, longer, subtotal)

    return lax.fori_loop(0, count - 1, turn, subtotal)


def recurrence_kernel(retain_ref, drive_ref, out_ref, *, reverse):
    steps = drive_ref.shape[0]
    keep = retain_ref[...]

    def advance(position, state):
        hour = steps - 1 - position if reverse else position
        state = keep * state + drive_ref[pl.ds(hour, 1), :]
        out_ref[pl.ds(hour, 1), :] = state
        return state

    lax.fori_loop(0, steps, advance, jnp.zeros_like(keep), unroll=8)


def recurrence(retain_row, drive, reverse=False):
    steps, width = drive.shape
    return pl.pallas_call(
        functools.partial(recurrence_kernel, reverse=reverse),
        out_shape=jax.ShapeDtypeStruct((steps, width), jnp.float32),
        in_specs=[pl.BlockSpec(memory_space=pltpu.VMEM), pl.BlockSpec(memory_space=pltpu.VMEM)],
        out_specs=pl.BlockSpec(memory_space=pltpu.VMEM),
        cost_estimate=pl.CostEstimate(
            flops=2 * steps * width, transcendentals=0, bytes_accessed=8 * steps * width + 4 * width
        ),
    )(retain_row, drive)


def split_pair(value):
    high = value.astype(jnp.bfloat16)
    low = (value - high.astype(jnp.float32)).astype(jnp.bfloat16)
    return jnp.concatenate([high, low], axis=0)


def forward_kernel(*refs, has_inflow):
    if has_inflow:
        coef_ref, upper_ref, side_ref, conf_ref, lateral_ref, out_ref, outlet_ref, inflow_ref = refs
    else:
        coef_ref, lateral_ref, out_ref, outlet_ref = refs
    steps = lateral_ref.shape[0]
    narrow = outlet_ref.shape[1]
    gain_now, gain_prev, gain_side = coef_ref[0:1, :], coef_ref[1:2, :], coef_ref[2:3, :]
    keep, live = coef_ref[3:4, :], coef_ref[4:5, :]
    if has_inflow:
        source = jnp.concatenate([upper_ref[...], side_ref[...]], axis=1)
        product = jnp.dot(split_pair(source), conf_ref[...], preferred_element_type=jnp.float32)
        inflow_ref[...] = product[:steps] + product[steps:]

    def advance(hour, carry):
        state, before = carry
        side_in = lateral_ref[pl.ds(hour, 1), :]
        if has_inflow:
            now = inflow_ref[pl.ds(hour, 1), :]
            drive = (gain_now * now + gain_prev * before) + gain_side * side_in
        else:
            now = before
            drive = gain_side * side_in
        state = keep * state + drive
        flow = state * live
        out_ref[pl.ds(hour, 1), :] = flow
        outlet_ref[pl.ds(hour, 1), :] = flow[:, :narrow]
        return state, now

    zero = jnp.zeros_like(keep)
    lax.fori_loop(0, steps, advance, (zero, zero), unroll=8)


def backward_kernel(*refs, has_down, emit):
    refs = list(refs)
    coef_ref, cot_ref = refs[0], refs[1]
    rest = refs[2:]
    if has_down:
        down_ref, side_ref = rest[0], rest[1]
        rest = rest[2:]
    if emit:
        conf_ref, adj_ref, own_ref, spill_ref, work_ref = rest
    else:
        (adj_ref,) = rest
    steps = cot_ref.shape[0]
    gain_now, gain_prev = coef_ref[0:1, :], coef_ref[1:2, :]
    keep, live = coef_ref[3:4, :], coef_ref[4:5, :]

    def advance(position, carry):
        hour = steps - 1 - position
        state, later = carry
        load = cot_ref[pl.ds(hour, 1), :]
        if has_down:
            down = down_ref[pl.ds(hour, 1), :]
            side = side_ref[pl.ds(hour, 1), :]
            narrow = side.shape[1]
            down = jnp.concatenate([down[:, :narrow] + side, down[:, narrow:]], axis=1)
            load = load + down
        state = keep * state + live * load
        adj_ref[pl.ds(hour, 1), :] = state
        if emit:
            work_ref[pl.ds(hour, 1), :] = gain_now * state + gain_prev * later
        return state, state

    zero = jnp.zeros_like(keep)
    lax.fori_loop(0, steps, advance, (zero, zero), unroll=8)
    if emit:
        spread = jnp.dot(split_pair(work_ref[...]), conf_ref[...], preferred_element_type=jnp.float32)
        width = own_ref.shape[1]
        own_ref[...] = spread[:steps, :width] + spread[steps:, :width]
        spill_ref[...] = spread[:steps, width:] + spread[steps:, width:]


def vmem_call(kernel, outs, *args, scratch=()):
    steps, width = outs[0]
    return pl.pallas_call(
        kernel,
        out_shape=[jax.ShapeDtypeStruct(shape, jnp.float32) for shape in outs],
        in_specs=[pl.BlockSpec(memory_space=pltpu.VMEM)] * len(args),
        out_specs=[pl.BlockSpec(memory_space=pltpu.VMEM)] * len(outs),
        scratch_shapes=[pltpu.VMEM(shape, jnp.float32) for shape in scratch],
        cost_estimate=pl.CostEstimate(
            flops=10 * steps * width + 4 * steps * width * (width + width // 8),
            transcendentals=0,
            bytes_accessed=sum(a.size * a.dtype.itemsize for a in args) + 4 * sum(r * c for r, c in outs),
        ),
    )(*args)


def routed(coef, lateral_all, upper=None, side=None, confluence=None):
    steps, width = lateral_all.shape
    narrow = width // 8
    if upper is None:
        kernel = functools.partial(forward_kernel, has_inflow=False)
        flow, outlet = vmem_call(kernel, [(steps, width), (steps, narrow)], coef, lateral_all)
        return flow, outlet, None
    kernel = functools.partial(forward_kernel, has_inflow=True)
    return vmem_call(
        kernel,
        [(steps, width), (steps, narrow), (steps, width)],
        coef, upper, side, confluence, lateral_all,
    )


def adjoined(coef, cotangent_all, down=None, side=None, confluence_t=None):
    steps, width = cotangent_all.shape
    emit = confluence_t is not None
    kernel = functools.partial(backward_kernel, has_down=down is not None, emit=emit)
    args = (coef, cotangent_all) if down is None else (coef, cotangent_all, down, side)
    if not emit:
        return vmem_call(kernel, [(steps, width)], *args)[0], None, None
    adjoint, own, spill = vmem_call(
        kernel,
        [(steps, width), (steps, width), (steps, width // 8)],
        *args,
        confluence_t,
        scratch=[(steps, width)],
    )
    return adjoint, own, spill


def split_three(value):
    pieces = []
    rest = value
    for _ in range(PIECES):
        piece = lax.reduce_precision(rest, exponent_bits=8, mantissa_bits=7)
        pieces.append(piece)
        rest = rest - piece
    return jnp.concatenate(pieces, axis=0).astype(jnp.bfloat16)


def joined_three(product):
    rows = product.shape[0] // PIECES
    total = product[:rows]
    for piece_at in range(1, PIECES):
        total = total + product[piece_at * rows : (piece_at + 1) * rows]
    return total


def coefficients(raw_params):
    travel = 1.0 + 47.0 * jax.nn.sigmoid(raw_params[0])
    weighting = 0.05 + 0.4 * jax.nn.sigmoid(raw_params[1])
    storage = travel * (1.0 - weighting)
    divisor = storage + 0.5
    return (
        (0.5 - travel * weighting) / divisor,
        (0.5 + travel * weighting) / divisor,
        (storage - 0.5) / divisor,
        1.0 / divisor,
    )


def affine_join(earlier, latter):
    return (earlier[0] * latter[0], latter[0] * earlier[1] + latter[1])


def stack_affine(pair):
    return jnp.stack([pair[0], pair[1]], axis=0)


def split_affine(stacked):
    return (stacked[0], stacked[1])


def stacked_affine(earlier, latter):
    return stack_affine(affine_join(split_affine(earlier), split_affine(latter)))


def linear_pairs(steps_up, steps_side, core):
    levels, basins, groups = (
        lax.axis_size("level"),
        lax.axis_size("basin"),
        lax.axis_size("group"),
    )
    pairs = []
    for level in range(levels):
        for basin in range(basins):
            target_level, target_basin = level + steps_up, basin + steps_side
            if 0 <= target_level < levels and 0 <= target_basin < basins:
                pairs.append(
                    (
                        (level * basins + basin) * groups + core,
                        (target_level * basins + target_basin) * groups + core,
                    )
                )
    return pairs


def both_ways(value, side_steps):
    axes = ("level", "basin", "group")
    upward = lax.ppermute(value, axes, linear_pairs(1, side_steps, 0))
    downward = lax.ppermute(value, axes, linear_pairs(-1, -side_steps, 1))
    return jnp.where(lax.axis_index("group") == 0, upward, downward)


def body(lateral, cotangent, attributes, region, feeders, feeder_count, live_blocks, net_weight):
    steps_dev, reach_dev = lateral.shape
    outlets = reach_dev // 8
    regions, attr_count, param_count = net_weight.shape
    levels = lax.axis_size("level")
    up_count = feeders.shape[0]
    mine = lax.axis_index("group")
    slot_ids = lax.broadcasted_iota(jnp.int32, (reach_dev,), 0)
    live_mask = (slot_ids < live_blocks[0] * BLOCK).astype(jnp.float32)
    member_table = (
        region[None, :] == lax.broadcasted_iota(jnp.int32, (regions, reach_dev), 0)
    ).astype(jnp.float32)
    per_region = jnp.dot(
        jnp.transpose(net_weight, (0, 2, 1)).reshape(regions * param_count, attr_count),
        attributes,
        precision=lax.Precision.HIGHEST,
        preferred_element_type=jnp.float32,
    )
    raw_params = jnp.einsum(
        "rpi,ri->pi",
        per_region.reshape(regions, param_count, reach_dev),
        member_table,
        precision=lax.Precision.HIGHEST,
    )
    coef_set, coef_pull = jax.vjp(coefficients, raw_params)
    gain_now, gain_prev, retain, gain_side = coef_set
    zero_row = jnp.zeros((reach_dev,), jnp.float32)
    coef = jnp.stack(
        [gain_now, gain_prev, gain_side, retain, live_mask, zero_row, zero_row, zero_row], axis=0
    )
    arrived = lax.ppermute(jnp.where(mine == 0, cotangent, lateral), "group", [(0, 1), (1, 0)])
    window = jnp.where(
        mine == 0,
        jnp.concatenate([lateral, arrived], axis=0),
        jnp.concatenate([arrived, cotangent], axis=0),
    )
    lateral_all = window
    cotangent_all = window
    steps_all = window.shape[0]
    source_ids = lax.broadcasted_iota(jnp.int32, (reach_dev + outlets, reach_dev), 0)
    confluence = jnp.zeros((reach_dev + outlets, reach_dev), jnp.float32)
    for upslot in range(up_count):
        confluence = confluence + (
            (source_ids == feeders[upslot][None, :]) & (upslot < feeder_count)[None, :]
        ).astype(jnp.float32)
    confluence = confluence.astype(jnp.bfloat16)
    target_ids = lax.broadcasted_iota(jnp.int32, (reach_dev, reach_dev + outlets), 1)
    confluence_t = jnp.zeros((reach_dev, reach_dev + outlets), jnp.float32)
    for upslot in range(up_count):
        confluence_t = confluence_t + (
            (target_ids == feeders[upslot][:, None]) & (upslot < feeder_count)[:, None]
        ).astype(jnp.float32)
    confluence_t = confluence_t.astype(jnp.bfloat16)
    zero_flow = jnp.zeros((steps_all, reach_dev), jnp.float32)

    def forward_first(operands):
        flow, outlet, unused = routed(coef, lateral_all)
        return flow, outlet, flow, zero_flow, lateral_all

    def backward_first(operands):
        adjoint, own, side = adjoined(coef, cotangent_all, confluence_t=confluence_t)
        return own, side, adjoint, zero_flow, zero_flow

    def forward_step(operands):
        upper, side = operands
        flow, outlet, inflow = routed(coef, lateral_all, upper, side, confluence)
        return flow, outlet, flow, inflow, lateral_all

    def backward_step(operands):
        upper, side = operands
        adjoint, own, side = adjoined(coef, cotangent_all, upper, side, confluence_t)
        return own, side, adjoint, zero_flow, zero_flow

    def backward_last(operands):
        upper, side = operands
        adjoint, unused, unused_side = adjoined(coef, cotangent_all, upper, side)
        return zero_flow, side, adjoint, zero_flow, zero_flow

    message, outlet_message, *kept = lax.cond(mine == 0, forward_first, backward_first, None)
    for level_step in range(1, levels):
        upper = both_ways(message, 0)
        side = both_ways(outlet_message, 1)
        later = backward_step if level_step + 1 < levels else backward_last
        message, outlet_message, *kept = lax.cond(
            mine == 0, forward_step, later, (upper, side)
        )
    kept = jnp.stack(kept, axis=0)
    other = lax.ppermute(kept, "group", [(0, 1), (1, 0)])
    forward_kept = jnp.where(mine == 0, kept, other)
    backward_kept = jnp.where(mine == 0, other, kept)
    outflow, inflow, lateral_all = forward_kept[0], forward_kept[1], forward_kept[2]
    adjoint = backward_kept[0]
    zero_first = jnp.zeros((1, reach_dev), jnp.float32)
    flow_before = jnp.concatenate([zero_first, outflow[:-1]], axis=0)
    inflow_before = jnp.concatenate([zero_first, inflow[:-1]], axis=0)
    coef_grads = (
        jnp.sum(adjoint * inflow, axis=0),
        jnp.sum(adjoint * inflow_before, axis=0),
        jnp.sum(adjoint * flow_before, axis=0),
        jnp.sum(adjoint * lateral_all, axis=0),
    )
    raw_grad = coef_pull(coef_grads)[0]
    owned_rows = regions // lax.axis_size("basin")
    weighted = (member_table[:, None, :] * raw_grad[None, :, :]).reshape(
        regions * param_count, reach_dev
    )
    summed = jnp.dot(
        weighted, attributes.T, precision=lax.Precision.HIGHEST, preferred_element_type=jnp.float32
    )
    local_grad = jnp.transpose(summed.reshape(regions, param_count, attr_count), (0, 2, 1))
    basins = lax.axis_size("basin")
    share_size = owned_rows * attr_count * param_count
    replicated = jnp.broadcast_to(
        local_grad.reshape(1, basins, share_size), (levels, basins, share_size)
    ).reshape(levels * basins, share_size)
    grad_net = jnp.sum(
        lax.all_to_all(replicated, ("level", "basin"), 0, 0, tiled=True), axis=0
    ).reshape(owned_rows, attr_count, param_count)
    own_hours = lax.dynamic_slice_in_dim(outflow, mine * steps_dev, steps_dev, axis=0)
    return (own_hours, grad_net)


def solution(mesh):
    in_specs = (
        P("group", ("level", "basin")),
        P("group", ("level", "basin")),
        P(None, ("level", "basin")),
        P(("level", "basin")),
        P(None, ("level", "basin")),
        P(("level", "basin")),
        P(("level", "basin")),
        P(),
    )
    out_specs = (P("group", ("level", "basin")), P("basin", None, None))
    return jax.shard_map(body, mesh=mesh, in_specs=in_specs, out_specs=out_specs, check_vma=False)
```

```python
import functools

import jax
import jax.numpy as jnp
from jax import lax
from jax.sharding import PartitionSpec as P
from jax.experimental import pallas as pl
from jax.experimental.pallas import tpu as pltpu

BLOCK = 128
PIECES = 2


def shifted(value, axis, steps):
    count = lax.axis_size(axis)
    leading, last = (max(0, -steps), min(count, count - steps))
    return lax.ppermute(value, axis, [(source, source + steps) for source in range(leading, last)])


def diagonal(value, steps):
    levels, basins = lax.axis_size("level"), lax.axis_size("basin")
    pairs = []
    for level in range(max(0, -steps), min(levels, levels - steps)):
        for basin in range(max(0, -steps), min(basins, basins - steps)):
            pairs.append((level * basins + basin, (level + steps) * basins + basin + steps))
    return lax.ppermute(value, ("level", "basin"), pairs)


def exchanged(value, axis, mask):
    count = lax.axis_size(axis)
    return lax.ppermute(value, axis, [(source, source ^ mask) for source in range(count)])


def scattered_sum(blocks, axis):
    count, mine = (lax.axis_size(axis), lax.axis_index(axis))
    width = count
    while width > 1:
        width //= 2
        lower, upper = blocks[:width], blocks[width:]
        high = (mine & width) > 0
        kept = jnp.where(high, upper, lower)
        sent = jnp.where(high, lower, upper)
        blocks = kept + exchanged(sent, axis, width)
    return blocks[0]


def butterfly_sum(value, axis):
    mask = 1
    while mask < lax.axis_size(axis):
        value = value + exchanged(value, axis, mask)
        mask *= 2
    return value


def whole_window(value):
    return lax.all_gather(value, "group", axis=0, tiled=True)


def carried_in(value, axis, join, neutral, backward):
    count, mine = (lax.axis_size(axis), lax.axis_index(axis))
    pieces = lax.all_gather(value, axis)
    if backward:
        pieces = pieces[::-1]
        mine = count - 1 - mine
    subtotal = jnp.full_like(value, 0) + jnp.asarray(neutral, value.dtype)

    def turn(position, subtotal):
        longer = join(subtotal, pieces[position])
        return jnp.where(position < mine, longer, subtotal)

    return lax.fori_loop(0, count - 1, turn, subtotal)


def recurrence_kernel(retain_ref, drive_ref, out_ref, *, reverse):
    steps = drive_ref.shape[0]
    keep = retain_ref[...]

    def advance(position, state):
        hour = steps - 1 - position if reverse else position
        state = keep * state + drive_ref[pl.ds(hour, 1), :]
        out_ref[pl.ds(hour, 1), :] = state
        return state

    lax.fori_loop(0, steps, advance, jnp.zeros_like(keep), unroll=8)


def recurrence(retain_row, drive, reverse=False):
    steps, width = drive.shape
    return pl.pallas_call(
        functools.partial(recurrence_kernel, reverse=reverse),
        out_shape=jax.ShapeDtypeStruct((steps, width), jnp.float32),
        in_specs=[pl.BlockSpec(memory_space=pltpu.VMEM), pl.BlockSpec(memory_space=pltpu.VMEM)],
        out_specs=pl.BlockSpec(memory_space=pltpu.VMEM),
        cost_estimate=pl.CostEstimate(
            flops=2 * steps * width, transcendentals=0, bytes_accessed=8 * steps * width + 4 * width
        ),
    )(retain_row, drive)


def split_pair(value):
    high = value.astype(jnp.bfloat16)
    low = (value - high.astype(jnp.float32)).astype(jnp.bfloat16)
    return jnp.concatenate([high, low], axis=0)


def shifted_rows(value, shift, fill):
    rows = lax.broadcasted_iota(jnp.int32, value.shape, 0)
    return jnp.where(rows >= shift, pltpu.roll(value, shift, 0), fill)


def forward_kernel(*refs, has_inflow):
    if has_inflow:
        coef_ref, upper_ref, side_ref, conf_ref, lateral_ref, out_ref, outlet_ref, inflow_ref = refs
    else:
        coef_ref, lateral_ref, out_ref, outlet_ref = refs
    steps, width = lateral_ref.shape
    narrow = outlet_ref.shape[1]
    tile = 8
    gain_now, gain_prev, gain_side = coef_ref[0:1, :], coef_ref[1:2, :], coef_ref[2:3, :]
    keep, live = coef_ref[3:4, :], coef_ref[4:5, :]
    if has_inflow:
        source = jnp.concatenate([upper_ref[...], side_ref[...]], axis=1)
        product = jnp.dot(split_pair(source), conf_ref[...], preferred_element_type=jnp.float32)
        inflow_ref[...] = product[:steps] + product[steps:]
    keep_tile = jnp.broadcast_to(keep, (tile, width))
    powers = keep_tile
    span = 1
    while span < tile:
        powers = powers * shifted_rows(powers, span, 1.0)
        span *= 2
    keep_steps = []
    factor = keep
    for unused in range(3):
        keep_steps.append(factor)
        factor = factor * factor

    def advance(block, carry):
        state, before = carry
        rows = pl.ds(pl.multiple_of(block * tile, tile), tile)
        drive_side = gain_side * lateral_ref[rows, :]
        if has_inflow:
            now = inflow_ref[rows, :]
            earlier = jnp.where(
                lax.broadcasted_iota(jnp.int32, (tile, width), 0) >= 1,
                pltpu.roll(now, 1, 0),
                before,
            )
            drive = (gain_now * now + gain_prev * earlier) + drive_side
            before = now[tile - 1 : tile, :]
        else:
            drive = drive_side
        span = 1
        for factor in keep_steps:
            drive = drive + factor * shifted_rows(drive, span, 0.0)
            span *= 2
        block_state = drive + powers * state
        flow = block_state * live
        out_ref[rows, :] = flow
        outlet_ref[rows, :] = flow[:, :narrow]
        return block_state[tile - 1 : tile, :], before

    zero = jnp.zeros_like(keep)
    lax.fori_loop(0, steps // tile, advance, (zero, zero), unroll=2)


def backward_kernel(*refs, has_down, emit):
    refs = list(refs)
    coef_ref, cot_ref = refs[0], refs[1]
    rest = refs[2:]
    if has_down:
        down_ref, side_ref = rest[0], rest[1]
        rest = rest[2:]
    if emit:
        conf_ref, adj_ref, own_ref, spill_ref, work_ref = rest
    else:
        (adj_ref,) = rest
    steps = cot_ref.shape[0]
    gain_now, gain_prev = coef_ref[0:1, :], coef_ref[1:2, :]
    keep, live = coef_ref[3:4, :], coef_ref[4:5, :]

    def advance(position, carry):
        hour = steps - 1 - position
        state, later = carry
        load = cot_ref[pl.ds(hour, 1), :]
        if has_down:
            down = down_ref[pl.ds(hour, 1), :]
            side = side_ref[pl.ds(hour, 1), :]
            narrow = side.shape[1]
            down = jnp.concatenate([down[:, :narrow] + side, down[:, narrow:]], axis=1)
            load = load + down
        state = keep * state + live * load
        adj_ref[pl.ds(hour, 1), :] = state
        if emit:
            work_ref[pl.ds(hour, 1), :] = gain_now * state + gain_prev * later
        return state, state

    zero = jnp.zeros_like(keep)
    lax.fori_loop(0, steps, advance, (zero, zero), unroll=8)
    if emit:
        spread = jnp.dot(split_pair(work_ref[...]), conf_ref[...], preferred_element_type=jnp.float32)
        width = own_ref.shape[1]
        own_ref[...] = spread[:steps, :width] + spread[steps:, :width]
        spill_ref[...] = spread[:steps, width:] + spread[steps:, width:]


def vmem_call(kernel, outs, *args, scratch=()):
    steps, width = outs[0]
    return pl.pallas_call(
        kernel,
        out_shape=[jax.ShapeDtypeStruct(shape, jnp.float32) for shape in outs],
        in_specs=[pl.BlockSpec(memory_space=pltpu.VMEM)] * len(args),
        out_specs=[pl.BlockSpec(memory_space=pltpu.VMEM)] * len(outs),
        scratch_shapes=[pltpu.VMEM(shape, jnp.float32) for shape in scratch],
        cost_estimate=pl.CostEstimate(
            flops=10 * steps * width + 4 * steps * width * (width + width // 8),
            transcendentals=0,
            bytes_accessed=sum(a.size * a.dtype.itemsize for a in args) + 4 * sum(r * c for r, c in outs),
        ),
    )(*args)


def routed(coef, lateral_all, upper=None, side=None, confluence=None):
    steps, width = lateral_all.shape
    narrow = width // 8
    if upper is None:
        kernel = functools.partial(forward_kernel, has_inflow=False)
        flow, outlet = vmem_call(kernel, [(steps, width), (steps, narrow)], coef, lateral_all)
        return flow, outlet, None
    kernel = functools.partial(forward_kernel, has_inflow=True)
    return vmem_call(
        kernel,
        [(steps, width), (steps, narrow), (steps, width)],
        coef, upper, side, confluence, lateral_all,
    )


def adjoined(coef, cotangent_all, down=None, side=None, confluence_t=None):
    steps, width = cotangent_all.shape
    emit = confluence_t is not None
    kernel = functools.partial(backward_kernel, has_down=down is not None, emit=emit)
    args = (coef, cotangent_all) if down is None else (coef, cotangent_all, down, side)
    if not emit:
        return vmem_call(kernel, [(steps, width)], *args)[0], None, None
    adjoint, own, spill = vmem_call(
        kernel,
        [(steps, width), (steps, width), (steps, width // 8)],
        *args,
        confluence_t,
        scratch=[(steps, width)],
    )
    return adjoint, own, spill


def split_three(value):
    pieces = []
    rest = value
    for _ in range(PIECES):
        piece = lax.reduce_precision(rest, exponent_bits=8, mantissa_bits=7)
        pieces.append(piece)
        rest = rest - piece
    return jnp.concatenate(pieces, axis=0).astype(jnp.bfloat16)


def joined_three(product):
    rows = product.shape[0] // PIECES
    total = product[:rows]
    for piece_at in range(1, PIECES):
        total = total + product[piece_at * rows : (piece_at + 1) * rows]
    return total


def coefficients(raw_params):
    travel = 1.0 + 47.0 * jax.nn.sigmoid(raw_params[0])
    weighting = 0.05 + 0.4 * jax.nn.sigmoid(raw_params[1])
    storage = travel * (1.0 - weighting)
    divisor = storage + 0.5
    return (
        (0.5 - travel * weighting) / divisor,
        (0.5 + travel * weighting) / divisor,
        (storage - 0.5) / divisor,
        1.0 / divisor,
    )


def affine_join(earlier, latter):
    return (earlier[0] * latter[0], latter[0] * earlier[1] + latter[1])


def stack_affine(pair):
    return jnp.stack([pair[0], pair[1]], axis=0)


def split_affine(stacked):
    return (stacked[0], stacked[1])


def stacked_affine(earlier, latter):
    return stack_affine(affine_join(split_affine(earlier), split_affine(latter)))


def linear_pairs(steps_up, steps_side, core):
    levels, basins, groups = (
        lax.axis_size("level"),
        lax.axis_size("basin"),
        lax.axis_size("group"),
    )
    pairs = []
    for level in range(levels):
        for basin in range(basins):
            target_level, target_basin = level + steps_up, basin + steps_side
            if 0 <= target_level < levels and 0 <= target_basin < basins:
                pairs.append(
                    (
                        (level * basins + basin) * groups + core,
                        (target_level * basins + target_basin) * groups + core,
                    )
                )
    return pairs


def both_ways(value, side_steps):
    pairs = linear_pairs(1, side_steps, 0) + linear_pairs(-1, -side_steps, 1)
    return lax.ppermute(value, ("level", "basin", "group"), pairs)


def body(lateral, cotangent, attributes, region, feeders, feeder_count, live_blocks, net_weight):
    steps_dev, reach_dev = lateral.shape
    outlets = reach_dev // 8
    regions, attr_count, param_count = net_weight.shape
    levels = lax.axis_size("level")
    up_count = feeders.shape[0]
    mine = lax.axis_index("group")
    slot_ids = lax.broadcasted_iota(jnp.int32, (reach_dev,), 0)
    live_mask = (slot_ids < live_blocks[0] * BLOCK).astype(jnp.float32)
    member_table = (
        region[None, :] == lax.broadcasted_iota(jnp.int32, (regions, reach_dev), 0)
    ).astype(jnp.float32)
    per_region = jnp.dot(
        jnp.transpose(net_weight, (0, 2, 1)).reshape(regions * param_count, attr_count),
        attributes,
        precision=lax.Precision.HIGHEST,
        preferred_element_type=jnp.float32,
    )
    raw_params = jnp.einsum(
        "rpi,ri->pi",
        per_region.reshape(regions, param_count, reach_dev),
        member_table,
        precision=lax.Precision.HIGHEST,
    )
    coef_set, coef_pull = jax.vjp(coefficients, raw_params)
    gain_now, gain_prev, retain, gain_side = coef_set
    zero_row = jnp.zeros((reach_dev,), jnp.float32)
    coef = jnp.stack(
        [gain_now, gain_prev, gain_side, retain, live_mask, zero_row, zero_row, zero_row], axis=0
    )
    arrived = lax.ppermute(jnp.where(mine == 0, cotangent, lateral), "group", [(0, 1), (1, 0)])
    window = jnp.where(
        mine == 0,
        jnp.concatenate([lateral, arrived], axis=0),
        jnp.concatenate([arrived, cotangent], axis=0),
    )
    lateral_all = window
    cotangent_all = window
    steps_all = window.shape[0]
    source_ids = lax.broadcasted_iota(jnp.int32, (reach_dev + outlets, reach_dev), 0)
    confluence = jnp.zeros((reach_dev + outlets, reach_dev), jnp.float32)
    for upslot in range(up_count):
        confluence = confluence + (
            (source_ids == feeders[upslot][None, :]) & (upslot < feeder_count)[None, :]
        ).astype(jnp.float32)
    confluence = confluence.astype(jnp.bfloat16)
    target_ids = lax.broadcasted_iota(jnp.int32, (reach_dev, reach_dev + outlets), 1)
    confluence_t = jnp.zeros((reach_dev, reach_dev + outlets), jnp.float32)
    for upslot in range(up_count):
        confluence_t = confluence_t + (
            (target_ids == feeders[upslot][:, None]) & (upslot < feeder_count)[:, None]
        ).astype(jnp.float32)
    confluence_t = confluence_t.astype(jnp.bfloat16)
    zero_flow = jnp.zeros((steps_all, reach_dev), jnp.float32)

    def forward_first(operands):
        flow, outlet, unused = routed(coef, lateral_all)
        return flow, outlet, flow, zero_flow, lateral_all

    def backward_first(operands):
        adjoint, own, side = adjoined(coef, cotangent_all, confluence_t=confluence_t)
        return own, side, adjoint, zero_flow, zero_flow

    def forward_step(operands):
        upper, side = operands
        flow, outlet, inflow = routed(coef, lateral_all, upper, side, confluence)
        return flow, outlet, flow, inflow, lateral_all

    def backward_step(operands):
        upper, side = operands
        adjoint, own, side = adjoined(coef, cotangent_all, upper, side, confluence_t)
        return own, side, adjoint, zero_flow, zero_flow

    def backward_last(operands):
        upper, side = operands
        adjoint, unused, unused_side = adjoined(coef, cotangent_all, upper, side)
        return zero_flow, side, adjoint, zero_flow, zero_flow

    message, outlet_message, *kept = lax.cond(mine == 0, forward_first, backward_first, None)
    for level_step in range(1, levels):
        upper = both_ways(message, 0)
        side = both_ways(outlet_message, 1)
        later = backward_step if level_step + 1 < levels else backward_last
        message, outlet_message, *kept = lax.cond(
            mine == 0, forward_step, later, (upper, side)
        )
    kept = jnp.stack(kept, axis=0)
    other = lax.ppermute(kept, "group", [(0, 1), (1, 0)])
    forward_kept = jnp.where(mine == 0, kept, other)
    backward_kept = jnp.where(mine == 0, other, kept)
    outflow, inflow, lateral_all = forward_kept[0], forward_kept[1], forward_kept[2]
    adjoint = backward_kept[0]
    zero_first = jnp.zeros((1, reach_dev), jnp.float32)
    flow_before = jnp.concatenate([zero_first, outflow[:-1]], axis=0)
    inflow_before = jnp.concatenate([zero_first, inflow[:-1]], axis=0)
    coef_grads = (
        jnp.sum(adjoint * inflow, axis=0),
        jnp.sum(adjoint * inflow_before, axis=0),
        jnp.sum(adjoint * flow_before, axis=0),
        jnp.sum(adjoint * lateral_all, axis=0),
    )
    raw_grad = coef_pull(coef_grads)[0]
    owned_rows = regions // lax.axis_size("basin")
    weighted = (member_table[:, None, :] * raw_grad[None, :, :]).reshape(
        regions * param_count, reach_dev
    )
    summed = jnp.dot(
        weighted, attributes.T, precision=lax.Precision.HIGHEST, preferred_element_type=jnp.float32
    )
    local_grad = jnp.transpose(summed.reshape(regions, param_count, attr_count), (0, 2, 1))
    basins = lax.axis_size("basin")
    share_size = owned_rows * attr_count * param_count
    replicated = jnp.broadcast_to(
        local_grad.reshape(1, basins, share_size), (levels, basins, share_size)
    ).reshape(levels * basins, share_size)
    grad_net = jnp.sum(
        lax.all_to_all(replicated, ("level", "basin"), 0, 0, tiled=True), axis=0
    ).reshape(owned_rows, attr_count, param_count)
    own_hours = lax.dynamic_slice_in_dim(outflow, mine * steps_dev, steps_dev, axis=0)
    return (own_hours, grad_net)


def solution(mesh):
    in_specs = (
        P("group", ("level", "basin")),
        P("group", ("level", "basin")),
        P(None, ("level", "basin")),
        P(("level", "basin")),
        P(None, ("level", "basin")),
        P(("level", "basin")),
        P(("level", "basin")),
        P(),
    )
    out_specs = (P("group", ("level", "basin")), P("basin", None, None))
    return jax.shard_map(body, mesh=mesh, in_specs=in_specs, out_specs=out_specs, check_vma=False)
```

```python
import functools

import jax
import jax.numpy as jnp
from jax import lax
from jax.sharding import PartitionSpec as P
from jax.experimental import pallas as pl
from jax.experimental.pallas import tpu as pltpu

BLOCK = 128
PIECES = 2


def shifted(value, axis, steps):
    count = lax.axis_size(axis)
    leading, last = (max(0, -steps), min(count, count - steps))
    return lax.ppermute(value, axis, [(source, source + steps) for source in range(leading, last)])


def diagonal(value, steps):
    levels, basins = lax.axis_size("level"), lax.axis_size("basin")
    pairs = []
    for level in range(max(0, -steps), min(levels, levels - steps)):
        for basin in range(max(0, -steps), min(basins, basins - steps)):
            pairs.append((level * basins + basin, (level + steps) * basins + basin + steps))
    return lax.ppermute(value, ("level", "basin"), pairs)


def exchanged(value, axis, mask):
    count = lax.axis_size(axis)
    return lax.ppermute(value, axis, [(source, source ^ mask) for source in range(count)])


def scattered_sum(blocks, axis):
    count, mine = (lax.axis_size(axis), lax.axis_index(axis))
    width = count
    while width > 1:
        width //= 2
        lower, upper = blocks[:width], blocks[width:]
        high = (mine & width) > 0
        kept = jnp.where(high, upper, lower)
        sent = jnp.where(high, lower, upper)
        blocks = kept + exchanged(sent, axis, width)
    return blocks[0]


def butterfly_sum(value, axis):
    mask = 1
    while mask < lax.axis_size(axis):
        value = value + exchanged(value, axis, mask)
        mask *= 2
    return value


def whole_window(value):
    return lax.all_gather(value, "group", axis=0, tiled=True)


def carried_in(value, axis, join, neutral, backward):
    count, mine = (lax.axis_size(axis), lax.axis_index(axis))
    pieces = lax.all_gather(value, axis)
    if backward:
        pieces = pieces[::-1]
        mine = count - 1 - mine
    subtotal = jnp.full_like(value, 0) + jnp.asarray(neutral, value.dtype)

    def turn(position, subtotal):
        longer = join(subtotal, pieces[position])
        return jnp.where(position < mine, longer, subtotal)

    return lax.fori_loop(0, count - 1, turn, subtotal)


def recurrence_kernel(retain_ref, drive_ref, out_ref, *, reverse):
    steps = drive_ref.shape[0]
    keep = retain_ref[...]

    def advance(position, state):
        hour = steps - 1 - position if reverse else position
        state = keep * state + drive_ref[pl.ds(hour, 1), :]
        out_ref[pl.ds(hour, 1), :] = state
        return state

    lax.fori_loop(0, steps, advance, jnp.zeros_like(keep), unroll=8)


def recurrence(retain_row, drive, reverse=False):
    steps, width = drive.shape
    return pl.pallas_call(
        functools.partial(recurrence_kernel, reverse=reverse),
        out_shape=jax.ShapeDtypeStruct((steps, width), jnp.float32),
        in_specs=[pl.BlockSpec(memory_space=pltpu.VMEM), pl.BlockSpec(memory_space=pltpu.VMEM)],
        out_specs=pl.BlockSpec(memory_space=pltpu.VMEM),
        cost_estimate=pl.CostEstimate(
            flops=2 * steps * width, transcendentals=0, bytes_accessed=8 * steps * width + 4 * width
        ),
    )(retain_row, drive)


def split_pair(value):
    high = value.astype(jnp.bfloat16)
    low = (value - high.astype(jnp.float32)).astype(jnp.bfloat16)
    return jnp.concatenate([high, low], axis=0)


def shifted_rows(value, shift, fill):
    rows = lax.broadcasted_iota(jnp.int32, value.shape, 0)
    return jnp.where(rows >= shift, pltpu.roll(value, shift, 0), fill)


def forward_kernel(*refs, has_inflow):
    if has_inflow:
        coef_ref, upper_ref, side_ref, conf_ref, lateral_ref, out_ref, outlet_ref, inflow_ref = refs
    else:
        coef_ref, lateral_ref, out_ref, outlet_ref = refs
    steps, width = lateral_ref.shape
    narrow = outlet_ref.shape[1]
    tile = 8
    gain_now, gain_prev, gain_side = coef_ref[0:1, :], coef_ref[1:2, :], coef_ref[2:3, :]
    keep, live = coef_ref[3:4, :], coef_ref[4:5, :]
    if has_inflow:
        source = jnp.concatenate([upper_ref[...], side_ref[...]], axis=1)
        product = jnp.dot(split_pair(source), conf_ref[...], preferred_element_type=jnp.float32)
        inflow_ref[...] = product[:steps] + product[steps:]
    keep_tile = jnp.broadcast_to(keep, (tile, width))
    powers = keep_tile
    span = 1
    while span < tile:
        powers = powers * shifted_rows(powers, span, 1.0)
        span *= 2
    keep_steps = []
    factor = keep
    for unused in range(3):
        keep_steps.append(factor)
        factor = factor * factor

    def advance(block, carry):
        state, before = carry
        rows = pl.ds(pl.multiple_of(block * tile, tile), tile)
        drive_side = gain_side * lateral_ref[rows, :]
        if has_inflow:
            now = inflow_ref[rows, :]
            earlier = jnp.where(
                lax.broadcasted_iota(jnp.int32, (tile, width), 0) >= 1,
                pltpu.roll(now, 1, 0),
                before,
            )
            drive = (gain_now * now + gain_prev * earlier) + drive_side
            before = now[tile - 1 : tile, :]
        else:
            drive = drive_side
        span = 1
        for factor in keep_steps:
            drive = drive + factor * shifted_rows(drive, span, 0.0)
            span *= 2
        block_state = drive + powers * state
        flow = block_state * live
        out_ref[rows, :] = flow
        outlet_ref[rows, :] = flow[:, :narrow]
        return block_state[tile - 1 : tile, :], before

    zero = jnp.zeros_like(keep)
    lax.fori_loop(0, steps // tile, advance, (zero, zero), unroll=2)


def backward_kernel(*refs, has_down, emit):
    refs = list(refs)
    coef_ref, cot_ref = refs[0], refs[1]
    rest = refs[2:]
    if has_down:
        down_ref, side_ref = rest[0], rest[1]
        rest = rest[2:]
    if emit:
        conf_ref, adj_ref, own_ref, spill_ref, work_ref = rest
    else:
        (adj_ref,) = rest
    steps = cot_ref.shape[0]
    gain_now, gain_prev = coef_ref[0:1, :], coef_ref[1:2, :]
    keep, live = coef_ref[3:4, :], coef_ref[4:5, :]

    def advance(position, carry):
        hour = steps - 1 - position
        state, later = carry
        load = cot_ref[pl.ds(hour, 1), :]
        if has_down:
            down = down_ref[pl.ds(hour, 1), :]
            side = side_ref[pl.ds(hour, 1), :]
            narrow = side.shape[1]
            down = jnp.concatenate([down[:, :narrow] + side, down[:, narrow:]], axis=1)
            load = load + down
        state = keep * state + live * load
        adj_ref[pl.ds(hour, 1), :] = state
        if emit:
            work_ref[pl.ds(hour, 1), :] = gain_now * state + gain_prev * later
        return state, state

    zero = jnp.zeros_like(keep)
    lax.fori_loop(0, steps, advance, (zero, zero), unroll=8)
    if emit:
        spread = jnp.dot(split_pair(work_ref[...]), conf_ref[...], preferred_element_type=jnp.float32)
        width = own_ref.shape[1]
        own_ref[...] = spread[:steps, :width] + spread[steps:, :width]
        spill_ref[...] = spread[:steps, width:] + spread[steps:, width:]


def vmem_call(kernel, outs, *args, scratch=()):
    steps, width = outs[0]
    return pl.pallas_call(
        kernel,
        out_shape=[jax.ShapeDtypeStruct(shape, jnp.float32) for shape in outs],
        in_specs=[pl.BlockSpec(memory_space=pltpu.VMEM)] * len(args),
        out_specs=[pl.BlockSpec(memory_space=pltpu.VMEM)] * len(outs),
        scratch_shapes=[pltpu.VMEM(shape, jnp.float32) for shape in scratch],
        cost_estimate=pl.CostEstimate(
            flops=10 * steps * width + 4 * steps * width * (width + width // 8),
            transcendentals=0,
            bytes_accessed=sum(a.size * a.dtype.itemsize for a in args) + 4 * sum(r * c for r, c in outs),
        ),
    )(*args)


def routed(coef, lateral_all, upper=None, side=None, confluence=None):
    steps, width = lateral_all.shape
    narrow = width // 8
    if upper is None:
        kernel = functools.partial(forward_kernel, has_inflow=False)
        flow, outlet = vmem_call(kernel, [(steps, width), (steps, narrow)], coef, lateral_all)
        return flow, outlet, None
    kernel = functools.partial(forward_kernel, has_inflow=True)
    return vmem_call(
        kernel,
        [(steps, width), (steps, narrow), (steps, width)],
        coef, upper, side, confluence, lateral_all,
    )


def adjoined(coef, cotangent_all, down=None, side=None, confluence_t=None):
    steps, width = cotangent_all.shape
    emit = confluence_t is not None
    kernel = functools.partial(backward_kernel, has_down=down is not None, emit=emit)
    args = (coef, cotangent_all) if down is None else (coef, cotangent_all, down, side)
    if not emit:
        return vmem_call(kernel, [(steps, width)], *args)[0], None, None
    adjoint, own, spill = vmem_call(
        kernel,
        [(steps, width), (steps, width), (steps, width // 8)],
        *args,
        confluence_t,
        scratch=[(steps, width)],
    )
    return adjoint, own, spill


def split_three(value):
    pieces = []
    rest = value
    for _ in range(PIECES):
        piece = lax.reduce_precision(rest, exponent_bits=8, mantissa_bits=7)
        pieces.append(piece)
        rest = rest - piece
    return jnp.concatenate(pieces, axis=0).astype(jnp.bfloat16)


def joined_three(product):
    rows = product.shape[0] // PIECES
    total = product[:rows]
    for piece_at in range(1, PIECES):
        total = total + product[piece_at * rows : (piece_at + 1) * rows]
    return total


def coefficients(raw_params):
    travel = 1.0 + 47.0 * jax.nn.sigmoid(raw_params[0])
    weighting = 0.05 + 0.4 * jax.nn.sigmoid(raw_params[1])
    storage = travel * (1.0 - weighting)
    divisor = storage + 0.5
    return (
        (0.5 - travel * weighting) / divisor,
        (0.5 + travel * weighting) / divisor,
        (storage - 0.5) / divisor,
        1.0 / divisor,
    )


def affine_join(earlier, latter):
    return (earlier[0] * latter[0], latter[0] * earlier[1] + latter[1])


def stack_affine(pair):
    return jnp.stack([pair[0], pair[1]], axis=0)


def split_affine(stacked):
    return (stacked[0], stacked[1])


def stacked_affine(earlier, latter):
    return stack_affine(affine_join(split_affine(earlier), split_affine(latter)))


def linear_pairs(steps_up, steps_side, core):
    levels, basins, groups = (
        lax.axis_size("level"),
        lax.axis_size("basin"),
        lax.axis_size("group"),
    )
    pairs = []
    for level in range(levels):
        for basin in range(basins):
            target_level, target_basin = level + steps_up, basin + steps_side
            if 0 <= target_level < levels and 0 <= target_basin < basins:
                pairs.append(
                    (
                        (level * basins + basin) * groups + core,
                        (target_level * basins + target_basin) * groups + core,
                    )
                )
    return pairs


def both_ways(value, side_steps):
    pairs = linear_pairs(1, side_steps, 0) + linear_pairs(-1, -side_steps, 1)
    return lax.ppermute(value, ("level", "basin", "group"), pairs)


def body(lateral, cotangent, attributes, region, feeders, feeder_count, live_blocks, net_weight):
    steps_dev, reach_dev = lateral.shape
    outlets = reach_dev // 8
    regions, attr_count, param_count = net_weight.shape
    levels = lax.axis_size("level")
    up_count = feeders.shape[0]
    mine = lax.axis_index("group")
    slot_ids = lax.broadcasted_iota(jnp.int32, (reach_dev,), 0)
    live_mask = (slot_ids < live_blocks[0] * BLOCK).astype(jnp.float32)
    member_table = (
        region[None, :] == lax.broadcasted_iota(jnp.int32, (regions, reach_dev), 0)
    ).astype(jnp.float32)
    per_region = jnp.dot(
        jnp.transpose(net_weight, (0, 2, 1)).reshape(regions * param_count, attr_count),
        attributes,
        precision=lax.Precision.HIGHEST,
        preferred_element_type=jnp.float32,
    )
    raw_params = jnp.einsum(
        "rpi,ri->pi",
        per_region.reshape(regions, param_count, reach_dev),
        member_table,
        precision=lax.Precision.HIGHEST,
    )
    coef_set, coef_pull = jax.vjp(coefficients, raw_params)
    gain_now, gain_prev, retain, gain_side = coef_set
    zero_row = jnp.zeros((reach_dev,), jnp.float32)
    coef = jnp.stack(
        [gain_now, gain_prev, gain_side, retain, live_mask, zero_row, zero_row, zero_row], axis=0
    )
    arrived = lax.ppermute(jnp.where(mine == 0, cotangent, lateral), "group", [(0, 1), (1, 0)])
    window = jnp.where(
        mine == 0,
        jnp.concatenate([lateral, arrived], axis=0),
        jnp.concatenate([arrived, cotangent], axis=0),
    )
    lateral_all = window
    cotangent_all = window
    steps_all = window.shape[0]
    source_ids = lax.broadcasted_iota(jnp.int32, (reach_dev + outlets, reach_dev), 0)
    confluence = jnp.zeros((reach_dev + outlets, reach_dev), jnp.float32)
    for upslot in range(up_count):
        confluence = confluence + (
            (source_ids == feeders[upslot][None, :]) & (upslot < feeder_count)[None, :]
        ).astype(jnp.float32)
    confluence = confluence.astype(jnp.bfloat16)
    target_ids = lax.broadcasted_iota(jnp.int32, (reach_dev, reach_dev + outlets), 1)
    confluence_t = jnp.zeros((reach_dev, reach_dev + outlets), jnp.float32)
    for upslot in range(up_count):
        confluence_t = confluence_t + (
            (target_ids == feeders[upslot][:, None]) & (upslot < feeder_count)[:, None]
        ).astype(jnp.float32)
    confluence_t = confluence_t.astype(jnp.bfloat16)
    zero_flow = jnp.zeros((steps_all, reach_dev), jnp.float32)

    def forward_first(operands):
        flow, outlet, unused = routed(coef, lateral_all)
        return flow, outlet, flow, zero_flow, lateral_all

    def backward_first(operands):
        adjoint, own, side = adjoined(coef, cotangent_all, confluence_t=confluence_t)
        return own, side, adjoint, zero_flow, zero_flow

    def forward_step(operands):
        upper, side = operands
        flow, outlet, inflow = routed(coef, lateral_all, upper, side, confluence)
        return flow, outlet, flow, inflow, lateral_all

    def backward_step(operands):
        upper, side = operands
        adjoint, own, side = adjoined(coef, cotangent_all, upper, side, confluence_t)
        return own, side, adjoint, zero_flow, zero_flow

    def backward_last(operands):
        upper, side = operands
        adjoint, unused, unused_side = adjoined(coef, cotangent_all, upper, side)
        return zero_flow, side, adjoint, zero_flow, zero_flow

    message, outlet_message, *kept = lax.cond(mine == 0, forward_first, backward_first, None)
    for level_step in range(1, levels):
        upper_early = both_ways(message[:steps_dev], 0)
        upper_late = both_ways(message[steps_dev:], 0)
        side = both_ways(outlet_message, 1)
        upper = jnp.concatenate([upper_early, upper_late], axis=0)
        later = backward_step if level_step + 1 < levels else backward_last
        message, outlet_message, *kept = lax.cond(
            mine == 0, forward_step, later, (upper, side)
        )
    kept = jnp.stack(kept, axis=0)
    other = lax.ppermute(kept, "group", [(0, 1), (1, 0)])
    forward_kept = jnp.where(mine == 0, kept, other)
    backward_kept = jnp.where(mine == 0, other, kept)
    outflow, inflow, lateral_all = forward_kept[0], forward_kept[1], forward_kept[2]
    adjoint = backward_kept[0]
    zero_first = jnp.zeros((1, reach_dev), jnp.float32)
    flow_before = jnp.concatenate([zero_first, outflow[:-1]], axis=0)
    inflow_before = jnp.concatenate([zero_first, inflow[:-1]], axis=0)
    coef_grads = (
        jnp.sum(adjoint * inflow, axis=0),
        jnp.sum(adjoint * inflow_before, axis=0),
        jnp.sum(adjoint * flow_before, axis=0),
        jnp.sum(adjoint * lateral_all, axis=0),
    )
    raw_grad = coef_pull(coef_grads)[0]
    owned_rows = regions // lax.axis_size("basin")
    weighted = (member_table[:, None, :] * raw_grad[None, :, :]).reshape(
        regions * param_count, reach_dev
    )
    summed = jnp.dot(
        weighted, attributes.T, precision=lax.Precision.HIGHEST, preferred_element_type=jnp.float32
    )
    local_grad = jnp.transpose(summed.reshape(regions, param_count, attr_count), (0, 2, 1))
    basins = lax.axis_size("basin")
    share_size = owned_rows * attr_count * param_count
    replicated = jnp.broadcast_to(
        local_grad.reshape(1, basins, share_size), (levels, basins, share_size)
    ).reshape(levels * basins, share_size)
    grad_net = jnp.sum(
        lax.all_to_all(replicated, ("level", "basin"), 0, 0, tiled=True), axis=0
    ).reshape(owned_rows, attr_count, param_count)
    own_hours = lax.dynamic_slice_in_dim(outflow, mine * steps_dev, steps_dev, axis=0)
    return (own_hours, grad_net)


def solution(mesh):
    in_specs = (
        P("group", ("level", "basin")),
        P("group", ("level", "basin")),
        P(None, ("level", "basin")),
        P(("level", "basin")),
        P(None, ("level", "basin")),
        P(("level", "basin")),
        P(("level", "basin")),
        P(),
    )
    out_specs = (P("group", ("level", "basin")), P("basin", None, None))
    return jax.shard_map(body, mesh=mesh, in_specs=in_specs, out_specs=out_specs, check_vma=False)
```

```python
import functools

import jax
import jax.numpy as jnp
from jax import lax
from jax.sharding import PartitionSpec as P
from jax.experimental import pallas as pl
from jax.experimental.pallas import tpu as pltpu

BLOCK = 128
PIECES = 2


def shifted(value, axis, steps):
    count = lax.axis_size(axis)
    leading, last = (max(0, -steps), min(count, count - steps))
    return lax.ppermute(value, axis, [(source, source + steps) for source in range(leading, last)])


def diagonal(value, steps):
    levels, basins = lax.axis_size("level"), lax.axis_size("basin")
    pairs = []
    for level in range(max(0, -steps), min(levels, levels - steps)):
        for basin in range(max(0, -steps), min(basins, basins - steps)):
            pairs.append((level * basins + basin, (level + steps) * basins + basin + steps))
    return lax.ppermute(value, ("level", "basin"), pairs)


def exchanged(value, axis, mask):
    count = lax.axis_size(axis)
    return lax.ppermute(value, axis, [(source, source ^ mask) for source in range(count)])


def scattered_sum(blocks, axis):
    count, mine = (lax.axis_size(axis), lax.axis_index(axis))
    width = count
    while width > 1:
        width //= 2
        lower, upper = blocks[:width], blocks[width:]
        high = (mine & width) > 0
        kept = jnp.where(high, upper, lower)
        sent = jnp.where(high, lower, upper)
        blocks = kept + exchanged(sent, axis, width)
    return blocks[0]


def butterfly_sum(value, axis):
    mask = 1
    while mask < lax.axis_size(axis):
        value = value + exchanged(value, axis, mask)
        mask *= 2
    return value


def whole_window(value):
    return lax.all_gather(value, "group", axis=0, tiled=True)


def carried_in(value, axis, join, neutral, backward):
    count, mine = (lax.axis_size(axis), lax.axis_index(axis))
    pieces = lax.all_gather(value, axis)
    if backward:
        pieces = pieces[::-1]
        mine = count - 1 - mine
    subtotal = jnp.full_like(value, 0) + jnp.asarray(neutral, value.dtype)

    def turn(position, subtotal):
        longer = join(subtotal, pieces[position])
        return jnp.where(position < mine, longer, subtotal)

    return lax.fori_loop(0, count - 1, turn, subtotal)


def recurrence_kernel(retain_ref, drive_ref, out_ref, *, reverse):
    steps = drive_ref.shape[0]
    keep = retain_ref[...]

    def advance(position, state):
        hour = steps - 1 - position if reverse else position
        state = keep * state + drive_ref[pl.ds(hour, 1), :]
        out_ref[pl.ds(hour, 1), :] = state
        return state

    lax.fori_loop(0, steps, advance, jnp.zeros_like(keep), unroll=8)


def recurrence(retain_row, drive, reverse=False):
    steps, width = drive.shape
    return pl.pallas_call(
        functools.partial(recurrence_kernel, reverse=reverse),
        out_shape=jax.ShapeDtypeStruct((steps, width), jnp.float32),
        in_specs=[pl.BlockSpec(memory_space=pltpu.VMEM), pl.BlockSpec(memory_space=pltpu.VMEM)],
        out_specs=pl.BlockSpec(memory_space=pltpu.VMEM),
        cost_estimate=pl.CostEstimate(
            flops=2 * steps * width, transcendentals=0, bytes_accessed=8 * steps * width + 4 * width
        ),
    )(retain_row, drive)


def split_pair(value):
    high = value.astype(jnp.bfloat16)
    low = (value - high.astype(jnp.float32)).astype(jnp.bfloat16)
    return jnp.concatenate([high, low], axis=0)


def shifted_rows(value, shift, fill):
    rows = lax.broadcasted_iota(jnp.int32, value.shape, 0)
    return jnp.where(rows >= shift, pltpu.roll(value, shift, 0), fill)


def forward_kernel(*refs, has_inflow):
    if has_inflow:
        coef_ref, upper_ref, side_ref, conf_ref, early_ref, late_ref, out_ref, outlet_ref, inflow_ref = refs
    else:
        coef_ref, early_ref, late_ref, out_ref, outlet_ref = refs
    half, width = early_ref.shape
    steps = 2 * half
    narrow = outlet_ref.shape[1]
    tile = 8
    gain_now, gain_prev, gain_side = coef_ref[0:1, :], coef_ref[1:2, :], coef_ref[2:3, :]
    keep, live = coef_ref[3:4, :], coef_ref[4:5, :]
    if has_inflow:
        source = jnp.concatenate([upper_ref[...], side_ref[...]], axis=1)
        product = jnp.dot(split_pair(source), conf_ref[...], preferred_element_type=jnp.float32)
        inflow_ref[...] = product[:steps] + product[steps:]
    keep_tile = jnp.broadcast_to(keep, (tile, width))
    powers = keep_tile
    span = 1
    while span < tile:
        powers = powers * shifted_rows(powers, span, 1.0)
        span *= 2
    keep_steps = []
    factor = keep
    for unused in range(3):
        keep_steps.append(factor)
        factor = factor * factor

    def advance(block, carry, lateral_ref, first):
        state, before = carry
        rows = pl.ds(pl.multiple_of((block + first) * tile, tile), tile)
        own_rows = pl.ds(pl.multiple_of(block * tile, tile), tile)
        drive_side = gain_side * lateral_ref[own_rows, :]
        if has_inflow:
            now = inflow_ref[rows, :]
            earlier = jnp.where(
                lax.broadcasted_iota(jnp.int32, (tile, width), 0) >= 1,
                pltpu.roll(now, 1, 0),
                before,
            )
            drive = (gain_now * now + gain_prev * earlier) + drive_side
            before = now[tile - 1 : tile, :]
        else:
            drive = drive_side
        span = 1
        for factor in keep_steps:
            drive = drive + factor * shifted_rows(drive, span, 0.0)
            span *= 2
        block_state = drive + powers * state
        flow = block_state * live
        out_ref[rows, :] = flow
        outlet_ref[rows, :] = flow[:, :narrow]
        return block_state[tile - 1 : tile, :], before

    zero = jnp.zeros_like(keep)
    blocks = half // tile
    carry = lax.fori_loop(
        0, blocks, lambda block, carry: advance(block, carry, early_ref, 0), (zero, zero), unroll=2
    )
    lax.fori_loop(
        0, blocks, lambda block, carry: advance(block, carry, late_ref, blocks), carry, unroll=2
    )


def backward_kernel(*refs, has_down, emit):
    refs = list(refs)
    coef_ref, early_ref, late_ref = refs[0], refs[1], refs[2]
    rest = refs[3:]
    if has_down:
        down_ref, side_ref = rest[0], rest[1]
        rest = rest[2:]
    if emit:
        conf_ref, adj_ref, own_ref, spill_ref, work_ref = rest
    else:
        (adj_ref,) = rest
    half = early_ref.shape[0]
    steps = 2 * half
    gain_now, gain_prev = coef_ref[0:1, :], coef_ref[1:2, :]
    keep, live = coef_ref[3:4, :], coef_ref[4:5, :]

    def advance(hour, carry, cot_ref, cot_at):
        state, later = carry
        load = cot_ref[pl.ds(cot_at, 1), :]
        if has_down:
            down = down_ref[pl.ds(hour, 1), :]
            side = side_ref[pl.ds(hour, 1), :]
            narrow = side.shape[1]
            down = jnp.concatenate([down[:, :narrow] + side, down[:, narrow:]], axis=1)
            load = load + down
        state = keep * state + live * load
        adj_ref[pl.ds(hour, 1), :] = state
        if emit:
            work_ref[pl.ds(hour, 1), :] = gain_now * state + gain_prev * later
        return state, state

    zero = jnp.zeros_like(keep)
    carry = lax.fori_loop(
        0,
        half,
        lambda position, carry: advance(steps - 1 - position, carry, late_ref, half - 1 - position),
        (zero, zero),
        unroll=8,
    )
    lax.fori_loop(
        0,
        half,
        lambda position, carry: advance(half - 1 - position, carry, early_ref, half - 1 - position),
        carry,
        unroll=8,
    )
    if emit:
        spread = jnp.dot(split_pair(work_ref[...]), conf_ref[...], preferred_element_type=jnp.float32)
        width = own_ref.shape[1]
        own_ref[...] = spread[:steps, :width] + spread[steps:, :width]
        spill_ref[...] = spread[:steps, width:] + spread[steps:, width:]


def vmem_call(kernel, outs, *args, scratch=()):
    steps, width = outs[0]
    return pl.pallas_call(
        kernel,
        out_shape=[jax.ShapeDtypeStruct(shape, jnp.float32) for shape in outs],
        in_specs=[pl.BlockSpec(memory_space=pltpu.VMEM)] * len(args),
        out_specs=[pl.BlockSpec(memory_space=pltpu.VMEM)] * len(outs),
        scratch_shapes=[pltpu.VMEM(shape, jnp.float32) for shape in scratch],
        cost_estimate=pl.CostEstimate(
            flops=10 * steps * width + 4 * steps * width * (width + width // 8),
            transcendentals=0,
            bytes_accessed=sum(a.size * a.dtype.itemsize for a in args) + 4 * sum(r * c for r, c in outs),
        ),
    )(*args)


def routed(coef, early, late, upper=None, side=None, confluence=None):
    half, width = early.shape
    steps = 2 * half
    narrow = width // 8
    if upper is None:
        kernel = functools.partial(forward_kernel, has_inflow=False)
        flow, outlet = vmem_call(kernel, [(steps, width), (steps, narrow)], coef, early, late)
        return flow, outlet, None
    kernel = functools.partial(forward_kernel, has_inflow=True)
    return vmem_call(
        kernel,
        [(steps, width), (steps, narrow), (steps, width)],
        coef, upper, side, confluence, early, late,
    )


def adjoined(coef, early, late, down=None, side=None, confluence_t=None):
    half, width = early.shape
    steps = 2 * half
    emit = confluence_t is not None
    kernel = functools.partial(backward_kernel, has_down=down is not None, emit=emit)
    args = (coef, early, late) if down is None else (coef, early, late, down, side)
    if not emit:
        return vmem_call(kernel, [(steps, width)], *args)[0], None, None
    adjoint, own, spill = vmem_call(
        kernel,
        [(steps, width), (steps, width), (steps, width // 8)],
        *args,
        confluence_t,
        scratch=[(steps, width)],
    )
    return adjoint, own, spill


def split_three(value):
    pieces = []
    rest = value
    for _ in range(PIECES):
        piece = lax.reduce_precision(rest, exponent_bits=8, mantissa_bits=7)
        pieces.append(piece)
        rest = rest - piece
    return jnp.concatenate(pieces, axis=0).astype(jnp.bfloat16)


def joined_three(product):
    rows = product.shape[0] // PIECES
    total = product[:rows]
    for piece_at in range(1, PIECES):
        total = total + product[piece_at * rows : (piece_at + 1) * rows]
    return total


def coefficients(raw_params):
    travel = 1.0 + 47.0 * jax.nn.sigmoid(raw_params[0])
    weighting = 0.05 + 0.4 * jax.nn.sigmoid(raw_params[1])
    storage = travel * (1.0 - weighting)
    divisor = storage + 0.5
    return (
        (0.5 - travel * weighting) / divisor,
        (0.5 + travel * weighting) / divisor,
        (storage - 0.5) / divisor,
        1.0 / divisor,
    )


def affine_join(earlier, latter):
    return (earlier[0] * latter[0], latter[0] * earlier[1] + latter[1])


def stack_affine(pair):
    return jnp.stack([pair[0], pair[1]], axis=0)


def split_affine(stacked):
    return (stacked[0], stacked[1])


def stacked_affine(earlier, latter):
    return stack_affine(affine_join(split_affine(earlier), split_affine(latter)))


def linear_pairs(steps_up, steps_side, core):
    levels, basins, groups = (
        lax.axis_size("level"),
        lax.axis_size("basin"),
        lax.axis_size("group"),
    )
    pairs = []
    for level in range(levels):
        for basin in range(basins):
            target_level, target_basin = level + steps_up, basin + steps_side
            if 0 <= target_level < levels and 0 <= target_basin < basins:
                pairs.append(
                    (
                        (level * basins + basin) * groups + core,
                        (target_level * basins + target_basin) * groups + core,
                    )
                )
    return pairs


def both_ways(value, side_steps):
    pairs = linear_pairs(1, side_steps, 0) + linear_pairs(-1, -side_steps, 1)
    return lax.ppermute(value, ("level", "basin", "group"), pairs)


def body(lateral, cotangent, attributes, region, feeders, feeder_count, live_blocks, net_weight):
    steps_dev, reach_dev = lateral.shape
    outlets = reach_dev // 8
    regions, attr_count, param_count = net_weight.shape
    levels = lax.axis_size("level")
    up_count = feeders.shape[0]
    mine = lax.axis_index("group")
    slot_ids = lax.broadcasted_iota(jnp.int32, (reach_dev,), 0)
    live_mask = (slot_ids < live_blocks[0] * BLOCK).astype(jnp.float32)
    member_table = (
        region[None, :] == lax.broadcasted_iota(jnp.int32, (regions, reach_dev), 0)
    ).astype(jnp.float32)
    per_region = jnp.dot(
        jnp.transpose(net_weight, (0, 2, 1)).reshape(regions * param_count, attr_count),
        attributes,
        precision=lax.Precision.HIGHEST,
        preferred_element_type=jnp.float32,
    )
    raw_params = jnp.einsum(
        "rpi,ri->pi",
        per_region.reshape(regions, param_count, reach_dev),
        member_table,
        precision=lax.Precision.HIGHEST,
    )
    coef_set, coef_pull = jax.vjp(coefficients, raw_params)
    gain_now, gain_prev, retain, gain_side = coef_set
    zero_row = jnp.zeros((reach_dev,), jnp.float32)
    coef = jnp.stack(
        [gain_now, gain_prev, gain_side, retain, live_mask, zero_row, zero_row, zero_row], axis=0
    )
    arrived = lax.ppermute(jnp.where(mine == 0, cotangent, lateral), "group", [(0, 1), (1, 0)])
    early = jnp.where(mine == 0, lateral, arrived)
    late = jnp.where(mine == 0, arrived, cotangent)
    steps_all = 2 * steps_dev
    source_ids = lax.broadcasted_iota(jnp.int32, (reach_dev + outlets, reach_dev), 0)
    confluence = jnp.zeros((reach_dev + outlets, reach_dev), jnp.float32)
    for upslot in range(up_count):
        confluence = confluence + (
            (source_ids == feeders[upslot][None, :]) & (upslot < feeder_count)[None, :]
        ).astype(jnp.float32)
    confluence = confluence.astype(jnp.bfloat16)
    target_ids = lax.broadcasted_iota(jnp.int32, (reach_dev, reach_dev + outlets), 1)
    confluence_t = jnp.zeros((reach_dev, reach_dev + outlets), jnp.float32)
    for upslot in range(up_count):
        confluence_t = confluence_t + (
            (target_ids == feeders[upslot][:, None]) & (upslot < feeder_count)[:, None]
        ).astype(jnp.float32)
    confluence_t = confluence_t.astype(jnp.bfloat16)
    zero_flow = jnp.zeros((steps_all, reach_dev), jnp.float32)

    def forward_first(operands):
        flow, outlet, unused = routed(coef, early, late)
        return flow, outlet, flow, zero_flow, zero_flow

    def backward_first(operands):
        adjoint, own, side = adjoined(coef, early, late, confluence_t=confluence_t)
        return own, side, adjoint, zero_flow, zero_flow

    def forward_step(operands):
        upper, side = operands
        flow, outlet, inflow = routed(coef, early, late, upper, side, confluence)
        return flow, outlet, flow, inflow, zero_flow

    def forward_last(operands):
        flow, outlet, first, inflow, unused = forward_step(operands)
        return flow, outlet, first, inflow, jnp.concatenate([early, late], axis=0)

    def backward_step(operands):
        upper, side = operands
        adjoint, own, side = adjoined(coef, early, late, upper, side, confluence_t)
        return own, side, adjoint, zero_flow, zero_flow

    def backward_last(operands):
        upper, side = operands
        adjoint, unused, unused_side = adjoined(coef, early, late, upper, side)
        return zero_flow, side, adjoint, zero_flow, zero_flow

    message, outlet_message, *kept = lax.cond(mine == 0, forward_first, backward_first, None)
    for level_step in range(1, levels):
        upper = both_ways(message, 0)
        side = both_ways(outlet_message, 1)
        last = level_step + 1 == levels
        message, outlet_message, *kept = lax.cond(
            mine == 0,
            forward_last if last else forward_step,
            backward_last if last else backward_step,
            (upper, side),
        )
    kept = jnp.stack(kept, axis=0)
    other = lax.ppermute(kept, "group", [(0, 1), (1, 0)])
    forward_kept = jnp.where(mine == 0, kept, other)
    backward_kept = jnp.where(mine == 0, other, kept)
    outflow, inflow, lateral_all = forward_kept[0], forward_kept[1], forward_kept[2]
    adjoint = backward_kept[0]
    zero_first = jnp.zeros((1, reach_dev), jnp.float32)
    flow_before = jnp.concatenate([zero_first, outflow[:-1]], axis=0)
    inflow_before = jnp.concatenate([zero_first, inflow[:-1]], axis=0)
    coef_grads = (
        jnp.sum(adjoint * inflow, axis=0),
        jnp.sum(adjoint * inflow_before, axis=0),
        jnp.sum(adjoint * flow_before, axis=0),
        jnp.sum(adjoint * lateral_all, axis=0),
    )
    raw_grad = coef_pull(coef_grads)[0]
    owned_rows = regions // lax.axis_size("basin")
    weighted = (member_table[:, None, :] * raw_grad[None, :, :]).reshape(
        regions * param_count, reach_dev
    )
    summed = jnp.dot(
        weighted, attributes.T, precision=lax.Precision.HIGHEST, preferred_element_type=jnp.float32
    )
    local_grad = jnp.transpose(summed.reshape(regions, param_count, attr_count), (0, 2, 1))
    basins = lax.axis_size("basin")
    share_size = owned_rows * attr_count * param_count
    replicated = jnp.broadcast_to(
        local_grad.reshape(1, basins, share_size), (levels, basins, share_size)
    ).reshape(levels * basins, share_size)
    grad_net = jnp.sum(
        lax.all_to_all(replicated, ("level", "basin"), 0, 0, tiled=True), axis=0
    ).reshape(owned_rows, attr_count, param_count)
    own_hours = lax.dynamic_slice_in_dim(outflow, mine * steps_dev, steps_dev, axis=0)
    return (own_hours, grad_net)


def solution(mesh):
    in_specs = (
        P("group", ("level", "basin")),
        P("group", ("level", "basin")),
        P(None, ("level", "basin")),
        P(("level", "basin")),
        P(None, ("level", "basin")),
        P(("level", "basin")),
        P(("level", "basin")),
        P(),
    )
    out_specs = (P("group", ("level", "basin")), P("basin", None, None))
    return jax.shard_map(body, mesh=mesh, in_specs=in_specs, out_specs=out_specs, check_vma=False)
```

```python
import functools

import jax
import jax.numpy as jnp
from jax import lax
from jax.sharding import PartitionSpec as P
from jax.experimental import pallas as pl
from jax.experimental.pallas import tpu as pltpu

BLOCK = 128
PIECES = 2


def shifted(value, axis, steps):
    count = lax.axis_size(axis)
    leading, last = (max(0, -steps), min(count, count - steps))
    return lax.ppermute(value, axis, [(source, source + steps) for source in range(leading, last)])


def diagonal(value, steps):
    levels, basins = lax.axis_size("level"), lax.axis_size("basin")
    pairs = []
    for level in range(max(0, -steps), min(levels, levels - steps)):
        for basin in range(max(0, -steps), min(basins, basins - steps)):
            pairs.append((level * basins + basin, (level + steps) * basins + basin + steps))
    return lax.ppermute(value, ("level", "basin"), pairs)


def exchanged(value, axis, mask):
    count = lax.axis_size(axis)
    return lax.ppermute(value, axis, [(source, source ^ mask) for source in range(count)])


def scattered_sum(blocks, axis):
    count, mine = (lax.axis_size(axis), lax.axis_index(axis))
    width = count
    while width > 1:
        width //= 2
        lower, upper = blocks[:width], blocks[width:]
        high = (mine & width) > 0
        kept = jnp.where(high, upper, lower)
        sent = jnp.where(high, lower, upper)
        blocks = kept + exchanged(sent, axis, width)
    return blocks[0]


def butterfly_sum(value, axis):
    mask = 1
    while mask < lax.axis_size(axis):
        value = value + exchanged(value, axis, mask)
        mask *= 2
    return value


def whole_window(value):
    return lax.all_gather(value, "group", axis=0, tiled=True)


def carried_in(value, axis, join, neutral, backward):
    count, mine = (lax.axis_size(axis), lax.axis_index(axis))
    pieces = lax.all_gather(value, axis)
    if backward:
        pieces = pieces[::-1]
        mine = count - 1 - mine
    subtotal = jnp.full_like(value, 0) + jnp.asarray(neutral, value.dtype)

    def turn(position, subtotal):
        longer = join(subtotal, pieces[position])
        return jnp.where(position < mine, longer, subtotal)

    return lax.fori_loop(0, count - 1, turn, subtotal)


def recurrence_kernel(retain_ref, drive_ref, out_ref, *, reverse):
    steps = drive_ref.shape[0]
    keep = retain_ref[...]

    def advance(position, state):
        hour = steps - 1 - position if reverse else position
        state = keep * state + drive_ref[pl.ds(hour, 1), :]
        out_ref[pl.ds(hour, 1), :] = state
        return state

    lax.fori_loop(0, steps, advance, jnp.zeros_like(keep), unroll=8)


def recurrence(retain_row, drive, reverse=False):
    steps, width = drive.shape
    return pl.pallas_call(
        functools.partial(recurrence_kernel, reverse=reverse),
        out_shape=jax.ShapeDtypeStruct((steps, width), jnp.float32),
        in_specs=[pl.BlockSpec(memory_space=pltpu.VMEM), pl.BlockSpec(memory_space=pltpu.VMEM)],
        out_specs=pl.BlockSpec(memory_space=pltpu.VMEM),
        cost_estimate=pl.CostEstimate(
            flops=2 * steps * width, transcendentals=0, bytes_accessed=8 * steps * width + 4 * width
        ),
    )(retain_row, drive)


def split_pair(value):
    high = value.astype(jnp.bfloat16)
    low = (value - high.astype(jnp.float32)).astype(jnp.bfloat16)
    return jnp.concatenate([high, low], axis=0)


def shifted_rows(value, shift, fill):
    rows = lax.broadcasted_iota(jnp.int32, value.shape, 0)
    return jnp.where(rows >= shift, pltpu.roll(value, shift, 0), fill)


def forward_kernel(*refs, has_inflow):
    if has_inflow:
        coef_ref, upper_ref, side_ref, conf_ref, early_ref, late_ref, out_ref, outlet_ref, inflow_ref = refs
    else:
        coef_ref, early_ref, late_ref, out_ref, outlet_ref = refs
    half, width = early_ref.shape
    steps = 2 * half
    narrow = outlet_ref.shape[1]
    tile = 8
    gain_now, gain_prev, gain_side = coef_ref[0:1, :], coef_ref[1:2, :], coef_ref[2:3, :]
    keep, live = coef_ref[3:4, :], coef_ref[4:5, :]
    if has_inflow:
        source = jnp.concatenate([upper_ref[...], side_ref[...]], axis=1)
        product = jnp.dot(split_pair(source), conf_ref[...], preferred_element_type=jnp.float32)
        inflow_ref[...] = product[:steps] + product[steps:]
    keep_tile = jnp.broadcast_to(keep, (tile, width))
    powers = keep_tile
    span = 1
    while span < tile:
        powers = powers * shifted_rows(powers, span, 1.0)
        span *= 2
    keep_steps = []
    factor = keep
    for unused in range(3):
        keep_steps.append(factor)
        factor = factor * factor

    def advance(block, carry, lateral_ref, first):
        state, before = carry
        rows = pl.ds(pl.multiple_of((block + first) * tile, tile), tile)
        own_rows = pl.ds(pl.multiple_of(block * tile, tile), tile)
        drive_side = gain_side * lateral_ref[own_rows, :]
        if has_inflow:
            now = inflow_ref[rows, :]
            earlier = jnp.where(
                lax.broadcasted_iota(jnp.int32, (tile, width), 0) >= 1,
                pltpu.roll(now, 1, 0),
                before,
            )
            drive = (gain_now * now + gain_prev * earlier) + drive_side
            before = now[tile - 1 : tile, :]
        else:
            drive = drive_side
        span = 1
        for factor in keep_steps:
            drive = drive + factor * shifted_rows(drive, span, 0.0)
            span *= 2
        block_state = drive + powers * state
        flow = block_state * live
        out_ref[rows, :] = flow
        outlet_ref[rows, :] = flow[:, :narrow]
        return block_state[tile - 1 : tile, :], before

    zero = jnp.zeros_like(keep)
    blocks = half // tile
    carry = lax.fori_loop(
        0, blocks, lambda block, carry: advance(block, carry, early_ref, 0), (zero, zero), unroll=2
    )
    lax.fori_loop(
        0, blocks, lambda block, carry: advance(block, carry, late_ref, blocks), carry, unroll=2
    )


def backward_kernel(*refs, has_down, emit):
    refs = list(refs)
    coef_ref, early_ref, late_ref = refs[0], refs[1], refs[2]
    rest = refs[3:]
    if has_down:
        down_ref, side_ref = rest[0], rest[1]
        rest = rest[2:]
    if emit:
        conf_ref, adj_ref, own_ref, spill_ref, work_ref = rest
    else:
        (adj_ref,) = rest
    half = early_ref.shape[0]
    steps = 2 * half
    gain_now, gain_prev = coef_ref[0:1, :], coef_ref[1:2, :]
    keep, live = coef_ref[3:4, :], coef_ref[4:5, :]

    def advance(hour, carry, cot_ref, cot_at):
        state, later = carry
        load = cot_ref[pl.ds(cot_at, 1), :]
        if has_down:
            down = down_ref[pl.ds(hour, 1), :]
            side = side_ref[pl.ds(hour, 1), :]
            narrow = side.shape[1]
            down = jnp.concatenate([down[:, :narrow] + side, down[:, narrow:]], axis=1)
            load = load + down
        state = keep * state + live * load
        adj_ref[pl.ds(hour, 1), :] = state
        if emit:
            work_ref[pl.ds(hour, 1), :] = gain_now * state + gain_prev * later
        return state, state

    zero = jnp.zeros_like(keep)
    carry = lax.fori_loop(
        0,
        half,
        lambda position, carry: advance(steps - 1 - position, carry, late_ref, half - 1 - position),
        (zero, zero),
        unroll=8,
    )
    lax.fori_loop(
        0,
        half,
        lambda position, carry: advance(half - 1 - position, carry, early_ref, half - 1 - position),
        carry,
        unroll=8,
    )
    if emit:
        spread = jnp.dot(split_pair(work_ref[...]), conf_ref[...], preferred_element_type=jnp.float32)
        width = own_ref.shape[1]
        own_ref[...] = spread[:steps, :width] + spread[steps:, :width]
        spill_ref[...] = spread[:steps, width:] + spread[steps:, width:]


def vmem_call(kernel, outs, *args, scratch=()):
    steps, width = outs[0]
    return pl.pallas_call(
        kernel,
        out_shape=[jax.ShapeDtypeStruct(shape, jnp.float32) for shape in outs],
        in_specs=[pl.BlockSpec(memory_space=pltpu.VMEM)] * len(args),
        out_specs=[pl.BlockSpec(memory_space=pltpu.VMEM)] * len(outs),
        scratch_shapes=[pltpu.VMEM(shape, jnp.float32) for shape in scratch],
        cost_estimate=pl.CostEstimate(
            flops=10 * steps * width + 4 * steps * width * (width + width // 8),
            transcendentals=0,
            bytes_accessed=sum(a.size * a.dtype.itemsize for a in args) + 4 * sum(r * c for r, c in outs),
        ),
    )(*args)


def routed(coef, early, late, upper=None, side=None, confluence=None):
    half, width = early.shape
    steps = 2 * half
    narrow = width // 8
    if upper is None:
        kernel = functools.partial(forward_kernel, has_inflow=False)
        flow, outlet = vmem_call(kernel, [(steps, width), (steps, narrow)], coef, early, late)
        return flow, outlet, None
    kernel = functools.partial(forward_kernel, has_inflow=True)
    return vmem_call(
        kernel,
        [(steps, width), (steps, narrow), (steps, width)],
        coef, upper, side, confluence, early, late,
    )


def adjoined(coef, early, late, down=None, side=None, confluence_t=None):
    half, width = early.shape
    steps = 2 * half
    emit = confluence_t is not None
    kernel = functools.partial(backward_kernel, has_down=down is not None, emit=emit)
    args = (coef, early, late) if down is None else (coef, early, late, down, side)
    if not emit:
        return vmem_call(kernel, [(steps, width)], *args)[0], None, None
    adjoint, own, spill = vmem_call(
        kernel,
        [(steps, width), (steps, width), (steps, width // 8)],
        *args,
        confluence_t,
        scratch=[(steps, width)],
    )
    return adjoint, own, spill


def split_three(value):
    pieces = []
    rest = value
    for _ in range(PIECES):
        piece = lax.reduce_precision(rest, exponent_bits=8, mantissa_bits=7)
        pieces.append(piece)
        rest = rest - piece
    return jnp.concatenate(pieces, axis=0).astype(jnp.bfloat16)


def joined_three(product):
    rows = product.shape[0] // PIECES
    total = product[:rows]
    for piece_at in range(1, PIECES):
        total = total + product[piece_at * rows : (piece_at + 1) * rows]
    return total


def coefficients(raw_params):
    travel = 1.0 + 47.0 * jax.nn.sigmoid(raw_params[0])
    weighting = 0.05 + 0.4 * jax.nn.sigmoid(raw_params[1])
    storage = travel * (1.0 - weighting)
    divisor = storage + 0.5
    return (
        (0.5 - travel * weighting) / divisor,
        (0.5 + travel * weighting) / divisor,
        (storage - 0.5) / divisor,
        1.0 / divisor,
    )


def affine_join(earlier, latter):
    return (earlier[0] * latter[0], latter[0] * earlier[1] + latter[1])


def stack_affine(pair):
    return jnp.stack([pair[0], pair[1]], axis=0)


def split_affine(stacked):
    return (stacked[0], stacked[1])


def stacked_affine(earlier, latter):
    return stack_affine(affine_join(split_affine(earlier), split_affine(latter)))


def linear_pairs(steps_up, steps_side, core):
    levels, basins, groups = (
        lax.axis_size("level"),
        lax.axis_size("basin"),
        lax.axis_size("group"),
    )
    pairs = []
    for level in range(levels):
        for basin in range(basins):
            target_level, target_basin = level + steps_up, basin + steps_side
            if 0 <= target_level < levels and 0 <= target_basin < basins:
                pairs.append(
                    (
                        (level * basins + basin) * groups + core,
                        (target_level * basins + target_basin) * groups + core,
                    )
                )
    return pairs


def both_ways(value, side_steps):
    pairs = linear_pairs(1, side_steps, 0) + linear_pairs(-1, -side_steps, 1)
    return lax.ppermute(value, ("level", "basin", "group"), pairs)


def body(lateral, cotangent, attributes, region, feeders, feeder_count, live_blocks, net_weight):
    steps_dev, reach_dev = lateral.shape
    outlets = reach_dev // 8
    regions, attr_count, param_count = net_weight.shape
    levels = lax.axis_size("level")
    up_count = feeders.shape[0]
    mine = lax.axis_index("group")
    slot_ids = lax.broadcasted_iota(jnp.int32, (reach_dev,), 0)
    live_mask = (slot_ids < live_blocks[0] * BLOCK).astype(jnp.float32)
    member_table = (
        region[None, :] == lax.broadcasted_iota(jnp.int32, (regions, reach_dev), 0)
    ).astype(jnp.float32)
    per_region = jnp.dot(
        jnp.transpose(net_weight, (0, 2, 1)).reshape(regions * param_count, attr_count),
        attributes,
        precision=lax.Precision.HIGHEST,
        preferred_element_type=jnp.float32,
    )
    raw_params = jnp.einsum(
        "rpi,ri->pi",
        per_region.reshape(regions, param_count, reach_dev),
        member_table,
        precision=lax.Precision.HIGHEST,
    )
    coef_set, coef_pull = jax.vjp(coefficients, raw_params)
    gain_now, gain_prev, retain, gain_side = coef_set
    zero_row = jnp.zeros((reach_dev,), jnp.float32)
    coef = jnp.stack(
        [gain_now, gain_prev, gain_side, retain, live_mask, zero_row, zero_row, zero_row], axis=0
    )
    arrived = lax.ppermute(jnp.where(mine == 0, cotangent, lateral), "group", [(0, 1), (1, 0)])
    steps_all = 2 * steps_dev
    source_ids = lax.broadcasted_iota(jnp.int32, (reach_dev + outlets, reach_dev), 0)
    confluence = jnp.zeros((reach_dev + outlets, reach_dev), jnp.float32)
    for upslot in range(up_count):
        confluence = confluence + (
            (source_ids == feeders[upslot][None, :]) & (upslot < feeder_count)[None, :]
        ).astype(jnp.float32)
    confluence = confluence.astype(jnp.bfloat16)
    target_ids = lax.broadcasted_iota(jnp.int32, (reach_dev, reach_dev + outlets), 1)
    confluence_t = jnp.zeros((reach_dev, reach_dev + outlets), jnp.float32)
    for upslot in range(up_count):
        confluence_t = confluence_t + (
            (target_ids == feeders[upslot][:, None]) & (upslot < feeder_count)[:, None]
        ).astype(jnp.float32)
    confluence_t = confluence_t.astype(jnp.bfloat16)
    zero_flow = jnp.zeros((steps_all, reach_dev), jnp.float32)

    def forward_first(operands):
        flow, outlet, unused = routed(coef, lateral, arrived)
        return flow, outlet, flow, zero_flow, zero_flow

    def backward_first(operands):
        adjoint, own, side = adjoined(coef, arrived, cotangent, confluence_t=confluence_t)
        return own, side, adjoint, zero_flow, zero_flow

    def forward_step(operands):
        upper, side = operands
        flow, outlet, inflow = routed(coef, lateral, arrived, upper, side, confluence)
        return flow, outlet, flow, inflow, zero_flow

    def forward_last(operands):
        flow, outlet, first, inflow, unused = forward_step(operands)
        return flow, outlet, first, inflow, jnp.concatenate([lateral, arrived], axis=0)

    def backward_step(operands):
        upper, side = operands
        adjoint, own, side = adjoined(coef, arrived, cotangent, upper, side, confluence_t)
        return own, side, adjoint, zero_flow, zero_flow

    def backward_last(operands):
        upper, side = operands
        adjoint, unused, unused_side = adjoined(coef, arrived, cotangent, upper, side)
        return zero_flow, side, adjoint, zero_flow, zero_flow

    message, outlet_message, *kept = lax.cond(mine == 0, forward_first, backward_first, None)
    for level_step in range(1, levels):
        upper = both_ways(message, 0)
        side = both_ways(outlet_message, 1)
        last = level_step + 1 == levels
        message, outlet_message, *kept = lax.cond(
            mine == 0,
            forward_last if last else forward_step,
            backward_last if last else backward_step,
            (upper, side),
        )
    kept = jnp.stack(kept, axis=0)
    other = lax.ppermute(kept, "group", [(0, 1), (1, 0)])
    forward_kept = jnp.where(mine == 0, kept, other)
    backward_kept = jnp.where(mine == 0, other, kept)
    outflow, inflow, lateral_all = forward_kept[0], forward_kept[1], forward_kept[2]
    adjoint = backward_kept[0]
    zero_first = jnp.zeros((1, reach_dev), jnp.float32)
    flow_before = jnp.concatenate([zero_first, outflow[:-1]], axis=0)
    inflow_before = jnp.concatenate([zero_first, inflow[:-1]], axis=0)
    coef_grads = (
        jnp.sum(adjoint * inflow, axis=0),
        jnp.sum(adjoint * inflow_before, axis=0),
        jnp.sum(adjoint * flow_before, axis=0),
        jnp.sum(adjoint * lateral_all, axis=0),
    )
    raw_grad = coef_pull(coef_grads)[0]
    owned_rows = regions // lax.axis_size("basin")
    weighted = (member_table[:, None, :] * raw_grad[None, :, :]).reshape(
        regions * param_count, reach_dev
    )
    summed = jnp.dot(
        weighted, attributes.T, precision=lax.Precision.HIGHEST, preferred_element_type=jnp.float32
    )
    local_grad = jnp.transpose(summed.reshape(regions, param_count, attr_count), (0, 2, 1))
    basins = lax.axis_size("basin")
    share_size = owned_rows * attr_count * param_count
    replicated = jnp.broadcast_to(
        local_grad.reshape(1, basins, share_size), (levels, basins, share_size)
    ).reshape(levels * basins, share_size)
    grad_net = jnp.sum(
        lax.all_to_all(replicated, ("level", "basin"), 0, 0, tiled=True), axis=0
    ).reshape(owned_rows, attr_count, param_count)
    own_hours = lax.dynamic_slice_in_dim(outflow, mine * steps_dev, steps_dev, axis=0)
    return (own_hours, grad_net)


def solution(mesh):
    in_specs = (
        P("group", ("level", "basin")),
        P("group", ("level", "basin")),
        P(None, ("level", "basin")),
        P(("level", "basin")),
        P(None, ("level", "basin")),
        P(("level", "basin")),
        P(("level", "basin")),
        P(),
    )
    out_specs = (P("group", ("level", "basin")), P("basin", None, None))
    return jax.shard_map(body, mesh=mesh, in_specs=in_specs, out_specs=out_specs, check_vma=False)
```
